32 devices in a mesh: dp: 8 (over z, x), head: 4 (over y, core).
Axes of the slice: x: 2, y: 2, z: 4, core: 2. Of those that a mesh axis runs over, the one named last changes fastest.
Arguments:
- tokens: bfloat16 [4096, 3072], P(('dp', 'head')), may hold values from -6 to 6
- norm_gain: bfloat16 [3072], replicated, may hold values from 0.099609375 to 1.8984375
- w_query: bfloat16 [3072, 1536], P(None, 'head'), may hold values from -0.109375 to 0.109375
- key_value_weight: bfloat16 [3072, 512], P(None, 'head'), may hold values from -0.21875 to 0.21875
- w_out: bfloat16 [1536, 3072], P('head'), may hold values from -0.15625 to 0.15625
- kv_pool: bfloat16 [384, 2, 2, 128, 128], P('dp'), may hold values from -400 to 400
- cache_lengths: int32 [8], replicated, may hold values from 3969 to 8192, as said below
- page_table: int32 [8, 64], replicated, may hold values from -1 to 383, as said below
- token_mask: int32 [4096], replicated, may hold values 0 or 1
Outputs:
- attn_out: bfloat16 [4096, 3072], P(('dp', 'head'))
The draws below stay inside these ranges and needn't reach their ends.
Inputs may be any that keep to these rules, and one draw needn't show every extreme that they name: Request r caches cache_lengths[r] tokens in its first ceil(cache_lengths[r] / 128) logical pages; exactly one request caches 64 * 128 tokens. page_table[r, j] is the pool page of logical page j of request r while j is below that request's page count, else -1; no pool page is named twice; pool page p sits on dp index p // 48; at most 8 pages of one request sit on one dp index, and one request has exactly 8 on every dp index.
All inputs are finite; a program needn't handle non-finite values.
Results may differ from the reference program's by a relative error of at most 0.0049.
The reference program's roundings to bfloat16 on the way count: a program that leaves them out, or rounds other values in their place, can miss the bound.
Values may be sent and summed in bfloat16 or wider, within the bound.
No kernel may reach another device: no remote copies, remote signals or barrier semaphores. Data moves between devices by JAX's collectives and lax.ppermute only.
A program may use at most 192 MiB of HBM per device.

```python
import math
import jax
import jax.numpy as jnp
from jax import lax

MODEL_WIDTH = 3072
QUERY_HEADS = 12
KEY_VALUE_HEADS = 2
HEAD_SIZE = 128
PAGE_TOKENS = 128
NEWTOK = 512
MOST_PAGES = 64
REQUESTS = 8
TOTAL_TOKENS = 4096
CAP = 8
PAGES_DEV = 48
POOL_PAGES = 384
N_DP = 8


def plan_pages(key):
    base = jax.random.fold_in(key, 7)
    key_pages, key_big, key_tail, key_order = jax.random.split(base, 4)
    counts = jax.random.randint(key_pages, (REQUESTS,), MOST_PAGES // 2, 11 * MOST_PAGES // 16 + 1)
    biggest = jax.random.randint(key_big, (), 0, REQUESTS)
    is_big = jnp.arange(REQUESTS, dtype=jnp.int32) == biggest
    counts = jnp.where(is_big, MOST_PAGES, counts).astype(jnp.int32)
    tail = jax.random.randint(key_tail, (REQUESTS,), 1, PAGE_TOKENS + 1)
    lengths = (counts - 1) * PAGE_TOKENS + jnp.where(is_big, PAGE_TOKENS, tail)
    order = jax.random.permutation(key_order, REQUESTS)
    ordered = counts[order]
    starts_ordered = jnp.cumsum(ordered) - ordered
    starts = jnp.zeros((REQUESTS,), jnp.int32).at[order].set(starts_ordered.astype(jnp.int32))
    logical = jnp.arange(MOST_PAGES, dtype=jnp.int32)
    serial = starts[:, None] + logical[None, :]
    owner = serial // CAP % N_DP
    place = serial // (CAP * N_DP) * CAP + serial % CAP
    table = jnp.where(logical[None, :] < counts[:, None], owner * PAGES_DEV + place, -1)
    return (lengths.astype(jnp.int32), table.astype(jnp.int32))


def draw_cache_lengths(key, part):
    return plan_pages(key)[0]


def draw_page_table(key, part):
    return plan_pages(key)[1]


def draw_kv_pool(key, part):
    key_base, key_mark, key_amplitude, key_direction, key_rotation = jax.random.split(jax.random.fold_in(key, 11), 5)
    array_shape = (POOL_PAGES, KEY_VALUE_HEADS, 2, PAGE_TOKENS, HEAD_SIZE)
    base = jnp.clip(jax.random.normal(key_base, array_shape, jnp.float32), -6.0, 6.0)
    marked = jax.random.randint(key_mark, (POOL_PAGES,), 0, 32) == 0
    amplitude = jnp.exp(jax.random.uniform(key_amplitude, (POOL_PAGES, KEY_VALUE_HEADS), jnp.float32, math.log(40.0), math.log(120.0)))
    rotation_direction = jnp.clip(jax.random.normal(key_direction, (POOL_PAGES, KEY_VALUE_HEADS, HEAD_SIZE), jnp.float32), -3.0, 3.0)
    rotation = jnp.clip(jax.random.normal(key_rotation, (POOL_PAGES, KEY_VALUE_HEADS, HEAD_SIZE), jnp.float32), -3.0, 3.0)
    first = amplitude[..., None] * rotation_direction
    second = first + 2.0 * rotation
    planted = jnp.stack([first, second], 2)
    keys = base[:, :, 0]
    keys_top = jnp.where(marked[:, None, None, None], planted, keys[:, :, :2])
    keys = jnp.concatenate([keys_top, keys[:, :, 2:]], 2)
    return jnp.stack([keys, base[:, :, 1]], 2).astype(jnp.bfloat16)


def touch_ends(entries, key, smallest, high):
    longest = entries.shape.index(max(entries.shape))
    spots = []
    for shift in (0, 1):
        where = [jax.random.randint(jax.random.fold_in(key, axis), (), 0, length) for axis, length in enumerate(entries.shape)]
        where[longest] = (where[longest] + shift) % entries.shape[longest]
        spots.append(tuple(where))
    return entries.at[spots[0]].set(smallest).at[spots[1]].set(high)


def block_levels(stream_key, dims, cuts, low, largest):
    level = 1.0
    for dim, parts in cuts:
        steps = jax.random.uniform(jax.random.fold_in(jax.random.fold_in(stream_key, 6), dim), (parts,), jnp.float32, low / len(cuts), largest / len(cuts))
        level = level * jnp.repeat(jnp.exp(steps), dims[dim] // parts).reshape((-1,) + (1,) * (len(dims) - 1 - dim))
    return level


def normal_values(key, extent, scale, reach, pieces=(), held_as=jnp.bfloat16):
    array = scale * jax.random.normal(key, extent, jnp.float32)
    if pieces:
        array = array * block_levels(key, extent, pieces, -0.22, 0.18)
    return jnp.clip(array, -reach, reach).astype(held_as)


def setup_inputs(seed: int = 0) -> dict:
    key_list = jax.random.split(jax.random.key(seed), 10)
    tokens = normal_values(key_list[0], (TOTAL_TOKENS, MODEL_WIDTH), 1.0, 6.0, ((0, 32),))
    norm_gain = jnp.clip(1.0 + 0.18 * jax.random.normal(key_list[1], (MODEL_WIDTH,), jnp.float32), 0.099609375, 1.8984375).astype(jnp.bfloat16)
    w_query = normal_values(key_list[2], (MODEL_WIDTH, QUERY_HEADS * HEAD_SIZE), MODEL_WIDTH ** -0.5, 0.109375, ((1, 4),))
    key_value_weight = normal_values(key_list[3], (MODEL_WIDTH, KEY_VALUE_HEADS * 2 * HEAD_SIZE), (MODEL_WIDTH // 4) ** -0.5, 0.21875, ((1, 4),))
    w_out = normal_values(key_list[4], (QUERY_HEADS * HEAD_SIZE, MODEL_WIDTH), (QUERY_HEADS * HEAD_SIZE) ** -0.5, 0.15625, ((0, 4),))
    kv_pool = draw_kv_pool(jax.random.fold_in(key_list[9], 71), 0)
    cache_lengths = draw_cache_lengths(jax.random.fold_in(key_list[9], 71), 0)
    page_table = draw_page_table(jax.random.fold_in(key_list[9], 71), 0)
    token_mask = touch_ends((jax.random.randint(key_list[8], (TOTAL_TOKENS,), 0, 2) < 1).astype(jnp.int32), jax.random.fold_in(key_list[8], 1), 0, 1)
    return dict(tokens=tokens, norm_gain=norm_gain, w_query=w_query, key_value_weight=key_value_weight, w_out=w_out, kv_pool=kv_pool, cache_lengths=cache_lengths, page_table=page_table, token_mask=token_mask)


rope_base = 100000000000.0

def rotate(values, positions):
    half_dim = values.shape[-1] // 2
    freqs = jnp.exp(jnp.arange(half_dim, dtype=jnp.float32) * (-2.0 * math.log(rope_base) / values.shape[-1]))
    angles = positions.astype(jnp.float32)[:, None] * freqs[None, :]
    cosine = jnp.cos(angles)[:, None, :]
    sine = jnp.sin(angles)[:, None, :]
    first = values[..., :half_dim]
    second = values[..., half_dim:]
    return jnp.concatenate([first * cosine - second * sine, second * cosine + first * sine], -1)

def reference(tokens, norm_gain, w_query, key_value_weight, w_out, kv_pool, cache_lengths, page_table, token_mask):
    wide = tokens.astype(jnp.float32)
    meansq = lax.optimization_barrier(jnp.mean(wide * wide, -1, keepdims=True))
    normalized_input = (wide * lax.rsqrt(meansq + 1e-05) * norm_gain.astype(jnp.float32)).astype(jnp.bfloat16)
    query_all = jnp.dot(normalized_input, w_query, preferred_element_type=jnp.float32).reshape(TOTAL_TOKENS, QUERY_HEADS, HEAD_SIZE)
    key_value_rows = jnp.dot(normalized_input, key_value_weight, preferred_element_type=jnp.float32).reshape(TOTAL_TOKENS, KEY_VALUE_HEADS, 2, HEAD_SIZE)
    offsets = jnp.arange(TOTAL_TOKENS, dtype=jnp.int32)
    positions = cache_lengths[offsets // NEWTOK] + offsets % NEWTOK
    queries = rotate(query_all, positions).astype(jnp.bfloat16)
    new_keys = rotate(key_value_rows[:, :, 0], positions).astype(jnp.bfloat16)
    new_values = key_value_rows[:, :, 1].astype(jnp.bfloat16)
    queries_per_group = QUERY_HEADS // KEY_VALUE_HEADS
    scale = 1.0 / math.sqrt(HEAD_SIZE)

    def one_request(index):
        start = (index * NEWTOK).astype(jnp.int32)
        q_rows = lax.dynamic_slice_in_dim(queries, start, NEWTOK, 0)
        k_rows = lax.dynamic_slice_in_dim(new_keys, start, NEWTOK, 0)
        v_rows = lax.dynamic_slice_in_dim(new_values, start, NEWTOK, 0)
        m_rows = lax.dynamic_slice_in_dim(token_mask, start, NEWTOK, 0)
        request_pages = kv_pool[jnp.maximum(page_table[index], 0)]
        cached_rows = jnp.transpose(request_pages, (1, 2, 0, 3, 4)).reshape(KEY_VALUE_HEADS, 2, MOST_PAGES * PAGE_TOKENS, HEAD_SIZE)
        cache_ok = jnp.arange(MOST_PAGES * PAGE_TOKENS, dtype=jnp.int32) < cache_lengths[index]
        rows_idx = jnp.arange(NEWTOK, dtype=jnp.int32)
        new_ok = (m_rows[None, :] == 1) & (rows_idx[None, :] <= rows_idx[:, None])
        valid = jnp.concatenate([jnp.broadcast_to(cache_ok[None, :], (NEWTOK, MOST_PAGES * PAGE_TOKENS)), new_ok], 1)
        outputs = []
        for head in range(QUERY_HEADS):
            key_value_head = head // queries_per_group
            keys = jnp.concatenate([cached_rows[key_value_head, 0], k_rows[:, key_value_head]], 0)
            vals = jnp.concatenate([cached_rows[key_value_head, 1], v_rows[:, key_value_head]], 0)
            scores = jnp.dot(q_rows[:, head], keys.T, preferred_element_type=jnp.float32) * scale
            masked = jnp.where(valid, scores, -jnp.inf)
            top = lax.optimization_barrier(jnp.max(masked, -1, keepdims=True))
            expo = jnp.exp(masked - top)
            probs = expo / lax.optimization_barrier(jnp.sum(expo, -1, keepdims=True))
            weights = probs.astype(jnp.bfloat16)
            outputs.append(jnp.dot(weights, vals, preferred_element_type=jnp.float32).astype(jnp.bfloat16))
        return jnp.concatenate(outputs, -1)
    attended = lax.map(one_request, jnp.arange(REQUESTS, dtype=jnp.int32)).reshape(TOTAL_TOKENS, QUERY_HEADS * HEAD_SIZE)
    return jnp.dot(attended, w_out, preferred_element_type=jnp.float32).astype(jnp.bfloat16)
```

```python
import math

import jax
import jax.numpy as jnp
from jax import lax
from jax.sharding import PartitionSpec as P

KEY_VALUE_HEADS = 2
HEAD_SIZE = 128
NEWTOK = 512
REQ_DEV = 1


rope_base = 100000000000.0


def from_partner(value, axis, stride):
    mask = 2**stride
    pairs = [(source, source ^ mask) for source in range(lax.axis_size(axis))]
    return lax.ppermute(value, axis, pairs)


def exchange(value, axis, mask):
    pairs = [(source, source ^ mask) for source in range(lax.axis_size(axis))]
    return lax.ppermute(value, axis, pairs)


def rotate(values, positions):
    half_dim = values.shape[-1] // 2
    freqs = jnp.exp(
        jnp.arange(half_dim, dtype=jnp.float32) * (-2.0 * math.log(rope_base) / values.shape[-1])
    )
    angles = positions.astype(jnp.float32)[:, None] * freqs[None, :]
    cosine = jnp.cos(angles)[:, None, :]
    sine = jnp.sin(angles)[:, None, :]
    first = values[..., :half_dim]
    second = values[..., half_dim:]
    return jnp.concatenate([first * cosine - second * sine, second * cosine + first * sine], -1)


def body(
    tokens,
    norm_gain,
    w_query,
    key_value_weight,
    w_out,
    kv_pool,
    cache_lengths,
    page_table,
    token_mask,
):
    n_dp = lax.axis_size("dp")
    head_number = lax.axis_size("head")
    me_dp = lax.axis_index("dp")
    current_head = lax.axis_index("head")
    local_rows = tokens.shape[0]
    block_rows = local_rows * head_number
    head_dim = HEAD_SIZE
    group_heads = w_query.shape[1] // head_dim
    page_len = kv_pool.shape[3]
    pool_rows = kv_pool.shape[0]
    max_pages = page_table.shape[1]
    slots = max_pages // n_dp
    key_value_head = current_head // (head_number // KEY_VALUE_HEADS)
    held_w = w_out
    held_ids = current_head[None]
    stride = head_number // 2
    while stride >= 1:
        held_w = jnp.concatenate([held_w, exchange(held_w, "head", stride)], 0)
        held_ids = jnp.concatenate([held_ids, held_ids ^ stride], 0)
        stride //= 2
    owner_of = jnp.where(page_table >= 0, page_table // pool_rows, -1)
    mine = (owner_of == me_dp).astype(jnp.int32)
    rank = jnp.cumsum(mine, 1) - 1
    slot_ids = jnp.arange(slots, dtype=jnp.int32)
    select = (mine[:, None, :] == 1) & (rank[:, None, :] == slot_ids[None, :, None])
    local_page = jnp.sum(jnp.where(select, (page_table % pool_rows)[:, None, :], 0), -1)
    present = jnp.any(select, -1).reshape(-1)
    outgoing = kv_pool[local_page.reshape(-1), key_value_head]
    outgoing = jnp.where(present[:, None, None, None], outgoing, jnp.zeros_like(outgoing))
    received = lax.all_to_all(outgoing, "dp", split_axis=0, concat_axis=0, tiled=True)
    within = jnp.arange(page_len, dtype=jnp.int32)
    owners_mine = lax.dynamic_slice_in_dim(owner_of, me_dp * REQ_DEV, REQ_DEV, 0)
    hits = (owners_mine[None, :, :] == jnp.arange(n_dp, dtype=jnp.int32)[:, None, None]).astype(
        jnp.int32
    )
    hit_rank = jnp.cumsum(hits, -1) - 1
    chosen = (hits[:, :, None, :] == 1) & (hit_rank[:, :, None, :] == slot_ids[None, None, :, None])
    logical = jnp.sum(
        jnp.where(chosen, jnp.arange(max_pages, dtype=jnp.int32)[None, None, None, :], 0), -1
    )
    has_page = jnp.any(chosen, -1)
    key_pos = logical[..., None] * page_len + within[None, None, None, :]
    received = received.reshape(n_dp, REQ_DEV, slots, 2, page_len, head_dim)
    wide = tokens.astype(jnp.float32)
    meansq = jnp.mean(wide * wide, -1, keepdims=True)
    normalized_input = (wide * lax.rsqrt(meansq + 1e-05) * norm_gain.astype(jnp.float32)).astype(
        jnp.bfloat16
    )
    piece = lax.all_gather(normalized_input, "head", axis=0, tiled=True)
    q_part = jnp.dot(piece, w_query, preferred_element_type=jnp.float32)
    kv_part = jnp.dot(piece, key_value_weight, preferred_element_type=jnp.float32)
    projected = jnp.concatenate([q_part, kv_part], 1)
    q_width = group_heads * head_dim
    row_ids = jnp.arange(block_rows, dtype=jnp.int32)
    my_lengths = lax.dynamic_slice_in_dim(cache_lengths, me_dp * REQ_DEV, REQ_DEV, 0)
    positions = my_lengths[row_ids // NEWTOK] + row_ids % NEWTOK
    queries = rotate(
        projected[:, :q_width].reshape(block_rows, group_heads, head_dim), positions
    ).astype(jnp.bfloat16)
    own_part = projected[:, q_width:]
    holds_keys = current_head % 2 == 0
    turned = rotate(own_part[:, None, :], positions)[:, 0]
    own_ready = jnp.where(holds_keys, turned, own_part).astype(jnp.bfloat16)
    partner_ready = from_partner(own_ready, "head", 0)
    new_keys = jnp.where(holds_keys, own_ready, partner_ready)
    new_values = jnp.where(holds_keys, partner_ready, own_ready)
    mask_rows = lax.dynamic_slice_in_dim(token_mask, me_dp * block_rows, block_rows, 0)
    scale = 1.0 / math.sqrt(head_dim)
    local_idx = jnp.arange(NEWTOK, dtype=jnp.int32)
    cache_keys = received[:, 0, :, 0].reshape(-1, head_dim)
    cache_vals = received[:, 0, :, 1].reshape(-1, head_dim)
    cache_ok = (has_page[:, 0, :, None] & (key_pos[:, 0] < my_lengths[0])).reshape(-1)
    new_ok = (mask_rows[None, :] == 1) & (local_idx[None, :] <= local_idx[:, None])
    valid = jnp.concatenate(
        [jnp.broadcast_to(cache_ok[None, :], (NEWTOK, cache_ok.shape[0])), new_ok], 1
    )
    keys = jnp.concatenate([cache_keys, new_keys], 0)
    vals = jnp.concatenate([cache_vals, new_values], 0)
    head_outs = []
    for head in range(group_heads):
        scores = (
            lax.dot_general(
                queries[0:NEWTOK, head],
                keys,
                (((1,), (1,)), ((), ())),
                preferred_element_type=jnp.float32,
            )
            * scale
        )
        masked = jnp.where(valid, scores, -jnp.inf)
        top = jnp.max(masked, -1, keepdims=True)
        expo = jnp.exp(masked - top)
        probs = expo / jnp.sum(expo, -1, keepdims=True)
        weights = probs.astype(jnp.bfloat16)
        head_outs.append(
            jnp.dot(weights, vals, preferred_element_type=jnp.float32).astype(jnp.bfloat16)
        )
    pieces = jnp.concatenate(head_outs, -1)
    gathered = lax.all_to_all(pieces, "head", split_axis=0, concat_axis=1, tiled=True)
    gathered = gathered.reshape(local_rows, head_number, group_heads * head_dim)
    ordered = jnp.take(gathered, held_ids, axis=1).reshape(local_rows, -1)
    out = jnp.dot(ordered, held_w, preferred_element_type=jnp.float32)
    return out.astype(jnp.bfloat16)


def solution(mesh):
    in_specs = (
        P(("dp", "head"), None),
        P(),
        P(None, "head"),
        P(None, "head"),
        P("head", None),
        P("dp", None, None, None, None),
        P(),
        P(),
        P(),
    )
    out_specs = P(("dp", "head"), None)
    return jax.shard_map(body, mesh=mesh, in_specs=in_specs, out_specs=out_specs, check_vma=False)
```

```python
import math

import jax
import jax.numpy as jnp
from jax import lax
from jax.sharding import PartitionSpec as P

KEY_VALUE_HEADS = 2
HEAD_SIZE = 128
NEWTOK = 512
REQ_DEV = 1


rope_base = 100000000000.0


def from_partner(value, axis, stride):
    mask = 2**stride
    pairs = [(source, source ^ mask) for source in range(lax.axis_size(axis))]
    return lax.ppermute(value, axis, pairs)


def exchange(value, axis, mask):
    pairs = [(source, source ^ mask) for source in range(lax.axis_size(axis))]
    return lax.ppermute(value, axis, pairs)


def rotate(values, positions):
    half_dim = values.shape[-1] // 2
    freqs = jnp.exp(
        jnp.arange(half_dim, dtype=jnp.float32) * (-2.0 * math.log(rope_base) / values.shape[-1])
    )
    angles = positions.astype(jnp.float32)[:, None] * freqs[None, :]
    cosine = jnp.cos(angles)[:, None, :]
    sine = jnp.sin(angles)[:, None, :]
    first = values[..., :half_dim]
    second = values[..., half_dim:]
    return jnp.concatenate([first * cosine - second * sine, second * cosine + first * sine], -1)


def body(
    tokens,
    norm_gain,
    w_query,
    key_value_weight,
    w_out,
    kv_pool,
    cache_lengths,
    page_table,
    token_mask,
):
    n_dp = lax.axis_size("dp")
    head_number = lax.axis_size("head")
    me_dp = lax.axis_index("dp")
    current_head = lax.axis_index("head")
    local_rows = tokens.shape[0]
    block_rows = local_rows * head_number
    head_dim = HEAD_SIZE
    group_heads = w_query.shape[1] // head_dim
    page_len = kv_pool.shape[3]
    pool_rows = kv_pool.shape[0]
    max_pages = page_table.shape[1]
    slots = max_pages // n_dp
    key_value_head = current_head // (head_number // KEY_VALUE_HEADS)
    owner_of = jnp.where(page_table >= 0, page_table // pool_rows, -1)
    mine = (owner_of == me_dp).astype(jnp.int32)
    rank = jnp.cumsum(mine, 1) - 1
    slot_ids = jnp.arange(slots, dtype=jnp.int32)
    select = (mine[:, None, :] == 1) & (rank[:, None, :] == slot_ids[None, :, None])
    local_page = jnp.sum(jnp.where(select, (page_table % pool_rows)[:, None, :], 0), -1)
    present = jnp.any(select, -1).reshape(-1)
    part = current_head % 2
    outgoing = kv_pool[local_page.reshape(-1), key_value_head, part]
    received = lax.all_to_all(outgoing, "dp", split_axis=0, concat_axis=0, tiled=True)
    other_half = exchange(received, "head", 1)
    cache_keys = jnp.where(part == 0, received, other_half).reshape(-1, HEAD_SIZE)
    cache_vals = jnp.where(part == 0, other_half, received).reshape(-1, HEAD_SIZE)
    within = jnp.arange(page_len, dtype=jnp.int32)
    owners_mine = lax.dynamic_slice_in_dim(owner_of, me_dp * REQ_DEV, REQ_DEV, 0)
    hits = (owners_mine[None, :, :] == jnp.arange(n_dp, dtype=jnp.int32)[:, None, None]).astype(
        jnp.int32
    )
    hit_rank = jnp.cumsum(hits, -1) - 1
    chosen = (hits[:, :, None, :] == 1) & (hit_rank[:, :, None, :] == slot_ids[None, None, :, None])
    logical = jnp.sum(
        jnp.where(chosen, jnp.arange(max_pages, dtype=jnp.int32)[None, None, None, :], 0), -1
    )
    has_page = jnp.any(chosen, -1)
    key_pos = logical[..., None] * page_len + within[None, None, None, :]
    wide = tokens.astype(jnp.float32)
    meansq = jnp.mean(wide * wide, -1, keepdims=True)
    normalized_input = (wide * lax.rsqrt(meansq + 1e-05) * norm_gain.astype(jnp.float32)).astype(
        jnp.bfloat16
    )
    piece = lax.all_gather(normalized_input, "head", axis=0, tiled=True)
    q_part = jnp.dot(piece, w_query, preferred_element_type=jnp.float32)
    kv_part = jnp.dot(piece, key_value_weight, preferred_element_type=jnp.float32)
    projected = jnp.concatenate([q_part, kv_part], 1)
    q_width = group_heads * head_dim
    row_ids = jnp.arange(block_rows, dtype=jnp.int32)
    my_lengths = lax.dynamic_slice_in_dim(cache_lengths, me_dp * REQ_DEV, REQ_DEV, 0)
    positions = my_lengths[row_ids // NEWTOK] + row_ids % NEWTOK
    queries = rotate(
        projected[:, :q_width].reshape(block_rows, group_heads, head_dim), positions
    ).astype(jnp.bfloat16)
    held_w = [w_out]
    held_ids = [current_head]
    stride = head_number // 2
    while stride >= 1:
        if stride != head_number // 2:
            late, queries = lax.optimization_barrier((held_w[1:], queries))
            held_w = held_w[:1] + list(late)
        held_w = held_w + [exchange(piece, "head", stride) for piece in held_w]
        held_ids = held_ids + [ident ^ stride for ident in held_ids]
        stride //= 2
    held_w = jnp.concatenate(held_w, 0)
    held_ids = jnp.stack(held_ids)
    own_part = projected[:, q_width:]
    holds_keys = current_head % 2 == 0
    turned = rotate(own_part[:, None, :], positions)[:, 0]
    own_ready = jnp.where(holds_keys, turned, own_part).astype(jnp.bfloat16)
    partner_ready = from_partner(own_ready, "head", 0)
    new_keys = jnp.where(holds_keys, own_ready, partner_ready)
    new_values = jnp.where(holds_keys, partner_ready, own_ready)
    mask_rows = lax.dynamic_slice_in_dim(token_mask, me_dp * block_rows, block_rows, 0)
    scale = 1.0 / math.sqrt(head_dim)
    local_idx = jnp.arange(NEWTOK, dtype=jnp.int32)
    cache_ok = (has_page[:, 0, :, None] & (key_pos[:, 0] < my_lengths[0])).reshape(-1)
    new_ok = (mask_rows[None, :] == 1) & (local_idx[None, :] <= local_idx[:, None])
    valid = jnp.concatenate(
        [jnp.broadcast_to(cache_ok[None, :], (NEWTOK, cache_ok.shape[0])), new_ok], 1
    )
    keys = jnp.concatenate([cache_keys, new_keys], 0)
    vals = jnp.concatenate([cache_vals, new_values], 0)
    head_outs = []
    for head in range(group_heads):
        scores = (
            lax.dot_general(
                queries[0:NEWTOK, head],
                keys,
                (((1,), (1,)), ((), ())),
                preferred_element_type=jnp.float32,
            )
            * scale
        )
        masked = jnp.where(valid, scores, -jnp.inf)
        top = jnp.max(masked, -1, keepdims=True)
        expo = jnp.exp(masked - top)
        probs = expo / jnp.sum(expo, -1, keepdims=True)
        weights = probs.astype(jnp.bfloat16)
        head_outs.append(
            jnp.dot(weights, vals, preferred_element_type=jnp.float32).astype(jnp.bfloat16)
        )
    pieces = jnp.concatenate(head_outs, -1)
    gathered = lax.all_to_all(pieces, "head", split_axis=0, concat_axis=1, tiled=True)
    gathered = gathered.reshape(local_rows, head_number, group_heads * head_dim)
    ordered = jnp.take(gathered, held_ids, axis=1).reshape(local_rows, -1)
    out = jnp.dot(ordered, held_w, preferred_element_type=jnp.float32)
    return out.astype(jnp.bfloat16)


def solution(mesh):
    in_specs = (
        P(("dp", "head"), None),
        P(),
        P(None, "head"),
        P(None, "head"),
        P("head", None),
        P("dp", None, None, None, None),
        P(),
        P(),
        P(),
    )
    out_specs = P(("dp", "head"), None)
    return jax.shard_map(body, mesh=mesh, in_specs=in_specs, out_specs=out_specs, check_vma=False)
```

```python
import math

import jax
import jax.numpy as jnp
from jax import lax
from jax.sharding import PartitionSpec as P
from jax.experimental import pallas as pl
from jax.experimental.pallas import tpu as pltpu

KEY_VALUE_HEADS = 2
HEAD_SIZE = 128
NEWTOK = 512
REQ_DEV = 1


rope_base = 100000000000.0


def from_partner(value, axis, stride):
    mask = 2**stride
    pairs = [(source, source ^ mask) for source in range(lax.axis_size(axis))]
    return lax.ppermute(value, axis, pairs)


def attend_kernel(n_cache, tk, scale, q_ref, k_ref, v_ref, ok_ref, o_ref, s_scr):
    bq = q_ref.shape[0]
    total = k_ref.shape[0]
    chunks = total // tk
    q = q_ref[...]
    row = pl.program_id(1) * bq + lax.broadcasted_iota(jnp.int32, (bq, tk), 0)
    lane = lax.broadcasted_iota(jnp.int32, (bq, tk), 1)

    def scores(c, top):
        start = pl.multiple_of(c * tk, tk)
        keys = k_ref[pl.ds(start, tk), :]
        s = lax.dot_general(q, keys, (((1,), (1,)), ((), ())), preferred_element_type=jnp.float32)
        s = s * scale
        col = start + lane
        ok = (ok_ref[:, pl.ds(start, tk)] != 0) & ((col < n_cache) | (col - n_cache <= row))
        s = jnp.where(ok, s, -jnp.inf)
        s_scr[:, pl.ds(start, tk)] = s
        return jnp.maximum(top, jnp.max(s, -1, keepdims=True))

    top = lax.fori_loop(0, chunks, scores, jnp.full((bq, 1), -jnp.inf, jnp.float32))

    def expo(c, total_sum):
        start = pl.multiple_of(c * tk, tk)
        e = jnp.exp(s_scr[:, pl.ds(start, tk)] - top)
        s_scr[:, pl.ds(start, tk)] = e
        return total_sum + jnp.sum(e, -1, keepdims=True)

    denom = lax.fori_loop(0, chunks, expo, jnp.zeros((bq, 1), jnp.float32))

    def weigh(c, acc):
        start = pl.multiple_of(c * tk, tk)
        w = (s_scr[:, pl.ds(start, tk)] / denom).astype(jnp.bfloat16)
        return acc + jnp.dot(w, v_ref[pl.ds(start, tk), :], preferred_element_type=jnp.float32)

    acc = lax.fori_loop(0, chunks, weigh, jnp.zeros((bq, q.shape[1]), jnp.float32))
    o_ref[...] = acc.astype(o_ref.dtype)


def attend(queries, keys, vals, key_ok, n_cache):
    rows, width = queries.shape
    total, head_dim = keys.shape
    heads = width // head_dim
    bq = 256 if rows % 256 == 0 else rows
    tk = next(t for t in (512, 256, 128) if total % t == 0 and n_cache % t == 0)
    scale = 1.0 / math.sqrt(head_dim)
    cost = pl.CostEstimate(
        flops=4 * rows * total * head_dim * heads,
        transcendentals=rows * total * heads,
        bytes_accessed=2 * (2 * total * head_dim + 2 * rows * width) + 4 * total,
    )
    return pl.pallas_call(
        lambda *refs: attend_kernel(n_cache, tk, scale, *refs),
        out_shape=jax.ShapeDtypeStruct((rows, width), jnp.bfloat16),
        grid=(heads, rows // bq),
        in_specs=[
            pl.BlockSpec((bq, head_dim), lambda h, b: (b, h)),
            pl.BlockSpec((total, head_dim), lambda h, b: (0, 0)),
            pl.BlockSpec((total, head_dim), lambda h, b: (0, 0)),
            pl.BlockSpec((1, total), lambda h, b: (0, 0)),
        ],
        out_specs=pl.BlockSpec((bq, head_dim), lambda h, b: (b, h)),
        scratch_shapes=[pltpu.VMEM((bq, total), jnp.float32)],
        compiler_params=pltpu.CompilerParams(dimension_semantics=("arbitrary", "arbitrary")),
        cost_estimate=cost,
        name="paged_prefill_attention",
    )(queries, keys, vals, key_ok)


def exchange(value, axis, mask):
    pairs = [(source, source ^ mask) for source in range(lax.axis_size(axis))]
    return lax.ppermute(value, axis, pairs)


def rotate(values, positions):
    half_dim = values.shape[-1] // 2
    freqs = jnp.exp(
        jnp.arange(half_dim, dtype=jnp.float32) * (-2.0 * math.log(rope_base) / values.shape[-1])
    )
    angles = positions.astype(jnp.float32)[:, None] * freqs[None, :]
    cosine = jnp.cos(angles)[:, None, :]
    sine = jnp.sin(angles)[:, None, :]
    first = values[..., :half_dim]
    second = values[..., half_dim:]
    return jnp.concatenate([first * cosine - second * sine, second * cosine + first * sine], -1)


def body(
    tokens,
    norm_gain,
    w_query,
    key_value_weight,
    w_out,
    kv_pool,
    cache_lengths,
    page_table,
    token_mask,
):
    n_dp = lax.axis_size("dp")
    head_number = lax.axis_size("head")
    me_dp = lax.axis_index("dp")
    current_head = lax.axis_index("head")
    local_rows = tokens.shape[0]
    block_rows = local_rows * head_number
    head_dim = HEAD_SIZE
    group_heads = w_query.shape[1] // head_dim
    page_len = kv_pool.shape[3]
    pool_rows = kv_pool.shape[0]
    max_pages = page_table.shape[1]
    slots = max_pages // n_dp
    key_value_head = current_head // (head_number // KEY_VALUE_HEADS)
    owner_of = jnp.where(page_table >= 0, page_table // pool_rows, -1)
    mine = (owner_of == me_dp).astype(jnp.int32)
    rank = jnp.cumsum(mine, 1) - 1
    slot_ids = jnp.arange(slots, dtype=jnp.int32)
    select = (mine[:, None, :] == 1) & (rank[:, None, :] == slot_ids[None, :, None])
    local_page = jnp.sum(jnp.where(select, (page_table % pool_rows)[:, None, :], 0), -1)
    present = jnp.any(select, -1).reshape(-1)
    part = current_head % 2
    outgoing = kv_pool[local_page.reshape(-1), key_value_head, part]
    received = lax.all_to_all(outgoing, "dp", split_axis=0, concat_axis=0, tiled=True)
    other_half = exchange(received, "head", 1)
    cache_keys = jnp.where(part == 0, received, other_half).reshape(-1, HEAD_SIZE)
    cache_vals = jnp.where(part == 0, other_half, received).reshape(-1, HEAD_SIZE)
    within = jnp.arange(page_len, dtype=jnp.int32)
    owners_mine = lax.dynamic_slice_in_dim(owner_of, me_dp * REQ_DEV, REQ_DEV, 0)
    hits = (owners_mine[None, :, :] == jnp.arange(n_dp, dtype=jnp.int32)[:, None, None]).astype(
        jnp.int32
    )
    hit_rank = jnp.cumsum(hits, -1) - 1
    chosen = (hits[:, :, None, :] == 1) & (hit_rank[:, :, None, :] == slot_ids[None, None, :, None])
    logical = jnp.sum(
        jnp.where(chosen, jnp.arange(max_pages, dtype=jnp.int32)[None, None, None, :], 0), -1
    )
    has_page = jnp.any(chosen, -1)
    key_pos = logical[..., None] * page_len + within[None, None, None, :]
    wide = tokens.astype(jnp.float32)
    meansq = jnp.mean(wide * wide, -1, keepdims=True)
    normalized_input = (wide * lax.rsqrt(meansq + 1e-05) * norm_gain.astype(jnp.float32)).astype(
        jnp.bfloat16
    )
    piece = lax.all_gather(normalized_input, "head", axis=0, tiled=True)
    q_part = jnp.dot(piece, w_query, preferred_element_type=jnp.float32)
    kv_part = jnp.dot(piece, key_value_weight, preferred_element_type=jnp.float32)
    projected = jnp.concatenate([q_part, kv_part], 1)
    q_width = group_heads * head_dim
    row_ids = jnp.arange(block_rows, dtype=jnp.int32)
    my_lengths = lax.dynamic_slice_in_dim(cache_lengths, me_dp * REQ_DEV, REQ_DEV, 0)
    positions = my_lengths[row_ids // NEWTOK] + row_ids % NEWTOK
    queries = rotate(
        projected[:, :q_width].reshape(block_rows, group_heads, head_dim), positions
    ).astype(jnp.bfloat16)
    held_w = [w_out]
    held_ids = [current_head]
    stride = head_number // 2
    while stride >= 1:
        if stride != head_number // 2:
            late, queries = lax.optimization_barrier((held_w[1:], queries))
            held_w = held_w[:1] + list(late)
        held_w = held_w + [exchange(piece, "head", stride) for piece in held_w]
        held_ids = held_ids + [ident ^ stride for ident in held_ids]
        stride //= 2
    held_w = jnp.concatenate(held_w, 0)
    held_ids = jnp.stack(held_ids)
    own_part = projected[:, q_width:]
    holds_keys = current_head % 2 == 0
    turned = rotate(own_part[:, None, :], positions)[:, 0]
    own_ready = jnp.where(holds_keys, turned, own_part).astype(jnp.bfloat16)
    partner_ready = from_partner(own_ready, "head", 0)
    new_keys = jnp.where(holds_keys, own_ready, partner_ready)
    new_values = jnp.where(holds_keys, partner_ready, own_ready)
    mask_rows = lax.dynamic_slice_in_dim(token_mask, me_dp * block_rows, block_rows, 0)
    cache_ok = (has_page[:, 0, :, None] & (key_pos[:, 0] < my_lengths[0])).reshape(-1)
    key_ok = jnp.concatenate([cache_ok.astype(jnp.int32), (mask_rows == 1).astype(jnp.int32)])
    keys = jnp.concatenate([cache_keys, new_keys], 0)
    vals = jnp.concatenate([cache_vals, new_values], 0)
    pieces = attend(
        queries[0:NEWTOK].reshape(NEWTOK, group_heads * head_dim),
        keys,
        vals,
        key_ok.reshape(1, -1),
        cache_ok.shape[0],
    )
    gathered = lax.all_to_all(pieces, "head", split_axis=0, concat_axis=1, tiled=True)
    gathered = gathered.reshape(local_rows, head_number, group_heads * head_dim)
    ordered = jnp.take(gathered, held_ids, axis=1).reshape(local_rows, -1)
    out = jnp.dot(ordered, held_w, preferred_element_type=jnp.float32)
    return out.astype(jnp.bfloat16)


def solution(mesh):
    in_specs = (
        P(("dp", "head"), None),
        P(),
        P(None, "head"),
        P(None, "head"),
        P("head", None),
        P("dp", None, None, None, None),
        P(),
        P(),
        P(),
    )
    out_specs = P(("dp", "head"), None)
    return jax.shard_map(body, mesh=mesh, in_specs=in_specs, out_specs=out_specs, check_vma=False)
```

```python
import math

import jax
import jax.numpy as jnp
from jax import lax
from jax.sharding import PartitionSpec as P
from jax.experimental import pallas as pl
from jax.experimental.pallas import tpu as pltpu

KEY_VALUE_HEADS = 2
HEAD_SIZE = 128
NEWTOK = 512
REQ_DEV = 1


rope_base = 100000000000.0


def from_partner(value, axis, stride):
    mask = 2**stride
    pairs = [(source, source ^ mask) for source in range(lax.axis_size(axis))]
    return lax.ppermute(value, axis, pairs)


def attend_kernel(n_cache, tk, scale, q_ref, k_ref, v_ref, bias_ref, o_ref, s_scr):
    bq, head_dim = q_ref.shape
    total = k_ref.shape[0]
    groups = tk // 128
    q = q_ref[...]
    row = pl.program_id(1) * bq + lax.broadcasted_iota(jnp.int32, (bq, tk), 0)
    lane = lax.broadcasted_iota(jnp.int32, (bq, tk), 1)

    def scores(c, top, causal):
        start = pl.multiple_of(c * tk, tk)
        keys = k_ref[pl.ds(start, tk), :]
        s = lax.dot_general(q, keys, (((1,), (1,)), ((), ())), preferred_element_type=jnp.float32)
        s = s * scale + bias_ref[:, pl.ds(start, tk)]
        if causal:
            s = jnp.where(start - n_cache + lane <= row, s, -jnp.inf)
        s_scr[:, pl.ds(start, tk)] = s
        for g in range(groups):
            top = jnp.maximum(top, s[:, g * 128:(g + 1) * 128])
        return top

    top = jnp.full((bq, 128), -jnp.inf, jnp.float32)
    top = lax.fori_loop(0, n_cache // tk, lambda c, t: scores(c, t, False), top, unroll=2)
    top = lax.fori_loop(n_cache // tk, total // tk, lambda c, t: scores(c, t, True), top)
    top = jnp.max(top, -1, keepdims=True)

    def expo(c, part):
        start = pl.multiple_of(c * tk, tk)
        e = jnp.exp(s_scr[:, pl.ds(start, tk)] - top)
        s_scr[:, pl.ds(start, tk)] = e
        for g in range(groups):
            part = part + e[:, g * 128:(g + 1) * 128]
        return part

    part = lax.fori_loop(0, total // tk, expo, jnp.zeros((bq, 128), jnp.float32), unroll=2)
    inverse = 1.0 / jnp.sum(part, -1, keepdims=True)

    def weigh(c, acc):
        start = pl.multiple_of(c * tk, tk)
        w = (s_scr[:, pl.ds(start, tk)] * inverse).astype(jnp.bfloat16)
        return acc + jnp.dot(w, v_ref[pl.ds(start, tk), :], preferred_element_type=jnp.float32)

    acc = lax.fori_loop(0, total // tk, weigh, jnp.zeros((bq, head_dim), jnp.float32), unroll=2)
    o_ref[...] = acc.astype(o_ref.dtype)


def attend(queries, keys, vals, bias, n_cache):
    rows, width = queries.shape
    total, head_dim = keys.shape
    heads = width // head_dim
    bq = rows
    tk = next(t for t in (256, 128) if total % t == 0 and n_cache % t == 0)
    scale = 1.0 / math.sqrt(head_dim)
    cost = pl.CostEstimate(
        flops=4 * rows * total * head_dim * heads,
        transcendentals=rows * total * heads,
        bytes_accessed=2 * (2 * total * head_dim + 2 * rows * width) + 4 * total,
    )
    return pl.pallas_call(
        lambda *refs: attend_kernel(n_cache, tk, scale, *refs),
        out_shape=jax.ShapeDtypeStruct((rows, width), jnp.bfloat16),
        grid=(heads, rows // bq),
        in_specs=[
            pl.BlockSpec((bq, head_dim), lambda h, b: (b, h)),
            pl.BlockSpec((total, head_dim), lambda h, b: (0, 0)),
            pl.BlockSpec((total, head_dim), lambda h, b: (0, 0)),
            pl.BlockSpec((1, total), lambda h, b: (0, 0)),
        ],
        out_specs=pl.BlockSpec((bq, head_dim), lambda h, b: (b, h)),
        scratch_shapes=[pltpu.VMEM((bq, total), jnp.float32)],
        compiler_params=pltpu.CompilerParams(dimension_semantics=("arbitrary", "arbitrary")),
        cost_estimate=cost,
        name="paged_prefill_attention",
    )(queries, keys, vals, bias)


def exchange(value, axis, mask):
    pairs = [(source, source ^ mask) for source in range(lax.axis_size(axis))]
    return lax.ppermute(value, axis, pairs)


def rotate(values, positions):
    half_dim = values.shape[-1] // 2
    freqs = jnp.exp(
        jnp.arange(half_dim, dtype=jnp.float32) * (-2.0 * math.log(rope_base) / values.shape[-1])
    )
    angles = positions.astype(jnp.float32)[:, None] * freqs[None, :]
    cosine = jnp.cos(angles)[:, None, :]
    sine = jnp.sin(angles)[:, None, :]
    first = values[..., :half_dim]
    second = values[..., half_dim:]
    return jnp.concatenate([first * cosine - second * sine, second * cosine + first * sine], -1)


def body(
    tokens,
    norm_gain,
    w_query,
    key_value_weight,
    w_out,
    kv_pool,
    cache_lengths,
    page_table,
    token_mask,
):
    n_dp = lax.axis_size("dp")
    head_number = lax.axis_size("head")
    me_dp = lax.axis_index("dp")
    current_head = lax.axis_index("head")
    local_rows = tokens.shape[0]
    block_rows = local_rows * head_number
    head_dim = HEAD_SIZE
    group_heads = w_query.shape[1] // head_dim
    page_len = kv_pool.shape[3]
    pool_rows = kv_pool.shape[0]
    max_pages = page_table.shape[1]
    slots = max_pages // n_dp
    key_value_head = current_head // (head_number // KEY_VALUE_HEADS)
    owner_of = jnp.where(page_table >= 0, page_table // pool_rows, -1)
    mine = (owner_of == me_dp).astype(jnp.int32)
    rank = jnp.cumsum(mine, 1) - 1
    slot_ids = jnp.arange(slots, dtype=jnp.int32)
    select = (mine[:, None, :] == 1) & (rank[:, None, :] == slot_ids[None, :, None])
    local_page = jnp.sum(jnp.where(select, (page_table % pool_rows)[:, None, :], 0), -1)
    present = jnp.any(select, -1).reshape(-1)
    part = current_head % 2
    outgoing = kv_pool[local_page.reshape(-1), key_value_head, part]
    received = lax.all_to_all(outgoing, "dp", split_axis=0, concat_axis=0, tiled=True)
    other_half = exchange(received, "head", 1)
    cache_keys = jnp.where(part == 0, received, other_half).reshape(-1, HEAD_SIZE)
    cache_vals = jnp.where(part == 0, other_half, received).reshape(-1, HEAD_SIZE)
    within = jnp.arange(page_len, dtype=jnp.int32)
    owners_mine = lax.dynamic_slice_in_dim(owner_of, me_dp * REQ_DEV, REQ_DEV, 0)
    hits = (owners_mine[None, :, :] == jnp.arange(n_dp, dtype=jnp.int32)[:, None, None]).astype(
        jnp.int32
    )
    hit_rank = jnp.cumsum(hits, -1) - 1
    chosen = (hits[:, :, None, :] == 1) & (hit_rank[:, :, None, :] == slot_ids[None, None, :, None])
    logical = jnp.sum(
        jnp.where(chosen, jnp.arange(max_pages, dtype=jnp.int32)[None, None, None, :], 0), -1
    )
    has_page = jnp.any(chosen, -1)
    key_pos = logical[..., None] * page_len + within[None, None, None, :]
    wide = tokens.astype(jnp.float32)
    meansq = jnp.mean(wide * wide, -1, keepdims=True)
    normalized_input = (wide * lax.rsqrt(meansq + 1e-05) * norm_gain.astype(jnp.float32)).astype(
        jnp.bfloat16
    )
    piece = lax.all_gather(normalized_input, "head", axis=0, tiled=True)
    q_part = jnp.dot(piece, w_query, preferred_element_type=jnp.float32)
    kv_part = jnp.dot(piece, key_value_weight, preferred_element_type=jnp.float32)
    projected = jnp.concatenate([q_part, kv_part], 1)
    q_width = group_heads * head_dim
    row_ids = jnp.arange(block_rows, dtype=jnp.int32)
    my_lengths = lax.dynamic_slice_in_dim(cache_lengths, me_dp * REQ_DEV, REQ_DEV, 0)
    positions = my_lengths[row_ids // NEWTOK] + row_ids % NEWTOK
    queries = rotate(
        projected[:, :q_width].reshape(block_rows, group_heads, head_dim), positions
    ).astype(jnp.bfloat16)
    held_w = [w_out]
    held_ids = [current_head]
    stride = head_number // 2
    while stride >= 1:
        if stride != head_number // 2:
            late, queries = lax.optimization_barrier((held_w[1:], queries))
            held_w = held_w[:1] + list(late)
        held_w = held_w + [exchange(piece, "head", stride) for piece in held_w]
        held_ids = held_ids + [ident ^ stride for ident in held_ids]
        stride //= 2
    held_w = jnp.concatenate(held_w, 0)
    held_ids = jnp.stack(held_ids)
    own_part = projected[:, q_width:]
    holds_keys = current_head % 2 == 0
    turned = rotate(own_part[:, None, :], positions)[:, 0]
    own_ready = jnp.where(holds_keys, turned, own_part).astype(jnp.bfloat16)
    partner_ready = from_partner(own_ready, "head", 0)
    new_keys = jnp.where(holds_keys, own_ready, partner_ready)
    new_values = jnp.where(holds_keys, partner_ready, own_ready)
    mask_rows = lax.dynamic_slice_in_dim(token_mask, me_dp * block_rows, block_rows, 0)
    cache_ok = (has_page[:, 0, :, None] & (key_pos[:, 0] < my_lengths[0])).reshape(-1)
    key_ok = jnp.concatenate([cache_ok, mask_rows == 1])
    bias = jnp.where(key_ok, 0.0, -jnp.inf).astype(jnp.float32)
    keys = jnp.concatenate([cache_keys, new_keys], 0)
    vals = jnp.concatenate([cache_vals, new_values], 0)
    pieces = attend(
        queries[0:NEWTOK].reshape(NEWTOK, group_heads * head_dim),
        keys,
        vals,
        bias.reshape(1, -1),
        cache_ok.shape[0],
    )
    gathered = lax.all_to_all(pieces, "head", split_axis=0, concat_axis=1, tiled=True)
    gathered = gathered.reshape(local_rows, head_number, group_heads * head_dim)
    ordered = jnp.take(gathered, held_ids, axis=1).reshape(local_rows, -1)
    out = jnp.dot(ordered, held_w, preferred_element_type=jnp.float32)
    return out.astype(jnp.bfloat16)


def solution(mesh):
    in_specs = (
        P(("dp", "head"), None),
        P(),
        P(None, "head"),
        P(None, "head"),
        P("head", None),
        P("dp", None, None, None, None),
        P(),
        P(),
        P(),
    )
    out_specs = P(("dp", "head"), None)
    return jax.shard_map(body, mesh=mesh, in_specs=in_specs, out_specs=out_specs, check_vma=False)
```

```python
import math

import jax
import jax.numpy as jnp
from jax import lax
from jax.sharding import PartitionSpec as P
from jax.experimental import pallas as pl
from jax.experimental.pallas import tpu as pltpu

KEY_VALUE_HEADS = 2
HEAD_SIZE = 128
NEWTOK = 512
REQ_DEV = 1


rope_base = 100000000000.0


def from_partner(value, axis, stride):
    mask = 2**stride
    pairs = [(source, source ^ mask) for source in range(lax.axis_size(axis))]
    return lax.ppermute(value, axis, pairs)


def attend_kernel(
    n_cache, tk, scale, part_ref, q_ref, mine_hbm, other_hbm, nk_hbm, nv_hbm, bias_ref,
    o_ref, k_scr, v_scr, s_scr, sems,
):
    bq, head_dim = q_ref.shape
    total = k_scr.shape[0]
    groups = tk // 128

    @pl.when(pl.program_id(0) == 0)
    def _():
        def load(src_k, src_v):
            copies = [
                pltpu.make_async_copy(src_k, k_scr.at[pl.ds(0, n_cache)], sems.at[0]),
                pltpu.make_async_copy(src_v, v_scr.at[pl.ds(0, n_cache)], sems.at[1]),
                pltpu.make_async_copy(nk_hbm, k_scr.at[pl.ds(n_cache, total - n_cache)], sems.at[2]),
                pltpu.make_async_copy(nv_hbm, v_scr.at[pl.ds(n_cache, total - n_cache)], sems.at[3]),
            ]
            for copy in copies:
                copy.start()
            for copy in copies:
                copy.wait()

        @pl.when(part_ref[0] == 0)
        def _():
            load(mine_hbm, other_hbm)

        @pl.when(part_ref[0] != 0)
        def _():
            load(other_hbm, mine_hbm)

    q = q_ref[...]
    row = lax.broadcasted_iota(jnp.int32, (bq, tk), 0)
    lane = lax.broadcasted_iota(jnp.int32, (bq, tk), 1)

    def scores(c, top, causal):
        start = pl.multiple_of(c * tk, tk)
        keys = k_scr[pl.ds(start, tk), :]
        s = lax.dot_general(q, keys, (((1,), (1,)), ((), ())), preferred_element_type=jnp.float32)
        s = s * scale + bias_ref[:, pl.ds(start, tk)]
        if causal:
            s = jnp.where(start - n_cache + lane <= row, s, -jnp.inf)
        s_scr[:, pl.ds(start, tk)] = s
        for g in range(groups):
            top = jnp.maximum(top, s[:, g * 128:(g + 1) * 128])
        return top

    top = jnp.full((bq, 128), -jnp.inf, jnp.float32)
    top = lax.fori_loop(0, n_cache // tk, lambda c, t: scores(c, t, False), top, unroll=2)
    top = lax.fori_loop(n_cache // tk, total // tk, lambda c, t: scores(c, t, True), top)
    top = jnp.max(top, -1, keepdims=True)

    def expo(c, part):
        start = pl.multiple_of(c * tk, tk)
        e = jnp.exp(s_scr[:, pl.ds(start, tk)] - top)
        s_scr[:, pl.ds(start, tk)] = e
        for g in range(groups):
            part = part + e[:, g * 128:(g + 1) * 128]
        return part

    part = lax.fori_loop(0, total // tk, expo, jnp.zeros((bq, 128), jnp.float32), unroll=2)
    inverse = 1.0 / jnp.sum(part, -1, keepdims=True)

    def weigh(c, acc):
        start = pl.multiple_of(c * tk, tk)
        w = (s_scr[:, pl.ds(start, tk)] * inverse).astype(jnp.bfloat16)
        return acc + jnp.dot(w, v_scr[pl.ds(start, tk), :], preferred_element_type=jnp.float32)

    acc = lax.fori_loop(0, total // tk, weigh, jnp.zeros((bq, head_dim), jnp.float32), unroll=2)
    o_ref[...] = acc.astype(o_ref.dtype)


def attend(queries, mine, other, new_keys, new_values, part, bias):
    rows, width = queries.shape
    n_cache, head_dim = mine.shape
    total = n_cache + new_keys.shape[0]
    heads = width // head_dim
    tk = next(t for t in (256, 128) if total % t == 0 and n_cache % t == 0)
    scale = 1.0 / math.sqrt(head_dim)
    cost = pl.CostEstimate(
        flops=4 * rows * total * head_dim * heads,
        transcendentals=rows * total * heads,
        bytes_accessed=2 * (2 * total * head_dim + 2 * rows * width) + 4 * total,
    )
    any_spec = pl.BlockSpec(memory_space=pl.ANY)
    grid_spec = pltpu.PrefetchScalarGridSpec(
        num_scalar_prefetch=1,
        grid=(heads,),
        in_specs=[
            pl.BlockSpec((rows, head_dim), lambda h, p: (0, h)),
            any_spec,
            any_spec,
            any_spec,
            any_spec,
            pl.BlockSpec((1, total), lambda h, p: (0, 0)),
        ],
        out_specs=pl.BlockSpec((rows, head_dim), lambda h, p: (0, h)),
        scratch_shapes=[
            pltpu.VMEM((total, head_dim), jnp.bfloat16),
            pltpu.VMEM((total, head_dim), jnp.bfloat16),
            pltpu.VMEM((rows, total), jnp.float32),
            pltpu.SemaphoreType.DMA((4,)),
        ],
    )
    return pl.pallas_call(
        lambda *refs: attend_kernel(n_cache, tk, scale, *refs),
        out_shape=jax.ShapeDtypeStruct((rows, width), jnp.bfloat16),
        grid_spec=grid_spec,
        compiler_params=pltpu.CompilerParams(dimension_semantics=("arbitrary",)),
        cost_estimate=cost,
        name="paged_prefill_attention",
    )(part.reshape(1).astype(jnp.int32), queries, mine, other, new_keys, new_values, bias)


def exchange(value, axis, mask):
    pairs = [(source, source ^ mask) for source in range(lax.axis_size(axis))]
    return lax.ppermute(value, axis, pairs)


def rotate(values, positions):
    half_dim = values.shape[-1] // 2
    freqs = jnp.exp(
        jnp.arange(half_dim, dtype=jnp.float32) * (-2.0 * math.log(rope_base) / values.shape[-1])
    )
    angles = positions.astype(jnp.float32)[:, None] * freqs[None, :]
    cosine = jnp.cos(angles)[:, None, :]
    sine = jnp.sin(angles)[:, None, :]
    first = values[..., :half_dim]
    second = values[..., half_dim:]
    return jnp.concatenate([first * cosine - second * sine, second * cosine + first * sine], -1)


def body(
    tokens,
    norm_gain,
    w_query,
    key_value_weight,
    w_out,
    kv_pool,
    cache_lengths,
    page_table,
    token_mask,
):
    n_dp = lax.axis_size("dp")
    head_number = lax.axis_size("head")
    me_dp = lax.axis_index("dp")
    current_head = lax.axis_index("head")
    local_rows = tokens.shape[0]
    block_rows = local_rows * head_number
    head_dim = HEAD_SIZE
    group_heads = w_query.shape[1] // head_dim
    page_len = kv_pool.shape[3]
    pool_rows = kv_pool.shape[0]
    max_pages = page_table.shape[1]
    slots = max_pages // n_dp
    key_value_head = current_head // (head_number // KEY_VALUE_HEADS)
    owner_of = jnp.where(page_table >= 0, page_table // pool_rows, -1)
    mine = (owner_of == me_dp).astype(jnp.int32)
    rank = jnp.cumsum(mine, 1) - 1
    slot_ids = jnp.arange(slots, dtype=jnp.int32)
    select = (mine[:, None, :] == 1) & (rank[:, None, :] == slot_ids[None, :, None])
    local_page = jnp.sum(jnp.where(select, (page_table % pool_rows)[:, None, :], 0), -1)
    present = jnp.any(select, -1).reshape(-1)
    part = current_head % 2
    outgoing = kv_pool[local_page.reshape(-1), key_value_head, part]
    received = lax.all_to_all(outgoing, "dp", split_axis=0, concat_axis=0, tiled=True)
    within = jnp.arange(page_len, dtype=jnp.int32)
    owners_mine = lax.dynamic_slice_in_dim(owner_of, me_dp * REQ_DEV, REQ_DEV, 0)
    hits = (owners_mine[None, :, :] == jnp.arange(n_dp, dtype=jnp.int32)[:, None, None]).astype(
        jnp.int32
    )
    hit_rank = jnp.cumsum(hits, -1) - 1
    chosen = (hits[:, :, None, :] == 1) & (hit_rank[:, :, None, :] == slot_ids[None, None, :, None])
    logical = jnp.sum(
        jnp.where(chosen, jnp.arange(max_pages, dtype=jnp.int32)[None, None, None, :], 0), -1
    )
    has_page = jnp.any(chosen, -1)
    key_pos = logical[..., None] * page_len + within[None, None, None, :]
    wide = tokens.astype(jnp.float32)
    meansq = jnp.mean(wide * wide, -1, keepdims=True)
    normalized_input = (wide * lax.rsqrt(meansq + 1e-05) * norm_gain.astype(jnp.float32)).astype(
        jnp.bfloat16
    )
    piece = lax.all_gather(normalized_input, "head", axis=0, tiled=True)
    q_part = jnp.dot(piece, w_query, preferred_element_type=jnp.float32)
    kv_part = jnp.dot(piece, key_value_weight, preferred_element_type=jnp.float32)
    projected = jnp.concatenate([q_part, kv_part], 1)
    q_width = group_heads * head_dim
    row_ids = jnp.arange(block_rows, dtype=jnp.int32)
    my_lengths = lax.dynamic_slice_in_dim(cache_lengths, me_dp * REQ_DEV, REQ_DEV, 0)
    positions = my_lengths[row_ids // NEWTOK] + row_ids % NEWTOK
    queries = rotate(
        projected[:, :q_width].reshape(block_rows, group_heads, head_dim), positions
    ).astype(jnp.bfloat16)
    held_w = [w_out]
    held_ids = [current_head]
    stride = head_number // 2
    while stride > 1:
        held_w = held_w + [exchange(piece, "head", stride) for piece in held_w]
        held_ids = held_ids + [ident ^ stride for ident in held_ids]
        stride //= 2
    own_part = projected[:, q_width:]
    holds_keys = current_head % 2 == 0
    turned = rotate(own_part[:, None, :], positions)[:, 0]
    own_ready = jnp.where(holds_keys, turned, own_part).astype(jnp.bfloat16)
    partner_ready = from_partner(own_ready, "head", 0)
    new_keys = jnp.where(holds_keys, own_ready, partner_ready)
    new_values = jnp.where(holds_keys, partner_ready, own_ready)
    mask_rows = lax.dynamic_slice_in_dim(token_mask, me_dp * block_rows, block_rows, 0)
    cache_ok = (has_page[:, 0, :, None] & (key_pos[:, 0] < my_lengths[0])).reshape(-1)
    key_ok = jnp.concatenate([cache_ok, mask_rows == 1])
    bias = jnp.where(key_ok, 0.0, -jnp.inf).astype(jnp.float32)
    queries = queries[0:NEWTOK].reshape(NEWTOK, group_heads * head_dim)
    received, queries, new_keys, new_values = lax.optimization_barrier(
        (received, queries, new_keys, new_values)
    )
    other_half = exchange(received, "head", 1)
    pieces = attend(
        queries,
        received.reshape(-1, head_dim),
        other_half.reshape(-1, head_dim),
        new_keys,
        new_values,
        part,
        bias.reshape(1, -1),
    )
    late_w, pieces = lax.optimization_barrier((held_w[1:], pieces))
    held_w = held_w[:1] + list(late_w)
    held_w = held_w + [exchange(piece, "head", 1) for piece in held_w]
    held_ids = held_ids + [ident ^ 1 for ident in held_ids]
    held_w = jnp.concatenate(held_w, 0)
    held_ids = jnp.stack(held_ids)
    gathered = lax.all_to_all(pieces, "head", split_axis=0, concat_axis=1, tiled=True)
    gathered = gathered.reshape(local_rows, head_number, group_heads * head_dim)
    ordered = jnp.take(gathered, held_ids, axis=1).reshape(local_rows, -1)
    out = jnp.dot(ordered, held_w, preferred_element_type=jnp.float32)
    return out.astype(jnp.bfloat16)


def solution(mesh):
    in_specs = (
        P(("dp", "head"), None),
        P(),
        P(None, "head"),
        P(None, "head"),
        P("head", None),
        P("dp", None, None, None, None),
        P(),
        P(),
        P(),
    )
    out_specs = P(("dp", "head"), None)
    return jax.shard_map(body, mesh=mesh, in_specs=in_specs, out_specs=out_specs, check_vma=False)
```

```python
import math

import jax
import jax.numpy as jnp
from jax import lax
from jax.sharding import PartitionSpec as P
from jax.experimental import pallas as pl
from jax.experimental.pallas import tpu as pltpu

KEY_VALUE_HEADS = 2
HEAD_SIZE = 128
NEWTOK = 512
REQ_DEV = 1


rope_base = 100000000000.0


def from_partner(value, axis, stride):
    mask = 2**stride
    pairs = [(source, source ^ mask) for source in range(lax.axis_size(axis))]
    return lax.ppermute(value, axis, pairs)


def attend_kernel(
    n_cache, tk, scale, part_ref, q_ref, mine_hbm, other_hbm, nk_hbm, nv_hbm, bias_ref,
    o_ref, k_scr, v_scr, s_scr, sems,
):
    bq, head_dim = q_ref.shape
    total = k_scr.shape[0]
    groups = tk // 128

    @pl.when(pl.program_id(0) == 0)
    def _():
        def load(src_k, src_v):
            copies = [
                pltpu.make_async_copy(src_k, k_scr.at[pl.ds(0, n_cache)], sems.at[0]),
                pltpu.make_async_copy(src_v, v_scr.at[pl.ds(0, n_cache)], sems.at[1]),
                pltpu.make_async_copy(nk_hbm, k_scr.at[pl.ds(n_cache, total - n_cache)], sems.at[2]),
                pltpu.make_async_copy(nv_hbm, v_scr.at[pl.ds(n_cache, total - n_cache)], sems.at[3]),
            ]
            for copy in copies:
                copy.start()
            for copy in copies:
                copy.wait()

        @pl.when(part_ref[0] == 0)
        def _():
            load(mine_hbm, other_hbm)

        @pl.when(part_ref[0] != 0)
        def _():
            load(other_hbm, mine_hbm)

    q = q_ref[...]
    row = lax.broadcasted_iota(jnp.int32, (bq, tk), 0)
    lane = lax.broadcasted_iota(jnp.int32, (bq, tk), 1)

    def scores(c, top, causal):
        start = pl.multiple_of(c * tk, tk)
        keys = k_scr[pl.ds(start, tk), :]
        s = lax.dot_general(q, keys, (((1,), (1,)), ((), ())), preferred_element_type=jnp.float32)
        s = s * scale + bias_ref[:, pl.ds(start, tk)]
        if causal:
            s = jnp.where(start - n_cache + lane <= row, s, -jnp.inf)
        s_scr[:, pl.ds(start, tk)] = s
        for g in range(groups):
            top = jnp.maximum(top, s[:, g * 128:(g + 1) * 128])
        return top

    top = jnp.full((bq, 128), -jnp.inf, jnp.float32)
    top = lax.fori_loop(0, n_cache // tk, lambda c, t: scores(c, t, False), top, unroll=8)
    top = lax.fori_loop(n_cache // tk, total // tk, lambda c, t: scores(c, t, True), top)
    top = jnp.max(top, -1, keepdims=True)

    def expo(c, part):
        start = pl.multiple_of(c * tk, tk)
        e = jnp.exp(s_scr[:, pl.ds(start, tk)] - top)
        s_scr[:, pl.ds(start, tk)] = e
        for g in range(groups):
            part = part + e[:, g * 128:(g + 1) * 128]
        return part

    part = lax.fori_loop(0, total // tk, expo, jnp.zeros((bq, 128), jnp.float32), unroll=8)
    inverse = 1.0 / jnp.sum(part, -1, keepdims=True)

    def weigh(c, acc):
        start = pl.multiple_of(c * tk, tk)
        w = (s_scr[:, pl.ds(start, tk)] * inverse).astype(jnp.bfloat16)
        return acc + jnp.dot(w, v_scr[pl.ds(start, tk), :], preferred_element_type=jnp.float32)

    acc = lax.fori_loop(0, total // tk, weigh, jnp.zeros((bq, head_dim), jnp.float32), unroll=8)
    o_ref[...] = acc.astype(o_ref.dtype)


def attend(queries, mine, other, new_keys, new_values, part, bias):
    rows, width = queries.shape
    n_cache, head_dim = mine.shape
    total = n_cache + new_keys.shape[0]
    heads = width // head_dim
    tk = next(t for t in (512, 256, 128) if total % t == 0 and n_cache % t == 0)
    scale = 1.0 / math.sqrt(head_dim)
    cost = pl.CostEstimate(
        flops=4 * rows * total * head_dim * heads,
        transcendentals=rows * total * heads,
        bytes_accessed=2 * (2 * total * head_dim + 2 * rows * width) + 4 * total,
    )
    any_spec = pl.BlockSpec(memory_space=pl.ANY)
    grid_spec = pltpu.PrefetchScalarGridSpec(
        num_scalar_prefetch=1,
        grid=(heads,),
        in_specs=[
            pl.BlockSpec((rows, head_dim), lambda h, p: (0, h)),
            any_spec,
            any_spec,
            any_spec,
            any_spec,
            pl.BlockSpec((1, total), lambda h, p: (0, 0)),
        ],
        out_specs=pl.BlockSpec((rows, head_dim), lambda h, p: (0, h)),
        scratch_shapes=[
            pltpu.VMEM((total, head_dim), jnp.bfloat16),
            pltpu.VMEM((total, head_dim), jnp.bfloat16),
            pltpu.VMEM((rows, total), jnp.float32),
            pltpu.SemaphoreType.DMA((4,)),
        ],
    )
    return pl.pallas_call(
        lambda *refs: attend_kernel(n_cache, tk, scale, *refs),
        out_shape=jax.ShapeDtypeStruct((rows, width), jnp.bfloat16),
        grid_spec=grid_spec,
        compiler_params=pltpu.CompilerParams(dimension_semantics=("arbitrary",)),
        cost_estimate=cost,
        name="paged_prefill_attention",
    )(part.reshape(1).astype(jnp.int32), queries, mine, other, new_keys, new_values, bias)


def exchange(value, axis, mask):
    pairs = [(source, source ^ mask) for source in range(lax.axis_size(axis))]
    return lax.ppermute(value, axis, pairs)


def rotate(values, positions):
    half_dim = values.shape[-1] // 2
    freqs = jnp.exp(
        jnp.arange(half_dim, dtype=jnp.float32) * (-2.0 * math.log(rope_base) / values.shape[-1])
    )
    angles = positions.astype(jnp.float32)[:, None] * freqs[None, :]
    cosine = jnp.cos(angles)[:, None, :]
    sine = jnp.sin(angles)[:, None, :]
    first = values[..., :half_dim]
    second = values[..., half_dim:]
    return jnp.concatenate([first * cosine - second * sine, second * cosine + first * sine], -1)


def body(
    tokens,
    norm_gain,
    w_query,
    key_value_weight,
    w_out,
    kv_pool,
    cache_lengths,
    page_table,
    token_mask,
):
    n_dp = lax.axis_size("dp")
    head_number = lax.axis_size("head")
    me_dp = lax.axis_index("dp")
    current_head = lax.axis_index("head")
    local_rows = tokens.shape[0]
    block_rows = local_rows * head_number
    head_dim = HEAD_SIZE
    group_heads = w_query.shape[1] // head_dim
    page_len = kv_pool.shape[3]
    pool_rows = kv_pool.shape[0]
    max_pages = page_table.shape[1]
    slots = max_pages // n_dp
    key_value_head = current_head // (head_number // KEY_VALUE_HEADS)
    owner_of = jnp.where(page_table >= 0, page_table // pool_rows, -1)
    mine = (owner_of == me_dp).astype(jnp.int32)
    rank = jnp.cumsum(mine, 1) - 1
    slot_ids = jnp.arange(slots, dtype=jnp.int32)
    select = (mine[:, None, :] == 1) & (rank[:, None, :] == slot_ids[None, :, None])
    local_page = jnp.sum(jnp.where(select, (page_table % pool_rows)[:, None, :], 0), -1)
    present = jnp.any(select, -1).reshape(-1)
    part = current_head % 2
    outgoing = kv_pool[local_page.reshape(-1), key_value_head, part]
    received = lax.all_to_all(outgoing, "dp", split_axis=0, concat_axis=0, tiled=True)
    within = jnp.arange(page_len, dtype=jnp.int32)
    owners_mine = lax.dynamic_slice_in_dim(owner_of, me_dp * REQ_DEV, REQ_DEV, 0)
    hits = (owners_mine[None, :, :] == jnp.arange(n_dp, dtype=jnp.int32)[:, None, None]).astype(
        jnp.int32
    )
    hit_rank = jnp.cumsum(hits, -1) - 1
    chosen = (hits[:, :, None, :] == 1) & (hit_rank[:, :, None, :] == slot_ids[None, None, :, None])
    logical = jnp.sum(
        jnp.where(chosen, jnp.arange(max_pages, dtype=jnp.int32)[None, None, None, :], 0), -1
    )
    has_page = jnp.any(chosen, -1)
    key_pos = logical[..., None] * page_len + within[None, None, None, :]
    wide = tokens.astype(jnp.float32)
    meansq = jnp.mean(wide * wide, -1, keepdims=True)
    normalized_input = (wide * lax.rsqrt(meansq + 1e-05) * norm_gain.astype(jnp.float32)).astype(
        jnp.bfloat16
    )
    piece = lax.all_gather(normalized_input, "head", axis=0, tiled=True)
    q_part = jnp.dot(piece, w_query, preferred_element_type=jnp.float32)
    kv_part = jnp.dot(piece, key_value_weight, preferred_element_type=jnp.float32)
    projected = jnp.concatenate([q_part, kv_part], 1)
    q_width = group_heads * head_dim
    row_ids = jnp.arange(block_rows, dtype=jnp.int32)
    my_lengths = lax.dynamic_slice_in_dim(cache_lengths, me_dp * REQ_DEV, REQ_DEV, 0)
    positions = my_lengths[row_ids // NEWTOK] + row_ids % NEWTOK
    queries = rotate(
        projected[:, :q_width].reshape(block_rows, group_heads, head_dim), positions
    ).astype(jnp.bfloat16)
    held_w = [w_out]
    held_ids = [current_head]
    stride = head_number // 2
    while stride > 1:
        held_w = held_w + [exchange(piece, "head", stride) for piece in held_w]
        held_ids = held_ids + [ident ^ stride for ident in held_ids]
        stride //= 2
    own_part = projected[:, q_width:]
    holds_keys = current_head % 2 == 0
    turned = rotate(own_part[:, None, :], positions)[:, 0]
    own_ready = jnp.where(holds_keys, turned, own_part).astype(jnp.bfloat16)
    partner_ready = from_partner(own_ready, "head", 0)
    new_keys = jnp.where(holds_keys, own_ready, partner_ready)
    new_values = jnp.where(holds_keys, partner_ready, own_ready)
    mask_rows = lax.dynamic_slice_in_dim(token_mask, me_dp * block_rows, block_rows, 0)
    cache_ok = (has_page[:, 0, :, None] & (key_pos[:, 0] < my_lengths[0])).reshape(-1)
    key_ok = jnp.concatenate([cache_ok, mask_rows == 1])
    bias = jnp.where(key_ok, 0.0, -jnp.inf).astype(jnp.float32)
    queries = queries[0:NEWTOK].reshape(NEWTOK, group_heads * head_dim)
    received, queries, new_keys, new_values = lax.optimization_barrier(
        (received, queries, new_keys, new_values)
    )
    other_half = exchange(received, "head", 1)
    pieces = attend(
        queries,
        received.reshape(-1, head_dim),
        other_half.reshape(-1, head_dim),
        new_keys,
        new_values,
        part,
        bias.reshape(1, -1),
    )
    late_w, pieces = lax.optimization_barrier((held_w[1:], pieces))
    held_w = held_w[:1] + list(late_w)
    held_w = held_w + [exchange(piece, "head", 1) for piece in held_w]
    held_ids = held_ids + [ident ^ 1 for ident in held_ids]
    held_w = jnp.concatenate(held_w, 0)
    held_ids = jnp.stack(held_ids)
    gathered = lax.all_to_all(pieces, "head", split_axis=0, concat_axis=1, tiled=True)
    gathered = gathered.reshape(local_rows, head_number, group_heads * head_dim)
    ordered = jnp.take(gathered, held_ids, axis=1).reshape(local_rows, -1)
    out = jnp.dot(ordered, held_w, preferred_element_type=jnp.float32)
    return out.astype(jnp.bfloat16)


def solution(mesh):
    in_specs = (
        P(("dp", "head"), None),
        P(),
        P(None, "head"),
        P(None, "head"),
        P("head", None),
        P("dp", None, None, None, None),
        P(),
        P(),
        P(),
    )
    out_specs = P(("dp", "head"), None)
    return jax.shard_map(body, mesh=mesh, in_specs=in_specs, out_specs=out_specs, check_vma=False)
```

```python
import math

import jax
import jax.numpy as jnp
from jax import lax
from jax.sharding import PartitionSpec as P
from jax.experimental import pallas as pl
from jax.experimental.pallas import tpu as pltpu

KEY_VALUE_HEADS = 2
HEAD_SIZE = 128
NEWTOK = 512
REQ_DEV = 1


rope_base = 100000000000.0


def from_partner(value, axis, stride):
    mask = 2**stride
    pairs = [(source, source ^ mask) for source in range(lax.axis_size(axis))]
    return lax.ppermute(value, axis, pairs)


def attend_kernel(
    n_cache, tk, scale, part_ref, q_ref, mine_hbm, other_hbm, nk_hbm, nv_hbm, bias_ref,
    o_ref, k_scr, v_scr, s_scr, sems,
):
    bq, head_dim = q_ref.shape
    total = k_scr.shape[0]
    groups = tk // 128

    @pl.when(pl.program_id(0) == 0)
    def _():
        def load(src_k, src_v):
            copies = [
                pltpu.make_async_copy(src_k, k_scr.at[pl.ds(0, n_cache)], sems.at[0]),
                pltpu.make_async_copy(src_v, v_scr.at[pl.ds(0, n_cache)], sems.at[1]),
                pltpu.make_async_copy(nk_hbm, k_scr.at[pl.ds(n_cache, total - n_cache)], sems.at[2]),
                pltpu.make_async_copy(nv_hbm, v_scr.at[pl.ds(n_cache, total - n_cache)], sems.at[3]),
            ]
            for copy in copies:
                copy.start()
            for copy in copies:
                copy.wait()

        @pl.when(part_ref[0] == 0)
        def _():
            load(mine_hbm, other_hbm)

        @pl.when(part_ref[0] != 0)
        def _():
            load(other_hbm, mine_hbm)

    q = q_ref[...]
    row = lax.broadcasted_iota(jnp.int32, (bq, tk), 0)
    lane = lax.broadcasted_iota(jnp.int32, (bq, tk), 1)

    def scores(c, top, causal):
        start = pl.multiple_of(c * tk, tk)
        keys = k_scr[pl.ds(start, tk), :]
        s = lax.dot_general(q, keys, (((1,), (1,)), ((), ())), preferred_element_type=jnp.float32)
        s = s * scale + bias_ref[:, pl.ds(start, tk)]
        if causal:
            s = jnp.where(start - n_cache + lane <= row, s, -jnp.inf)
        s_scr[:, pl.ds(start, tk)] = s
        for g in range(groups):
            top = jnp.maximum(top, s[:, g * 128:(g + 1) * 128])
        return top

    top = jnp.full((bq, 128), -jnp.inf, jnp.float32)
    top = lax.fori_loop(0, n_cache // tk, lambda c, t: scores(c, t, False), top, unroll=8)
    top = lax.fori_loop(n_cache // tk, total // tk, lambda c, t: scores(c, t, True), top)
    top = jnp.max(top, -1, keepdims=True)

    def expo(c, part):
        start = pl.multiple_of(c * tk, tk)
        e = jnp.exp(s_scr[:, pl.ds(start, tk)] - top)
        s_scr[:, pl.ds(start, tk)] = e
        for g in range(groups):
            part = part + e[:, g * 128:(g + 1) * 128]
        return part

    part = lax.fori_loop(0, total // tk, expo, jnp.zeros((bq, 128), jnp.float32), unroll=8)
    inverse = 1.0 / jnp.sum(part, -1, keepdims=True)

    def weigh(c, acc):
        start = pl.multiple_of(c * tk, tk)
        w = (s_scr[:, pl.ds(start, tk)] * inverse).astype(jnp.bfloat16)
        return acc + jnp.dot(w, v_scr[pl.ds(start, tk), :], preferred_element_type=jnp.float32)

    acc = lax.fori_loop(0, total // tk, weigh, jnp.zeros((bq, head_dim), jnp.float32), unroll=8)
    o_ref[...] = acc.astype(o_ref.dtype)


def attend(queries, mine, other, new_keys, new_values, part, bias):
    rows, width = queries.shape
    n_cache, head_dim = mine.shape
    total = n_cache + new_keys.shape[0]
    heads = width // head_dim
    tk = next(t for t in (512, 256, 128) if total % t == 0 and n_cache % t == 0)
    scale = 1.0 / math.sqrt(head_dim)
    cost = pl.CostEstimate(
        flops=4 * rows * total * head_dim * heads,
        transcendentals=rows * total * heads,
        bytes_accessed=2 * (2 * total * head_dim + 2 * rows * width) + 4 * total,
    )
    any_spec = pl.BlockSpec(memory_space=pl.ANY)
    grid_spec = pltpu.PrefetchScalarGridSpec(
        num_scalar_prefetch=1,
        grid=(heads,),
        in_specs=[
            pl.BlockSpec((rows, head_dim), lambda h, p: (0, h)),
            any_spec,
            any_spec,
            any_spec,
            any_spec,
            pl.BlockSpec((1, total), lambda h, p: (0, 0)),
        ],
        out_specs=pl.BlockSpec((rows, head_dim), lambda h, p: (0, h)),
        scratch_shapes=[
            pltpu.VMEM((total, head_dim), jnp.bfloat16),
            pltpu.VMEM((total, head_dim), jnp.bfloat16),
            pltpu.VMEM((rows, total), jnp.float32),
            pltpu.SemaphoreType.DMA((4,)),
        ],
    )
    return pl.pallas_call(
        lambda *refs: attend_kernel(n_cache, tk, scale, *refs),
        out_shape=jax.ShapeDtypeStruct((rows, width), jnp.bfloat16),
        grid_spec=grid_spec,
        compiler_params=pltpu.CompilerParams(dimension_semantics=("arbitrary",)),
        cost_estimate=cost,
        name="paged_prefill_attention",
    )(part.reshape(1).astype(jnp.int32), queries, mine, other, new_keys, new_values, bias)


def exchange(value, axis, mask):
    pairs = [(source, source ^ mask) for source in range(lax.axis_size(axis))]
    return lax.ppermute(value, axis, pairs)


def rotate(values, positions):
    half_dim = values.shape[-1] // 2
    freqs = jnp.exp(
        jnp.arange(half_dim, dtype=jnp.float32) * (-2.0 * math.log(rope_base) / values.shape[-1])
    )
    angles = positions.astype(jnp.float32)[:, None] * freqs[None, :]
    cosine = jnp.cos(angles)[:, None, :]
    sine = jnp.sin(angles)[:, None, :]
    first = values[..., :half_dim]
    second = values[..., half_dim:]
    return jnp.concatenate([first * cosine - second * sine, second * cosine + first * sine], -1)


def body(
    tokens,
    norm_gain,
    w_query,
    key_value_weight,
    w_out,
    kv_pool,
    cache_lengths,
    page_table,
    token_mask,
):
    n_dp = lax.axis_size("dp")
    head_number = lax.axis_size("head")
    me_dp = lax.axis_index("dp")
    current_head = lax.axis_index("head")
    local_rows = tokens.shape[0]
    block_rows = local_rows * head_number
    head_dim = HEAD_SIZE
    group_heads = w_query.shape[1] // head_dim
    page_len = kv_pool.shape[3]
    pool_rows = kv_pool.shape[0]
    max_pages = page_table.shape[1]
    slots = max_pages // n_dp
    key_value_head = current_head // (head_number // KEY_VALUE_HEADS)
    owner_of = jnp.where(page_table >= 0, page_table // pool_rows, -1)
    mine = (owner_of == me_dp).astype(jnp.int32)
    rank = jnp.cumsum(mine, 1) - 1
    slot_ids = jnp.arange(slots, dtype=jnp.int32)
    select = (mine[:, None, :] == 1) & (rank[:, None, :] == slot_ids[None, :, None])
    local_page = jnp.sum(jnp.where(select, (page_table % pool_rows)[:, None, :], 0), -1)
    present = jnp.any(select, -1).reshape(-1)
    part = current_head % 2
    outgoing = kv_pool[local_page.reshape(-1), key_value_head, part]
    outgoing, tokens = lax.optimization_barrier((outgoing, tokens))
    received = lax.all_to_all(outgoing, "dp", split_axis=0, concat_axis=0, tiled=True)
    within = jnp.arange(page_len, dtype=jnp.int32)
    owners_mine = lax.dynamic_slice_in_dim(owner_of, me_dp * REQ_DEV, REQ_DEV, 0)
    hits = (owners_mine[None, :, :] == jnp.arange(n_dp, dtype=jnp.int32)[:, None, None]).astype(
        jnp.int32
    )
    hit_rank = jnp.cumsum(hits, -1) - 1
    chosen = (hits[:, :, None, :] == 1) & (hit_rank[:, :, None, :] == slot_ids[None, None, :, None])
    logical = jnp.sum(
        jnp.where(chosen, jnp.arange(max_pages, dtype=jnp.int32)[None, None, None, :], 0), -1
    )
    has_page = jnp.any(chosen, -1)
    key_pos = logical[..., None] * page_len + within[None, None, None, :]
    wide = tokens.astype(jnp.float32)
    meansq = jnp.mean(wide * wide, -1, keepdims=True)
    normalized_input = (wide * lax.rsqrt(meansq + 1e-05) * norm_gain.astype(jnp.float32)).astype(
        jnp.bfloat16
    )
    piece = lax.all_gather(normalized_input, "head", axis=0, tiled=True)
    w_late, piece = lax.optimization_barrier((w_out, piece))
    held_w = [w_out]
    masks = [0]
    stride = head_number // 2
    while stride > 1:
        held_w = held_w + [exchange(w_late if i == 0 else p, "head", stride) for i, p in enumerate(held_w)]
        masks = masks + [m ^ stride for m in masks]
        stride //= 2
    q_part = jnp.dot(piece, w_query, preferred_element_type=jnp.float32)
    kv_part = jnp.dot(piece, key_value_weight, preferred_element_type=jnp.float32)
    projected = jnp.concatenate([q_part, kv_part], 1)
    q_width = group_heads * head_dim
    row_ids = jnp.arange(block_rows, dtype=jnp.int32)
    my_lengths = lax.dynamic_slice_in_dim(cache_lengths, me_dp * REQ_DEV, REQ_DEV, 0)
    positions = my_lengths[row_ids // NEWTOK] + row_ids % NEWTOK
    queries = rotate(
        projected[:, :q_width].reshape(block_rows, group_heads, head_dim), positions
    ).astype(jnp.bfloat16)
    own_part = projected[:, q_width:]
    holds_keys = current_head % 2 == 0
    turned = rotate(own_part[:, None, :], positions)[:, 0]
    own_ready = jnp.where(holds_keys, turned, own_part).astype(jnp.bfloat16)
    partner_ready = from_partner(own_ready, "head", 0)
    new_keys = jnp.where(holds_keys, own_ready, partner_ready)
    new_values = jnp.where(holds_keys, partner_ready, own_ready)
    mask_rows = lax.dynamic_slice_in_dim(token_mask, me_dp * block_rows, block_rows, 0)
    cache_ok = (has_page[:, 0, :, None] & (key_pos[:, 0] < my_lengths[0])).reshape(-1)
    key_ok = jnp.concatenate([cache_ok, mask_rows == 1])
    bias = jnp.where(key_ok, 0.0, -jnp.inf).astype(jnp.float32)
    queries = queries[0:NEWTOK].reshape(NEWTOK, group_heads * head_dim)
    received, queries, new_keys, new_values = lax.optimization_barrier(
        (received, queries, new_keys, new_values)
    )
    other_half = exchange(received, "head", 1)
    pieces = attend(
        queries,
        received.reshape(-1, head_dim),
        other_half.reshape(-1, head_dim),
        new_keys,
        new_values,
        part,
        bias.reshape(1, -1),
    )
    late_w, pieces = lax.optimization_barrier((held_w[1:], pieces))
    held_w = held_w[:1] + list(late_w)
    held_w = held_w + [exchange(piece, "head", 1) for piece in held_w]
    masks = masks + [m ^ 1 for m in masks]
    held_w = jnp.concatenate(held_w, 0)
    columns = []
    for m in masks:
        block = lax.dynamic_slice_in_dim(pieces, (current_head ^ m) * local_rows, local_rows, 0)
        columns.append(block if m == 0 else exchange(block, "head", m))
    ordered = jnp.concatenate(columns, 1)
    out = jnp.dot(ordered, held_w, preferred_element_type=jnp.float32)
    return out.astype(jnp.bfloat16)


def solution(mesh):
    in_specs = (
        P(("dp", "head"), None),
        P(),
        P(None, "head"),
        P(None, "head"),
        P("head", None),
        P("dp", None, None, None, None),
        P(),
        P(),
        P(),
    )
    out_specs = P(("dp", "head"), None)
    return jax.shard_map(body, mesh=mesh, in_specs=in_specs, out_specs=out_specs, check_vma=False)
```

```python
import math

import jax
import jax.numpy as jnp
from jax import lax
from jax.sharding import PartitionSpec as P
from jax.experimental import pallas as pl
from jax.experimental.pallas import tpu as pltpu

KEY_VALUE_HEADS = 2
HEAD_SIZE = 128
NEWTOK = 512
REQ_DEV = 1


rope_base = 100000000000.0


def from_partner(value, axis, stride):
    mask = 2**stride
    pairs = [(source, source ^ mask) for source in range(lax.axis_size(axis))]
    return lax.ppermute(value, axis, pairs)


def attend_kernel(
    n_cache, tk, scale, part_ref, q_ref, mine_hbm, other_hbm, nk_hbm, nv_hbm, bias_ref,
    o_ref, k_scr, v_scr, s_scr, sems,
):
    bq, head_dim = q_ref.shape
    total = k_scr.shape[0]
    groups = tk // 128

    @pl.when(pl.program_id(0) == 0)
    def _():
        def load(src_k, src_v):
            copies = [
                pltpu.make_async_copy(src_k, k_scr.at[pl.ds(0, n_cache)], sems.at[0]),
                pltpu.make_async_copy(src_v, v_scr.at[pl.ds(0, n_cache)], sems.at[1]),
                pltpu.make_async_copy(nk_hbm, k_scr.at[pl.ds(n_cache, total - n_cache)], sems.at[2]),
                pltpu.make_async_copy(nv_hbm, v_scr.at[pl.ds(n_cache, total - n_cache)], sems.at[3]),
            ]
            for copy in copies:
                copy.start()
            for copy in copies:
                copy.wait()

        @pl.when(part_ref[0] == 0)
        def _():
            load(mine_hbm, other_hbm)

        @pl.when(part_ref[0] != 0)
        def _():
            load(other_hbm, mine_hbm)

    q = q_ref[...]
    row = lax.broadcasted_iota(jnp.int32, (bq, tk), 0)
    lane = lax.broadcasted_iota(jnp.int32, (bq, tk), 1)

    def scores(c, top, causal):
        start = pl.multiple_of(c * tk, tk)
        keys = k_scr[pl.ds(start, tk), :]
        s = lax.dot_general(q, keys, (((1,), (1,)), ((), ())), preferred_element_type=jnp.float32)
        s = s * scale + bias_ref[:, pl.ds(start, tk)]
        if causal:
            s = jnp.where(start - n_cache + lane <= row, s, -jnp.inf)
        s_scr[:, pl.ds(start, tk)] = s
        for g in range(groups):
            top = jnp.maximum(top, s[:, g * 128:(g + 1) * 128])
        return top

    top = jnp.full((bq, 128), -jnp.inf, jnp.float32)
    top = lax.fori_loop(0, n_cache // tk, lambda c, t: scores(c, t, False), top, unroll=8)
    top = lax.fori_loop(n_cache // tk, total // tk, lambda c, t: scores(c, t, True), top)
    top = jnp.max(top, -1, keepdims=True)

    def expo(c, part):
        start = pl.multiple_of(c * tk, tk)
        e = jnp.exp(s_scr[:, pl.ds(start, tk)] - top)
        s_scr[:, pl.ds(start, tk)] = e
        for g in range(groups):
            part = part + e[:, g * 128:(g + 1) * 128]
        return part

    part = lax.fori_loop(0, total // tk, expo, jnp.zeros((bq, 128), jnp.float32), unroll=8)
    inverse = 1.0 / jnp.sum(part, -1, keepdims=True)

    def weigh(c, acc):
        start = pl.multiple_of(c * tk, tk)
        w = (s_scr[:, pl.ds(start, tk)] * inverse).astype(jnp.bfloat16)
        return acc + jnp.dot(w, v_scr[pl.ds(start, tk), :], preferred_element_type=jnp.float32)

    acc = lax.fori_loop(0, total // tk, weigh, jnp.zeros((bq, head_dim), jnp.float32), unroll=8)
    o_ref[...] = acc.astype(o_ref.dtype)


def attend(queries, mine, other, new_keys, new_values, part, bias):
    rows, width = queries.shape
    n_cache, head_dim = mine.shape
    total = n_cache + new_keys.shape[0]
    heads = width // head_dim
    tk = next(t for t in (512, 256, 128) if total % t == 0 and n_cache % t == 0)
    scale = 1.0 / math.sqrt(head_dim)
    cost = pl.CostEstimate(
        flops=4 * rows * total * head_dim * heads,
        transcendentals=rows * total * heads,
        bytes_accessed=2 * (2 * total * head_dim + 2 * rows * width) + 4 * total,
    )
    any_spec = pl.BlockSpec(memory_space=pl.ANY)
    grid_spec = pltpu.PrefetchScalarGridSpec(
        num_scalar_prefetch=1,
        grid=(heads,),
        in_specs=[
            pl.BlockSpec((rows, head_dim), lambda h, p: (0, h)),
            any_spec,
            any_spec,
            any_spec,
            any_spec,
            pl.BlockSpec((1, total), lambda h, p: (0, 0)),
        ],
        out_specs=pl.BlockSpec((rows, head_dim), lambda h, p: (0, h)),
        scratch_shapes=[
            pltpu.VMEM((total, head_dim), jnp.bfloat16),
            pltpu.VMEM((total, head_dim), jnp.bfloat16),
            pltpu.VMEM((rows, total), jnp.float32),
            pltpu.SemaphoreType.DMA((4,)),
        ],
    )
    return pl.pallas_call(
        lambda *refs: attend_kernel(n_cache, tk, scale, *refs),
        out_shape=jax.ShapeDtypeStruct((rows, width), jnp.bfloat16),
        grid_spec=grid_spec,
        compiler_params=pltpu.CompilerParams(dimension_semantics=("arbitrary",)),
        cost_estimate=cost,
        name="paged_prefill_attention",
    )(part.reshape(1).astype(jnp.int32), queries, mine, other, new_keys, new_values, bias)


def exchange(value, axis, mask):
    pairs = [(source, source ^ mask) for source in range(lax.axis_size(axis))]
    return lax.ppermute(value, axis, pairs)


def rotate(values, positions):
    half_dim = values.shape[-1] // 2
    freqs = jnp.exp(
        jnp.arange(half_dim, dtype=jnp.float32) * (-2.0 * math.log(rope_base) / values.shape[-1])
    )
    angles = positions.astype(jnp.float32)[:, None] * freqs[None, :]
    cosine = jnp.cos(angles)[:, None, :]
    sine = jnp.sin(angles)[:, None, :]
    first = values[..., :half_dim]
    second = values[..., half_dim:]
    return jnp.concatenate([first * cosine - second * sine, second * cosine + first * sine], -1)


def body(
    tokens,
    norm_gain,
    w_query,
    key_value_weight,
    w_out,
    kv_pool,
    cache_lengths,
    page_table,
    token_mask,
):
    n_dp = lax.axis_size("dp")
    head_number = lax.axis_size("head")
    me_dp = lax.axis_index("dp")
    current_head = lax.axis_index("head")
    local_rows = tokens.shape[0]
    block_rows = local_rows * head_number
    head_dim = HEAD_SIZE
    group_heads = w_query.shape[1] // head_dim
    page_len = kv_pool.shape[3]
    pool_rows = kv_pool.shape[0]
    max_pages = page_table.shape[1]
    slots = max_pages // n_dp
    key_value_head = current_head // (head_number // KEY_VALUE_HEADS)
    owner_of = jnp.where(page_table >= 0, page_table // pool_rows, -1)
    mine = (owner_of == me_dp).astype(jnp.int32)
    rank = jnp.cumsum(mine, 1) - 1
    slot_ids = jnp.arange(slots, dtype=jnp.int32)
    select = (mine[:, None, :] == 1) & (rank[:, None, :] == slot_ids[None, :, None])
    local_page = jnp.sum(jnp.where(select, (page_table % pool_rows)[:, None, :], 0), -1)
    present = jnp.any(select, -1).reshape(-1)
    part = current_head % 2
    outgoing = kv_pool[local_page.reshape(-1), key_value_head, part]
    outgoing, tokens = lax.optimization_barrier((outgoing, tokens))
    received = lax.all_to_all(outgoing, "dp", split_axis=0, concat_axis=0, tiled=True)
    within = jnp.arange(page_len, dtype=jnp.int32)
    owners_mine = lax.dynamic_slice_in_dim(owner_of, me_dp * REQ_DEV, REQ_DEV, 0)
    hits = (owners_mine[None, :, :] == jnp.arange(n_dp, dtype=jnp.int32)[:, None, None]).astype(
        jnp.int32
    )
    hit_rank = jnp.cumsum(hits, -1) - 1
    chosen = (hits[:, :, None, :] == 1) & (hit_rank[:, :, None, :] == slot_ids[None, None, :, None])
    logical = jnp.sum(
        jnp.where(chosen, jnp.arange(max_pages, dtype=jnp.int32)[None, None, None, :], 0), -1
    )
    has_page = jnp.any(chosen, -1)
    key_pos = logical[..., None] * page_len + within[None, None, None, :]
    wide = tokens.astype(jnp.float32)
    meansq = jnp.mean(wide * wide, -1, keepdims=True)
    normalized_input = (wide * lax.rsqrt(meansq + 1e-05) * norm_gain.astype(jnp.float32)).astype(
        jnp.bfloat16
    )
    piece = lax.all_gather(normalized_input, "head", axis=0, tiled=True)
    held_w = [w_out]
    masks = [0]
    stride = head_number // 2
    while stride > 1:
        held_w = held_w + [exchange(p, "head", stride) for p in held_w]
        masks = masks + [m ^ stride for m in masks]
        stride //= 2
    q_part = jnp.dot(piece, w_query, preferred_element_type=jnp.float32)
    kv_part = jnp.dot(piece, key_value_weight, preferred_element_type=jnp.float32)
    projected = jnp.concatenate([q_part, kv_part], 1)
    q_width = group_heads * head_dim
    row_ids = jnp.arange(block_rows, dtype=jnp.int32)
    my_lengths = lax.dynamic_slice_in_dim(cache_lengths, me_dp * REQ_DEV, REQ_DEV, 0)
    positions = my_lengths[row_ids // NEWTOK] + row_ids % NEWTOK
    queries = rotate(
        projected[:, :q_width].reshape(block_rows, group_heads, head_dim), positions
    ).astype(jnp.bfloat16)
    own_part = projected[:, q_width:]
    holds_keys = current_head % 2 == 0
    turned = rotate(own_part[:, None, :], positions)[:, 0]
    own_ready = jnp.where(holds_keys, turned, own_part).astype(jnp.bfloat16)
    partner_ready = from_partner(own_ready, "head", 0)
    new_keys = jnp.where(holds_keys, own_ready, partner_ready)
    new_values = jnp.where(holds_keys, partner_ready, own_ready)
    mask_rows = lax.dynamic_slice_in_dim(token_mask, me_dp * block_rows, block_rows, 0)
    cache_ok = (has_page[:, 0, :, None] & (key_pos[:, 0] < my_lengths[0])).reshape(-1)
    key_ok = jnp.concatenate([cache_ok, mask_rows == 1])
    bias = jnp.where(key_ok, 0.0, -jnp.inf).astype(jnp.float32)
    queries = queries[0:NEWTOK].reshape(NEWTOK, group_heads * head_dim)
    received, queries, new_keys, new_values = lax.optimization_barrier(
        (received, queries, new_keys, new_values)
    )
    other_half = exchange(received, "head", 1)
    pieces = attend(
        queries,
        received.reshape(-1, head_dim),
        other_half.reshape(-1, head_dim),
        new_keys,
        new_values,
        part,
        bias.reshape(1, -1),
    )
    late_w, pieces = lax.optimization_barrier((held_w[1:], pieces))
    held_w = held_w[:1] + list(late_w)
    held_w = held_w + [exchange(piece, "head", 1) for piece in held_w]
    masks = masks + [m ^ 1 for m in masks]
    held_w = jnp.concatenate(held_w, 0)
    columns = []
    for m in masks:
        block = lax.dynamic_slice_in_dim(pieces, (current_head ^ m) * local_rows, local_rows, 0)
        columns.append(block if m == 0 else exchange(block, "head", m))
    ordered = jnp.concatenate(columns, 1)
    out = jnp.dot(ordered, held_w, preferred_element_type=jnp.float32)
    return out.astype(jnp.bfloat16)


def solution(mesh):
    in_specs = (
        P(("dp", "head"), None),
        P(),
        P(None, "head"),
        P(None, "head"),
        P("head", None),
        P("dp", None, None, None, None),
        P(),
        P(),
        P(),
    )
    out_specs = P(("dp", "head"), None)
    return jax.shard_map(body, mesh=mesh, in_specs=in_specs, out_specs=out_specs, check_vma=False)
```

```python
import math

import jax
import jax.numpy as jnp
from jax import lax
from jax.sharding import PartitionSpec as P
from jax.experimental import pallas as pl
from jax.experimental.pallas import tpu as pltpu

KEY_VALUE_HEADS = 2
HEAD_SIZE = 128
NEWTOK = 512
REQ_DEV = 1


rope_base = 100000000000.0


def from_partner(value, axis, stride):
    mask = 2**stride
    pairs = [(source, source ^ mask) for source in range(lax.axis_size(axis))]
    return lax.ppermute(value, axis, pairs)


def attend_kernel(
    n_cache, tk, scale, part_ref, q_ref, mine_hbm, other_hbm, nk_hbm, nv_hbm, bias_ref,
    o_ref, k_scr, v_scr, s_scr, sems,
):
    bq, head_dim = q_ref.shape
    total = k_scr.shape[0]
    groups = tk // 128

    @pl.when(pl.program_id(0) == 0)
    def _():
        def load(src_k, src_v):
            copies = [
                pltpu.make_async_copy(src_k, k_scr.at[pl.ds(0, n_cache)], sems.at[0]),
                pltpu.make_async_copy(src_v, v_scr.at[pl.ds(0, n_cache)], sems.at[1]),
                pltpu.make_async_copy(nk_hbm, k_scr.at[pl.ds(n_cache, total - n_cache)], sems.at[2]),
                pltpu.make_async_copy(nv_hbm, v_scr.at[pl.ds(n_cache, total - n_cache)], sems.at[3]),
            ]
            for copy in copies:
                copy.start()
            for copy in copies:
                copy.wait()

        @pl.when(part_ref[0] == 0)
        def _():
            load(mine_hbm, other_hbm)

        @pl.when(part_ref[0] != 0)
        def _():
            load(other_hbm, mine_hbm)

    q = q_ref[...]
    row = lax.broadcasted_iota(jnp.int32, (bq, tk), 0)
    lane = lax.broadcasted_iota(jnp.int32, (bq, tk), 1)

    def scores(c, top, causal):
        start = pl.multiple_of(c * tk, tk)
        keys = k_scr[pl.ds(start, tk), :]
        s = lax.dot_general(q, keys, (((1,), (1,)), ((), ())), preferred_element_type=jnp.float32)
        s = s * scale + bias_ref[:, pl.ds(start, tk)]
        if causal:
            s = jnp.where(start - n_cache + lane <= row, s, -jnp.inf)
        s_scr[:, pl.ds(start, tk)] = s
        for g in range(groups):
            top = jnp.maximum(top, s[:, g * 128:(g + 1) * 128])
        return top

    top = jnp.full((bq, 128), -jnp.inf, jnp.float32)
    top = lax.fori_loop(0, n_cache // tk, lambda c, t: scores(c, t, False), top, unroll=8)
    top = lax.fori_loop(n_cache // tk, total // tk, lambda c, t: scores(c, t, True), top)
    top = jnp.max(top, -1, keepdims=True)

    def expo(c, part):
        start = pl.multiple_of(c * tk, tk)
        e = jnp.exp(s_scr[:, pl.ds(start, tk)] - top)
        s_scr[:, pl.ds(start, tk)] = e
        for g in range(groups):
            part = part + e[:, g * 128:(g + 1) * 128]
        return part

    part = lax.fori_loop(0, total // tk, expo, jnp.zeros((bq, 128), jnp.float32), unroll=8)
    inverse = 1.0 / jnp.sum(part, -1, keepdims=True)

    def weigh(c, acc):
        start = pl.multiple_of(c * tk, tk)
        w = (s_scr[:, pl.ds(start, tk)] * inverse).astype(jnp.bfloat16)
        return acc + jnp.dot(w, v_scr[pl.ds(start, tk), :], preferred_element_type=jnp.float32)

    acc = lax.fori_loop(0, total // tk, weigh, jnp.zeros((bq, head_dim), jnp.float32), unroll=8)
    o_ref[...] = acc.astype(o_ref.dtype)


def attend(queries, mine, other, new_keys, new_values, part, bias):
    rows, width = queries.shape
    n_cache, head_dim = mine.shape
    total = n_cache + new_keys.shape[0]
    heads = width // head_dim
    tk = next(t for t in (512, 256, 128) if total % t == 0 and n_cache % t == 0)
    scale = 1.0 / math.sqrt(head_dim)
    cost = pl.CostEstimate(
        flops=4 * rows * total * head_dim * heads,
        transcendentals=rows * total * heads,
        bytes_accessed=2 * (2 * total * head_dim + 2 * rows * width) + 4 * total,
    )
    any_spec = pl.BlockSpec(memory_space=pl.ANY)
    grid_spec = pltpu.PrefetchScalarGridSpec(
        num_scalar_prefetch=1,
        grid=(heads,),
        in_specs=[
            pl.BlockSpec((rows, head_dim), lambda h, p: (0, h)),
            any_spec,
            any_spec,
            any_spec,
            any_spec,
            pl.BlockSpec((1, total), lambda h, p: (0, 0)),
        ],
        out_specs=pl.BlockSpec((rows, head_dim), lambda h, p: (0, h)),
        scratch_shapes=[
            pltpu.VMEM((total, head_dim), jnp.bfloat16),
            pltpu.VMEM((total, head_dim), jnp.bfloat16),
            pltpu.VMEM((rows, total), jnp.float32),
            pltpu.SemaphoreType.DMA((4,)),
        ],
    )
    return pl.pallas_call(
        lambda *refs: attend_kernel(n_cache, tk, scale, *refs),
        out_shape=jax.ShapeDtypeStruct((rows, width), jnp.bfloat16),
        grid_spec=grid_spec,
        compiler_params=pltpu.CompilerParams(dimension_semantics=("arbitrary",)),
        cost_estimate=cost,
        name="paged_prefill_attention",
    )(part.reshape(1).astype(jnp.int32), queries, mine, other, new_keys, new_values, bias)


def exchange(value, axis, mask):
    pairs = [(source, source ^ mask) for source in range(lax.axis_size(axis))]
    return lax.ppermute(value, axis, pairs)


def rotate(values, positions):
    half_dim = values.shape[-1] // 2
    freqs = jnp.exp(
        jnp.arange(half_dim, dtype=jnp.float32) * (-2.0 * math.log(rope_base) / values.shape[-1])
    )
    angles = positions.astype(jnp.float32)[:, None] * freqs[None, :]
    cosine = jnp.cos(angles)[:, None, :]
    sine = jnp.sin(angles)[:, None, :]
    first = values[..., :half_dim]
    second = values[..., half_dim:]
    return jnp.concatenate([first * cosine - second * sine, second * cosine + first * sine], -1)


def body(
    tokens,
    norm_gain,
    w_query,
    key_value_weight,
    w_out,
    kv_pool,
    cache_lengths,
    page_table,
    token_mask,
):
    n_dp = lax.axis_size("dp")
    head_number = lax.axis_size("head")
    me_dp = lax.axis_index("dp")
    current_head = lax.axis_index("head")
    local_rows = tokens.shape[0]
    block_rows = local_rows * head_number
    head_dim = HEAD_SIZE
    group_heads = w_query.shape[1] // head_dim
    page_len = kv_pool.shape[3]
    pool_rows = kv_pool.shape[0]
    max_pages = page_table.shape[1]
    slots = max_pages // n_dp
    key_value_head = current_head // (head_number // KEY_VALUE_HEADS)
    owner_of = jnp.where(page_table >= 0, page_table // pool_rows, -1)
    mine = (owner_of == me_dp).astype(jnp.int32)
    rank = jnp.cumsum(mine, 1) - 1
    slot_ids = jnp.arange(slots, dtype=jnp.int32)
    select = (mine[:, None, :] == 1) & (rank[:, None, :] == slot_ids[None, :, None])
    local_page = jnp.sum(jnp.where(select, (page_table % pool_rows)[:, None, :], 0), -1)
    present = jnp.any(select, -1).reshape(-1)
    part = current_head % 2
    outgoing = kv_pool[local_page.reshape(-1), key_value_head, part]
    outgoing, tokens = lax.optimization_barrier((outgoing, tokens))
    received = lax.all_to_all(outgoing, "dp", split_axis=0, concat_axis=0, tiled=True)
    within = jnp.arange(page_len, dtype=jnp.int32)
    owners_mine = lax.dynamic_slice_in_dim(owner_of, me_dp * REQ_DEV, REQ_DEV, 0)
    hits = (owners_mine[None, :, :] == jnp.arange(n_dp, dtype=jnp.int32)[:, None, None]).astype(
        jnp.int32
    )
    hit_rank = jnp.cumsum(hits, -1) - 1
    chosen = (hits[:, :, None, :] == 1) & (hit_rank[:, :, None, :] == slot_ids[None, None, :, None])
    logical = jnp.sum(
        jnp.where(chosen, jnp.arange(max_pages, dtype=jnp.int32)[None, None, None, :], 0), -1
    )
    has_page = jnp.any(chosen, -1)
    key_pos = logical[..., None] * page_len + within[None, None, None, :]
    wide = tokens.astype(jnp.float32)
    meansq = jnp.mean(wide * wide, -1, keepdims=True)
    normalized_input = (wide * lax.rsqrt(meansq + 1e-05) * norm_gain.astype(jnp.float32)).astype(
        jnp.bfloat16
    )
    rows_in = [normalized_input]
    masks = [0]
    stride = head_number // 2
    while stride >= 1:
        rows_in = rows_in + [exchange(p, "head", stride) for p in rows_in]
        masks = masks + [m ^ stride for m in masks]
        stride //= 2
    piece = jnp.zeros((block_rows, normalized_input.shape[1]), normalized_input.dtype)
    for p, m in zip(rows_in, masks):
        piece = lax.dynamic_update_slice_in_dim(piece, p, (current_head ^ m) * local_rows, 0)
    held_w = [w_out]
    masks = [0]
    stride = head_number // 2
    while stride > 1:
        held_w = held_w + [exchange(p, "head", stride) for p in held_w]
        masks = masks + [m ^ stride for m in masks]
        stride //= 2
    q_part = jnp.dot(piece, w_query, preferred_element_type=jnp.float32)
    kv_part = jnp.dot(piece, key_value_weight, preferred_element_type=jnp.float32)
    projected = jnp.concatenate([q_part, kv_part], 1)
    q_width = group_heads * head_dim
    row_ids = jnp.arange(block_rows, dtype=jnp.int32)
    my_lengths = lax.dynamic_slice_in_dim(cache_lengths, me_dp * REQ_DEV, REQ_DEV, 0)
    positions = my_lengths[row_ids // NEWTOK] + row_ids % NEWTOK
    queries = rotate(
        projected[:, :q_width].reshape(block_rows, group_heads, head_dim), positions
    ).astype(jnp.bfloat16)
    own_part = projected[:, q_width:]
    holds_keys = current_head % 2 == 0
    turned = rotate(own_part[:, None, :], positions)[:, 0]
    own_ready = jnp.where(holds_keys, turned, own_part).astype(jnp.bfloat16)
    partner_ready = from_partner(own_ready, "head", 0)
    new_keys = jnp.where(holds_keys, own_ready, partner_ready)
    new_values = jnp.where(holds_keys, partner_ready, own_ready)
    mask_rows = lax.dynamic_slice_in_dim(token_mask, me_dp * block_rows, block_rows, 0)
    cache_ok = (has_page[:, 0, :, None] & (key_pos[:, 0] < my_lengths[0])).reshape(-1)
    key_ok = jnp.concatenate([cache_ok, mask_rows == 1])
    bias = jnp.where(key_ok, 0.0, -jnp.inf).astype(jnp.float32)
    queries = queries[0:NEWTOK].reshape(NEWTOK, group_heads * head_dim)
    received, queries, new_keys, new_values = lax.optimization_barrier(
        (received, queries, new_keys, new_values)
    )
    other_half = exchange(received, "head", 1)
    pieces = attend(
        queries,
        received.reshape(-1, head_dim),
        other_half.reshape(-1, head_dim),
        new_keys,
        new_values,
        part,
        bias.reshape(1, -1),
    )
    late_w, pieces = lax.optimization_barrier((held_w[1:], pieces))
    held_w = held_w[:1] + list(late_w)
    held_w = held_w + [exchange(piece, "head", 1) for piece in held_w]
    masks = masks + [m ^ 1 for m in masks]
    held_w = jnp.concatenate(held_w, 0)
    columns = []
    for m in masks:
        block = lax.dynamic_slice_in_dim(pieces, (current_head ^ m) * local_rows, local_rows, 0)
        columns.append(block if m == 0 else exchange(block, "head", m))
    ordered = jnp.concatenate(columns, 1)
    out = jnp.dot(ordered, held_w, preferred_element_type=jnp.float32)
    return out.astype(jnp.bfloat16)


def solution(mesh):
    in_specs = (
        P(("dp", "head"), None),
        P(),
        P(None, "head"),
        P(None, "head"),
        P("head", None),
        P("dp", None, None, None, None),
        P(),
        P(),
        P(),
    )
    out_specs = P(("dp", "head"), None)
    return jax.shard_map(body, mesh=mesh, in_specs=in_specs, out_specs=out_specs, check_vma=False)
```

```python
import math

import jax
import jax.numpy as jnp
from jax import lax
from jax.sharding import PartitionSpec as P
from jax.experimental import pallas as pl
from jax.experimental.pallas import tpu as pltpu

KEY_VALUE_HEADS = 2
HEAD_SIZE = 128
NEWTOK = 512
REQ_DEV = 1


rope_base = 100000000000.0


def from_partner(value, axis, stride):
    mask = 2**stride
    pairs = [(source, source ^ mask) for source in range(lax.axis_size(axis))]
    return lax.ppermute(value, axis, pairs)


def attend_kernel(
    n_cache, tk, scale, part_ref, q_ref, mine_hbm, other_hbm, nk_hbm, nv_hbm, bias_ref,
    row_ref, key_ref, o_ref, k_scr, v_scr, s_scr, sems,
):
    bq, head_dim = q_ref.shape
    total = k_scr.shape[0]
    groups = tk // 128

    @pl.when(pl.program_id(0) == 0)
    def _():
        def load(src_k, src_v):
            copies = [
                pltpu.make_async_copy(src_k, k_scr.at[pl.ds(0, n_cache)], sems.at[0]),
                pltpu.make_async_copy(src_v, v_scr.at[pl.ds(0, n_cache)], sems.at[1]),
                pltpu.make_async_copy(nk_hbm, k_scr.at[pl.ds(n_cache, total - n_cache)], sems.at[2]),
                pltpu.make_async_copy(nv_hbm, v_scr.at[pl.ds(n_cache, total - n_cache)], sems.at[3]),
            ]
            for copy in copies:
                copy.start()
            for copy in copies:
                copy.wait()

        @pl.when(part_ref[0] == 0)
        def _():
            load(mine_hbm, other_hbm)

        @pl.when(part_ref[0] != 0)
        def _():
            load(other_hbm, mine_hbm)

    q = q_ref[...]

    def scores(c, top, causal):
        start = pl.multiple_of(c * tk, tk)
        keys = k_scr[pl.ds(start, tk), :]
        s = lax.dot_general(q, keys, (((1,), (1,)), ((), ())), preferred_element_type=jnp.float32)
        s = s * scale + bias_ref[:, pl.ds(start, tk)]
        if causal:
            s = jnp.where(key_ref[:, pl.ds(start - n_cache, tk)] <= row_ref[...], s, -jnp.inf)
        s_scr[:, pl.ds(start, tk)] = s
        for g in range(groups):
            top = jnp.maximum(top, s[:, g * 128:(g + 1) * 128])
        return top

    top = jnp.full((bq, 128), -jnp.inf, jnp.float32)
    top = lax.fori_loop(0, n_cache // tk, lambda c, t: scores(c, t, False), top, unroll=8)
    top = lax.fori_loop(n_cache // tk, total // tk, lambda c, t: scores(c, t, True), top)
    top = jnp.max(top, -1, keepdims=True)

    def expo(c, part):
        start = pl.multiple_of(c * tk, tk)
        e = jnp.exp(s_scr[:, pl.ds(start, tk)] - top)
        s_scr[:, pl.ds(start, tk)] = e
        for g in range(groups):
            part = part + e[:, g * 128:(g + 1) * 128]
        return part

    part = lax.fori_loop(0, total // tk, expo, jnp.zeros((bq, 128), jnp.float32), unroll=8)
    inverse = 1.0 / jnp.sum(part, -1, keepdims=True)

    def weigh(c, acc):
        start = pl.multiple_of(c * tk, tk)
        w = (s_scr[:, pl.ds(start, tk)] * inverse).astype(jnp.bfloat16)
        return acc + jnp.dot(w, v_scr[pl.ds(start, tk), :], preferred_element_type=jnp.float32)

    acc = lax.fori_loop(0, total // tk, weigh, jnp.zeros((bq, head_dim), jnp.float32), unroll=8)
    o_ref[...] = acc.astype(o_ref.dtype)


def attend(queries, mine, other, new_keys, new_values, part, bias, true_row):
    rows, width = queries.shape
    n_cache, head_dim = mine.shape
    total = n_cache + new_keys.shape[0]
    heads = width // head_dim
    tk = next(t for t in (512, 256, 128) if total % t == 0 and n_cache % t == 0)
    scale = 1.0 / math.sqrt(head_dim)
    cost = pl.CostEstimate(
        flops=4 * rows * total * head_dim * heads,
        transcendentals=rows * total * heads,
        bytes_accessed=2 * (2 * total * head_dim + 2 * rows * width) + 4 * total,
    )
    any_spec = pl.BlockSpec(memory_space=pl.ANY)
    grid_spec = pltpu.PrefetchScalarGridSpec(
        num_scalar_prefetch=1,
        grid=(heads,),
        in_specs=[
            pl.BlockSpec((rows, head_dim), lambda h, p: (0, h)),
            any_spec,
            any_spec,
            any_spec,
            any_spec,
            pl.BlockSpec((1, total), lambda h, p: (0, 0)),
            pl.BlockSpec((rows, 1), lambda h, p: (0, 0)),
            pl.BlockSpec((1, rows), lambda h, p: (0, 0)),
        ],
        out_specs=pl.BlockSpec((rows, head_dim), lambda h, p: (0, h)),
        scratch_shapes=[
            pltpu.VMEM((total, head_dim), jnp.bfloat16),
            pltpu.VMEM((total, head_dim), jnp.bfloat16),
            pltpu.VMEM((rows, total), jnp.float32),
            pltpu.SemaphoreType.DMA((4,)),
        ],
    )
    return pl.pallas_call(
        lambda *refs: attend_kernel(n_cache, tk, scale, *refs),
        out_shape=jax.ShapeDtypeStruct((rows, width), jnp.bfloat16),
        grid_spec=grid_spec,
        compiler_params=pltpu.CompilerParams(dimension_semantics=("arbitrary",)),
        cost_estimate=cost,
        name="paged_prefill_attention",
    )(
        part.reshape(1).astype(jnp.int32), queries, mine, other, new_keys, new_values, bias,
        true_row.reshape(rows, 1), true_row.reshape(1, rows),
    )


def exchange(value, axis, mask):
    pairs = [(source, source ^ mask) for source in range(lax.axis_size(axis))]
    return lax.ppermute(value, axis, pairs)


def rotate(values, positions):
    half_dim = values.shape[-1] // 2
    freqs = jnp.exp(
        jnp.arange(half_dim, dtype=jnp.float32) * (-2.0 * math.log(rope_base) / values.shape[-1])
    )
    angles = positions.astype(jnp.float32)[:, None] * freqs[None, :]
    cosine = jnp.cos(angles)[:, None, :]
    sine = jnp.sin(angles)[:, None, :]
    first = values[..., :half_dim]
    second = values[..., half_dim:]
    return jnp.concatenate([first * cosine - second * sine, second * cosine + first * sine], -1)


def body(
    tokens,
    norm_gain,
    w_query,
    key_value_weight,
    w_out,
    kv_pool,
    cache_lengths,
    page_table,
    token_mask,
):
    n_dp = lax.axis_size("dp")
    head_number = lax.axis_size("head")
    me_dp = lax.axis_index("dp")
    current_head = lax.axis_index("head")
    local_rows = tokens.shape[0]
    block_rows = local_rows * head_number
    head_dim = HEAD_SIZE
    group_heads = w_query.shape[1] // head_dim
    page_len = kv_pool.shape[3]
    pool_rows = kv_pool.shape[0]
    max_pages = page_table.shape[1]
    slots = max_pages // n_dp
    key_value_head = current_head // (head_number // KEY_VALUE_HEADS)
    owner_of = jnp.where(page_table >= 0, page_table // pool_rows, -1)
    mine = (owner_of == me_dp).astype(jnp.int32)
    rank = jnp.cumsum(mine, 1) - 1
    slot_ids = jnp.arange(slots, dtype=jnp.int32)
    select = (mine[:, None, :] == 1) & (rank[:, None, :] == slot_ids[None, :, None])
    local_page = jnp.sum(jnp.where(select, (page_table % pool_rows)[:, None, :], 0), -1)
    present = jnp.any(select, -1).reshape(-1)
    part = current_head % 2
    outgoing = kv_pool[local_page.reshape(-1), key_value_head, part]
    outgoing, tokens = lax.optimization_barrier((outgoing, tokens))
    received = lax.all_to_all(outgoing, "dp", split_axis=0, concat_axis=0, tiled=True)
    within = jnp.arange(page_len, dtype=jnp.int32)
    owners_mine = lax.dynamic_slice_in_dim(owner_of, me_dp * REQ_DEV, REQ_DEV, 0)
    hits = (owners_mine[None, :, :] == jnp.arange(n_dp, dtype=jnp.int32)[:, None, None]).astype(
        jnp.int32
    )
    hit_rank = jnp.cumsum(hits, -1) - 1
    chosen = (hits[:, :, None, :] == 1) & (hit_rank[:, :, None, :] == slot_ids[None, None, :, None])
    logical = jnp.sum(
        jnp.where(chosen, jnp.arange(max_pages, dtype=jnp.int32)[None, None, None, :], 0), -1
    )
    has_page = jnp.any(chosen, -1)
    key_pos = logical[..., None] * page_len + within[None, None, None, :]
    wide = tokens.astype(jnp.float32)
    meansq = jnp.mean(wide * wide, -1, keepdims=True)
    normalized_input = (wide * lax.rsqrt(meansq + 1e-05) * norm_gain.astype(jnp.float32)).astype(
        jnp.bfloat16
    )
    rows_in = [normalized_input]
    row_masks = [0]
    stride = head_number // 2
    while stride >= 1:
        rows_in = rows_in + [exchange(p, "head", stride) for p in rows_in]
        row_masks = row_masks + [m ^ stride for m in row_masks]
        stride //= 2
    piece = jnp.concatenate(rows_in, 0)
    within_rows = jnp.arange(local_rows, dtype=jnp.int32)
    true_row = jnp.concatenate([(current_head ^ m) * local_rows + within_rows for m in row_masks])
    held_w = [w_out]
    masks = [0]
    stride = head_number // 2
    while stride > 1:
        held_w = held_w + [exchange(p, "head", stride) for p in held_w]
        masks = masks + [m ^ stride for m in masks]
        stride //= 2
    q_part = jnp.dot(piece, w_query, preferred_element_type=jnp.float32)
    kv_part = jnp.dot(piece, key_value_weight, preferred_element_type=jnp.float32)
    projected = jnp.concatenate([q_part, kv_part], 1)
    q_width = group_heads * head_dim
    my_lengths = lax.dynamic_slice_in_dim(cache_lengths, me_dp * REQ_DEV, REQ_DEV, 0)
    positions = my_lengths[true_row // NEWTOK] + true_row % NEWTOK
    queries = rotate(
        projected[:, :q_width].reshape(block_rows, group_heads, head_dim), positions
    ).astype(jnp.bfloat16)
    own_part = projected[:, q_width:]
    holds_keys = current_head % 2 == 0
    turned = rotate(own_part[:, None, :], positions)[:, 0]
    own_ready = jnp.where(holds_keys, turned, own_part).astype(jnp.bfloat16)
    partner_ready = from_partner(own_ready, "head", 0)
    partner_blocks = [row_masks.index(m ^ 1) for m in row_masks]
    partner_ready = jnp.concatenate(
        [partner_ready[j * local_rows:(j + 1) * local_rows] for j in partner_blocks], 0
    )
    new_keys = jnp.where(holds_keys, own_ready, partner_ready)
    new_values = jnp.where(holds_keys, partner_ready, own_ready)
    mask_rows = lax.dynamic_slice_in_dim(token_mask, me_dp * block_rows, block_rows, 0)
    cache_ok = (has_page[:, 0, :, None] & (key_pos[:, 0] < my_lengths[0])).reshape(-1)
    key_ok = jnp.concatenate([cache_ok, jnp.take(mask_rows, true_row) == 1])
    bias = jnp.where(key_ok, 0.0, -jnp.inf).astype(jnp.float32)
    queries = queries[0:NEWTOK].reshape(NEWTOK, group_heads * head_dim)
    received, queries, new_keys, new_values = lax.optimization_barrier(
        (received, queries, new_keys, new_values)
    )
    other_half = exchange(received, "head", 1)
    pieces = attend(
        queries,
        received.reshape(-1, head_dim),
        other_half.reshape(-1, head_dim),
        new_keys,
        new_values,
        part,
        bias.reshape(1, -1),
        true_row,
    )
    late_w, pieces = lax.optimization_barrier((held_w[1:], pieces))
    held_w = held_w[:1] + list(late_w)
    held_w = held_w + [exchange(piece, "head", 1) for piece in held_w]
    masks = masks + [m ^ 1 for m in masks]
    held_w = jnp.concatenate(held_w, 0)
    columns = []
    for m in masks:
        k = row_masks.index(m)
        block = pieces[k * local_rows:(k + 1) * local_rows]
        columns.append(block if m == 0 else exchange(block, "head", m))
    ordered = jnp.concatenate(columns, 1)
    out = jnp.dot(ordered, held_w, preferred_element_type=jnp.float32)
    return out.astype(jnp.bfloat16)


def solution(mesh):
    in_specs = (
        P(("dp", "head"), None),
        P(),
        P(None, "head"),
        P(None, "head"),
        P("head", None),
        P("dp", None, None, None, None),
        P(),
        P(),
        P(),
    )
    out_specs = P(("dp", "head"), None)
    return jax.shard_map(body, mesh=mesh, in_specs=in_specs, out_specs=out_specs, check_vma=False)
```

```python
import math

import jax
import jax.numpy as jnp
from jax import lax
from jax.sharding import PartitionSpec as P
from jax.experimental import pallas as pl
from jax.experimental.pallas import tpu as pltpu

KEY_VALUE_HEADS = 2
HEAD_SIZE = 128
NEWTOK = 512
REQ_DEV = 1


rope_base = 100000000000.0


def from_partner(value, axis, stride):
    mask = 2**stride
    pairs = [(source, source ^ mask) for source in range(lax.axis_size(axis))]
    return lax.ppermute(value, axis, pairs)


def attend_kernel(
    n_cache, tk, scale, part_ref, q_ref, mine_hbm, other_hbm, nk_hbm, nv_hbm, bias_ref,
    row_ref, key_ref, o_ref, k_scr, v_scr, s_scr, sems,
):
    bq, head_dim = q_ref.shape
    total = k_scr.shape[0]
    groups = tk // 128

    @pl.when(pl.program_id(0) == 0)
    def _():
        def load(src_k, src_v):
            copies = [
                pltpu.make_async_copy(src_k, k_scr.at[pl.ds(0, n_cache)], sems.at[0]),
                pltpu.make_async_copy(src_v, v_scr.at[pl.ds(0, n_cache)], sems.at[1]),
                pltpu.make_async_copy(nk_hbm, k_scr.at[pl.ds(n_cache, total - n_cache)], sems.at[2]),
                pltpu.make_async_copy(nv_hbm, v_scr.at[pl.ds(n_cache, total - n_cache)], sems.at[3]),
            ]
            for copy in copies:
                copy.start()
            for copy in copies:
                copy.wait()

        @pl.when(part_ref[0] == 0)
        def _():
            load(mine_hbm, other_hbm)

        @pl.when(part_ref[0] != 0)
        def _():
            load(other_hbm, mine_hbm)

    q = q_ref[...]

    def scores(c, top, causal):
        start = pl.multiple_of(c * tk, tk)
        keys = k_scr[pl.ds(start, tk), :]
        s = lax.dot_general(q, keys, (((1,), (1,)), ((), ())), preferred_element_type=jnp.float32)
        s = s * scale + bias_ref[:, pl.ds(start, tk)]
        if causal:
            s = jnp.where(key_ref[:, pl.ds(start - n_cache, tk)] <= row_ref[...], s, -jnp.inf)
        s_scr[:, pl.ds(start, tk)] = s
        for g in range(groups):
            top = jnp.maximum(top, s[:, g * 128:(g + 1) * 128])
        return top

    top = jnp.full((bq, 128), -jnp.inf, jnp.float32)
    top = lax.fori_loop(0, n_cache // tk, lambda c, t: scores(c, t, False), top, unroll=8)
    top = lax.fori_loop(n_cache // tk, total // tk, lambda c, t: scores(c, t, True), top)
    top = jnp.max(top, -1, keepdims=True)

    def expo(c, part):
        start = pl.multiple_of(c * tk, tk)
        e = jnp.exp(s_scr[:, pl.ds(start, tk)] - top)
        s_scr[:, pl.ds(start, tk)] = e
        for g in range(groups):
            part = part + e[:, g * 128:(g + 1) * 128]
        return part

    part = lax.fori_loop(0, total // tk, expo, jnp.zeros((bq, 128), jnp.float32), unroll=8)
    inverse = 1.0 / jnp.sum(part, -1, keepdims=True)

    def weigh(c, acc):
        start = pl.multiple_of(c * tk, tk)
        w = (s_scr[:, pl.ds(start, tk)] * inverse).astype(jnp.bfloat16)
        return acc + jnp.dot(w, v_scr[pl.ds(start, tk), :], preferred_element_type=jnp.float32)

    acc = lax.fori_loop(0, total // tk, weigh, jnp.zeros((bq, head_dim), jnp.float32), unroll=8)
    o_ref[...] = acc.astype(o_ref.dtype)


def attend(queries, mine, other, new_keys, new_values, part, bias, true_row):
    rows, width = queries.shape
    n_cache, head_dim = mine.shape
    total = n_cache + new_keys.shape[0]
    heads = width // head_dim
    tk = next(t for t in (512, 256, 128) if total % t == 0 and n_cache % t == 0)
    scale = 1.0 / math.sqrt(head_dim)
    cost = pl.CostEstimate(
        flops=4 * rows * total * head_dim * heads,
        transcendentals=rows * total * heads,
        bytes_accessed=2 * (2 * total * head_dim + 2 * rows * width) + 4 * total,
    )
    any_spec = pl.BlockSpec(memory_space=pl.ANY)
    grid_spec = pltpu.PrefetchScalarGridSpec(
        num_scalar_prefetch=1,
        grid=(heads,),
        in_specs=[
            pl.BlockSpec((rows, head_dim), lambda h, p: (0, h)),
            any_spec,
            any_spec,
            any_spec,
            any_spec,
            pl.BlockSpec((1, total), lambda h, p: (0, 0)),
            pl.BlockSpec((rows, 1), lambda h, p: (0, 0)),
            pl.BlockSpec((1, rows), lambda h, p: (0, 0)),
        ],
        out_specs=pl.BlockSpec((rows, head_dim), lambda h, p: (0, h)),
        scratch_shapes=[
            pltpu.VMEM((total, head_dim), jnp.bfloat16),
            pltpu.VMEM((total, head_dim), jnp.bfloat16),
            pltpu.VMEM((rows, total), jnp.float32),
            pltpu.SemaphoreType.DMA((4,)),
        ],
    )
    return pl.pallas_call(
        lambda *refs: attend_kernel(n_cache, tk, scale, *refs),
        out_shape=jax.ShapeDtypeStruct((rows, width), jnp.bfloat16),
        grid_spec=grid_spec,
        compiler_params=pltpu.CompilerParams(dimension_semantics=("arbitrary",)),
        cost_estimate=cost,
        name="paged_prefill_attention",
    )(
        part.reshape(1).astype(jnp.int32), queries, mine, other, new_keys, new_values, bias,
        true_row.reshape(rows, 1), true_row.reshape(1, rows),
    )


def exchange(value, axis, mask):
    pairs = [(source, source ^ mask) for source in range(lax.axis_size(axis))]
    return lax.ppermute(value, axis, pairs)


def rotate(values, positions):
    half_dim = values.shape[-1] // 2
    freqs = jnp.exp(
        jnp.arange(half_dim, dtype=jnp.float32) * (-2.0 * math.log(rope_base) / values.shape[-1])
    )
    angles = positions.astype(jnp.float32)[:, None] * freqs[None, :]
    cosine = jnp.cos(angles)[:, None, :]
    sine = jnp.sin(angles)[:, None, :]
    first = values[..., :half_dim]
    second = values[..., half_dim:]
    return jnp.concatenate([first * cosine - second * sine, second * cosine + first * sine], -1)


def body(
    tokens,
    norm_gain,
    w_query,
    key_value_weight,
    w_out,
    kv_pool,
    cache_lengths,
    page_table,
    token_mask,
):
    n_dp = lax.axis_size("dp")
    head_number = lax.axis_size("head")
    me_dp = lax.axis_index("dp")
    current_head = lax.axis_index("head")
    local_rows = tokens.shape[0]
    block_rows = local_rows * head_number
    head_dim = HEAD_SIZE
    group_heads = w_query.shape[1] // head_dim
    page_len = kv_pool.shape[3]
    pool_rows = kv_pool.shape[0]
    max_pages = page_table.shape[1]
    slots = max_pages // n_dp
    key_value_head = current_head // (head_number // KEY_VALUE_HEADS)
    owner_of = jnp.where(page_table >= 0, page_table // pool_rows, -1)
    mine = (owner_of == me_dp).astype(jnp.int32)
    rank = jnp.cumsum(mine, 1) - 1
    slot_ids = jnp.arange(slots, dtype=jnp.int32)
    select = (mine[:, None, :] == 1) & (rank[:, None, :] == slot_ids[None, :, None])
    local_page = jnp.sum(jnp.where(select, (page_table % pool_rows)[:, None, :], 0), -1)
    present = jnp.any(select, -1).reshape(-1)
    part = current_head % 2
    outgoing = kv_pool[local_page.reshape(-1), key_value_head, part]
    outgoing, tokens = lax.optimization_barrier((outgoing, tokens))
    received = lax.all_to_all(outgoing, "dp", split_axis=0, concat_axis=0, tiled=True)
    within = jnp.arange(page_len, dtype=jnp.int32)
    owners_mine = lax.dynamic_slice_in_dim(owner_of, me_dp * REQ_DEV, REQ_DEV, 0)
    hits = (owners_mine[None, :, :] == jnp.arange(n_dp, dtype=jnp.int32)[:, None, None]).astype(
        jnp.int32
    )
    hit_rank = jnp.cumsum(hits, -1) - 1
    chosen = (hits[:, :, None, :] == 1) & (hit_rank[:, :, None, :] == slot_ids[None, None, :, None])
    logical = jnp.sum(
        jnp.where(chosen, jnp.arange(max_pages, dtype=jnp.int32)[None, None, None, :], 0), -1
    )
    has_page = jnp.any(chosen, -1)
    key_pos = logical[..., None] * page_len + within[None, None, None, :]
    wide = tokens.astype(jnp.float32)
    meansq = jnp.mean(wide * wide, -1, keepdims=True)
    normalized_input = (wide * lax.rsqrt(meansq + 1e-05) * norm_gain.astype(jnp.float32)).astype(
        jnp.bfloat16
    )
    rows_in = [normalized_input]
    row_masks = [0]
    stride = head_number // 2
    while stride >= 1:
        rows_in = rows_in + [exchange(p, "head", stride) for p in rows_in]
        row_masks = row_masks + [m ^ stride for m in row_masks]
        stride //= 2
    piece = jnp.concatenate(rows_in, 0)
    within_rows = jnp.arange(local_rows, dtype=jnp.int32)
    true_row = jnp.concatenate([(current_head ^ m) * local_rows + within_rows for m in row_masks])
    held_w = [w_out]
    masks = [0]
    stride = head_number // 2
    while stride > 1:
        held_w = held_w + [exchange(p, "head", stride) for p in held_w]
        masks = masks + [m ^ stride for m in masks]
        stride //= 2
    q_part = jnp.dot(piece, w_query, preferred_element_type=jnp.float32)
    kv_part = jnp.dot(piece, key_value_weight, preferred_element_type=jnp.float32)
    projected = jnp.concatenate([q_part, kv_part], 1)
    q_width = group_heads * head_dim
    my_lengths = lax.dynamic_slice_in_dim(cache_lengths, me_dp * REQ_DEV, REQ_DEV, 0)
    positions = my_lengths[true_row // NEWTOK] + true_row % NEWTOK
    queries = rotate(
        projected[:, :q_width].reshape(block_rows, group_heads, head_dim), positions
    ).astype(jnp.bfloat16)
    own_part = projected[:, q_width:]
    holds_keys = current_head % 2 == 0
    turned = rotate(own_part[:, None, :], positions)[:, 0]
    own_ready = jnp.where(holds_keys, turned, own_part).astype(jnp.bfloat16)
    received, own_ready = lax.optimization_barrier((received, own_ready))
    partner_ready = from_partner(own_ready, "head", 0)
    partner_blocks = [row_masks.index(m ^ 1) for m in row_masks]
    partner_ready = jnp.concatenate(
        [partner_ready[j * local_rows:(j + 1) * local_rows] for j in partner_blocks], 0
    )
    new_keys = jnp.where(holds_keys, own_ready, partner_ready)
    new_values = jnp.where(holds_keys, partner_ready, own_ready)
    mask_rows = lax.dynamic_slice_in_dim(token_mask, me_dp * block_rows, block_rows, 0)
    cache_ok = (has_page[:, 0, :, None] & (key_pos[:, 0] < my_lengths[0])).reshape(-1)
    key_ok = jnp.concatenate([cache_ok, jnp.take(mask_rows, true_row) == 1])
    bias = jnp.where(key_ok, 0.0, -jnp.inf).astype(jnp.float32)
    queries = queries[0:NEWTOK].reshape(NEWTOK, group_heads * head_dim)
    other_half = exchange(received, "head", 1)
    pieces = attend(
        queries,
        received.reshape(-1, head_dim),
        other_half.reshape(-1, head_dim),
        new_keys,
        new_values,
        part,
        bias.reshape(1, -1),
        true_row,
    )
    late_w, pieces = lax.optimization_barrier((held_w[1:], pieces))
    held_w = held_w[:1] + list(late_w)
    held_w = held_w + [exchange(piece, "head", 1) for piece in held_w]
    masks = masks + [m ^ 1 for m in masks]
    held_w = jnp.concatenate(held_w, 0)
    columns = []
    for m in masks:
        k = row_masks.index(m)
        block = pieces[k * local_rows:(k + 1) * local_rows]
        columns.append(block if m == 0 else exchange(block, "head", m))
    ordered = jnp.concatenate(columns, 1)
    out = jnp.dot(ordered, held_w, preferred_element_type=jnp.float32)
    return out.astype(jnp.bfloat16)


def solution(mesh):
    in_specs = (
        P(("dp", "head"), None),
        P(),
        P(None, "head"),
        P(None, "head"),
        P("head", None),
        P("dp", None, None, None, None),
        P(),
        P(),
        P(),
    )
    out_specs = P(("dp", "head"), None)
    return jax.shard_map(body, mesh=mesh, in_specs=in_specs, out_specs=out_specs, check_vma=False)
```

```python
import math

import jax
import jax.numpy as jnp
from jax import lax
from jax.sharding import PartitionSpec as P
from jax.experimental import pallas as pl
from jax.experimental.pallas import tpu as pltpu

KEY_VALUE_HEADS = 2
HEAD_SIZE = 128
NEWTOK = 512
REQ_DEV = 1


rope_base = 100000000000.0


def from_partner(value, axis, stride):
    mask = 2**stride
    pairs = [(source, source ^ mask) for source in range(lax.axis_size(axis))]
    return lax.ppermute(value, axis, pairs)


def attend_kernel(
    n_cache, tk, scale, part_ref, q_ref, mine_hbm, other_hbm, nk_hbm, nv_hbm, bias_ref,
    row_ref, key_ref, *rest,
):
    *o_refs, k_scr, v_scr, s_scr, sems = rest
    bq, head_dim = q_ref.shape
    total = k_scr.shape[0]
    groups = tk // 128

    @pl.when(pl.program_id(0) == 0)
    def _():
        def load(src_k, src_v):
            copies = [
                pltpu.make_async_copy(src_k, k_scr.at[pl.ds(0, n_cache)], sems.at[0]),
                pltpu.make_async_copy(src_v, v_scr.at[pl.ds(0, n_cache)], sems.at[1]),
                pltpu.make_async_copy(nk_hbm, k_scr.at[pl.ds(n_cache, total - n_cache)], sems.at[2]),
                pltpu.make_async_copy(nv_hbm, v_scr.at[pl.ds(n_cache, total - n_cache)], sems.at[3]),
            ]
            for copy in copies:
                copy.start()
            for copy in copies:
                copy.wait()

        @pl.when(part_ref[0] == 0)
        def _():
            load(mine_hbm, other_hbm)

        @pl.when(part_ref[0] != 0)
        def _():
            load(other_hbm, mine_hbm)

    q = q_ref[...]

    def scores(c, top, causal):
        start = pl.multiple_of(c * tk, tk)
        keys = k_scr[pl.ds(start, tk), :]
        s = lax.dot_general(q, keys, (((1,), (1,)), ((), ())), preferred_element_type=jnp.float32)
        s = s * scale + bias_ref[:, pl.ds(start, tk)]
        if causal:
            s = jnp.where(key_ref[:, pl.ds(start - n_cache, tk)] <= row_ref[...], s, -jnp.inf)
        s_scr[:, pl.ds(start, tk)] = s
        for g in range(groups):
            top = jnp.maximum(top, s[:, g * 128:(g + 1) * 128])
        return top

    top = jnp.full((bq, 128), -jnp.inf, jnp.float32)
    top = lax.fori_loop(0, n_cache // tk, lambda c, t: scores(c, t, False), top, unroll=8)
    top = lax.fori_loop(n_cache // tk, total // tk, lambda c, t: scores(c, t, True), top)
    top = jnp.max(top, -1, keepdims=True)

    def expo(c, part):
        start = pl.multiple_of(c * tk, tk)
        e = jnp.exp(s_scr[:, pl.ds(start, tk)] - top)
        s_scr[:, pl.ds(start, tk)] = e
        for g in range(groups):
            part = part + e[:, g * 128:(g + 1) * 128]
        return part

    part = lax.fori_loop(0, total // tk, expo, jnp.zeros((bq, 128), jnp.float32), unroll=8)
    inverse = 1.0 / jnp.sum(part, -1, keepdims=True)

    def weigh(c, acc):
        start = pl.multiple_of(c * tk, tk)
        w = (s_scr[:, pl.ds(start, tk)] * inverse).astype(jnp.bfloat16)
        return acc + jnp.dot(w, v_scr[pl.ds(start, tk), :], preferred_element_type=jnp.float32)

    acc = lax.fori_loop(0, total // tk, weigh, jnp.zeros((bq, head_dim), jnp.float32), unroll=8)
    part_rows = bq // len(o_refs)
    for k, o_ref in enumerate(o_refs):
        o_ref[...] = acc[k * part_rows:(k + 1) * part_rows].astype(o_ref.dtype)


def attend(queries, mine, other, new_keys, new_values, part, bias, true_row, splits):
    rows, width = queries.shape
    n_cache, head_dim = mine.shape
    total = n_cache + new_keys.shape[0]
    heads = width // head_dim
    tk = next(t for t in (512, 256, 128) if total % t == 0 and n_cache % t == 0)
    scale = 1.0 / math.sqrt(head_dim)
    cost = pl.CostEstimate(
        flops=4 * rows * total * head_dim * heads,
        transcendentals=rows * total * heads,
        bytes_accessed=2 * (2 * total * head_dim + 2 * rows * width) + 4 * total,
    )
    any_spec = pl.BlockSpec(memory_space=pl.ANY)
    grid_spec = pltpu.PrefetchScalarGridSpec(
        num_scalar_prefetch=1,
        grid=(heads,),
        in_specs=[
            pl.BlockSpec((rows, head_dim), lambda h, p: (0, h)),
            any_spec,
            any_spec,
            any_spec,
            any_spec,
            pl.BlockSpec((1, total), lambda h, p: (0, 0)),
            pl.BlockSpec((rows, 1), lambda h, p: (0, 0)),
            pl.BlockSpec((1, rows), lambda h, p: (0, 0)),
        ],
        out_specs=[pl.BlockSpec((rows // splits, head_dim), lambda h, p: (0, h))] * splits,
        scratch_shapes=[
            pltpu.VMEM((total, head_dim), jnp.bfloat16),
            pltpu.VMEM((total, head_dim), jnp.bfloat16),
            pltpu.VMEM((rows, total), jnp.float32),
            pltpu.SemaphoreType.DMA((4,)),
        ],
    )
    return pl.pallas_call(
        lambda *refs: attend_kernel(n_cache, tk, scale, *refs),
        out_shape=[jax.ShapeDtypeStruct((rows // splits, width), jnp.bfloat16)] * splits,
        grid_spec=grid_spec,
        compiler_params=pltpu.CompilerParams(dimension_semantics=("arbitrary",)),
        cost_estimate=cost,
        name="paged_prefill_attention",
    )(
        part.reshape(1).astype(jnp.int32), queries, mine, other, new_keys, new_values, bias,
        true_row.reshape(rows, 1), true_row.reshape(1, rows),
    )


def exchange(value, axis, mask):
    pairs = [(source, source ^ mask) for source in range(lax.axis_size(axis))]
    return lax.ppermute(value, axis, pairs)


def rotate(values, positions):
    half_dim = values.shape[-1] // 2
    freqs = jnp.exp(
        jnp.arange(half_dim, dtype=jnp.float32) * (-2.0 * math.log(rope_base) / values.shape[-1])
    )
    angles = positions.astype(jnp.float32)[:, None] * freqs[None, :]
    cosine = jnp.cos(angles)[:, None, :]
    sine = jnp.sin(angles)[:, None, :]
    first = values[..., :half_dim]
    second = values[..., half_dim:]
    return jnp.concatenate([first * cosine - second * sine, second * cosine + first * sine], -1)


def body(
    tokens,
    norm_gain,
    w_query,
    key_value_weight,
    w_out,
    kv_pool,
    cache_lengths,
    page_table,
    token_mask,
):
    n_dp = lax.axis_size("dp")
    head_number = lax.axis_size("head")
    me_dp = lax.axis_index("dp")
    current_head = lax.axis_index("head")
    local_rows = tokens.shape[0]
    block_rows = local_rows * head_number
    head_dim = HEAD_SIZE
    group_heads = w_query.shape[1] // head_dim
    page_len = kv_pool.shape[3]
    pool_rows = kv_pool.shape[0]
    max_pages = page_table.shape[1]
    slots = max_pages // n_dp
    key_value_head = current_head // (head_number // KEY_VALUE_HEADS)
    owner_of = jnp.where(page_table >= 0, page_table // pool_rows, -1)
    mine = (owner_of == me_dp).astype(jnp.int32)
    rank = jnp.cumsum(mine, 1) - 1
    slot_ids = jnp.arange(slots, dtype=jnp.int32)
    select = (mine[:, None, :] == 1) & (rank[:, None, :] == slot_ids[None, :, None])
    local_page = jnp.sum(jnp.where(select, (page_table % pool_rows)[:, None, :], 0), -1)
    present = jnp.any(select, -1).reshape(-1)
    part = current_head % 2
    outgoing = kv_pool[local_page.reshape(-1), key_value_head, part]
    outgoing, tokens = lax.optimization_barrier((outgoing, tokens))
    received = lax.all_to_all(outgoing, "dp", split_axis=0, concat_axis=0, tiled=True)
    within = jnp.arange(page_len, dtype=jnp.int32)
    owners_mine = lax.dynamic_slice_in_dim(owner_of, me_dp * REQ_DEV, REQ_DEV, 0)
    hits = (owners_mine[None, :, :] == jnp.arange(n_dp, dtype=jnp.int32)[:, None, None]).astype(
        jnp.int32
    )
    hit_rank = jnp.cumsum(hits, -1) - 1
    chosen = (hits[:, :, None, :] == 1) & (hit_rank[:, :, None, :] == slot_ids[None, None, :, None])
    logical = jnp.sum(
        jnp.where(chosen, jnp.arange(max_pages, dtype=jnp.int32)[None, None, None, :], 0), -1
    )
    has_page = jnp.any(chosen, -1)
    key_pos = logical[..., None] * page_len + within[None, None, None, :]
    wide = tokens.astype(jnp.float32)
    meansq = jnp.mean(wide * wide, -1, keepdims=True)
    normalized_input = (wide * lax.rsqrt(meansq + 1e-05) * norm_gain.astype(jnp.float32)).astype(
        jnp.bfloat16
    )
    rows_in = [normalized_input]
    row_masks = [0]
    stride = head_number // 2
    while stride >= 1:
        rows_in = rows_in + [exchange(p, "head", stride) for p in rows_in]
        row_masks = row_masks + [m ^ stride for m in row_masks]
        stride //= 2
    piece = jnp.concatenate(rows_in, 0)
    within_rows = jnp.arange(local_rows, dtype=jnp.int32)
    true_row = jnp.concatenate([(current_head ^ m) * local_rows + within_rows for m in row_masks])
    held_w = [w_out]
    masks = [0]
    stride = head_number // 2
    while stride > 1:
        held_w = held_w + [exchange(p, "head", stride) for p in held_w]
        masks = masks + [m ^ stride for m in masks]
        stride //= 2
    q_part = jnp.dot(piece, w_query, preferred_element_type=jnp.float32)
    kv_part = jnp.dot(piece, key_value_weight, preferred_element_type=jnp.float32)
    projected = jnp.concatenate([q_part, kv_part], 1)
    q_width = group_heads * head_dim
    my_lengths = lax.dynamic_slice_in_dim(cache_lengths, me_dp * REQ_DEV, REQ_DEV, 0)
    positions = my_lengths[true_row // NEWTOK] + true_row % NEWTOK
    queries = rotate(
        projected[:, :q_width].reshape(block_rows, group_heads, head_dim), positions
    ).astype(jnp.bfloat16)
    own_part = projected[:, q_width:]
    holds_keys = current_head % 2 == 0
    turned = rotate(own_part[:, None, :], positions)[:, 0]
    own_ready = jnp.where(holds_keys, turned, own_part).astype(jnp.bfloat16)
    received, own_ready = lax.optimization_barrier((received, own_ready))
    partner_ready = from_partner(own_ready, "head", 0)
    partner_blocks = [row_masks.index(m ^ 1) for m in row_masks]
    partner_ready = jnp.concatenate(
        [partner_ready[j * local_rows:(j + 1) * local_rows] for j in partner_blocks], 0
    )
    new_keys = jnp.where(holds_keys, own_ready, partner_ready)
    new_values = jnp.where(holds_keys, partner_ready, own_ready)
    mask_rows = lax.dynamic_slice_in_dim(token_mask, me_dp * block_rows, block_rows, 0)
    cache_ok = (has_page[:, 0, :, None] & (key_pos[:, 0] < my_lengths[0])).reshape(-1)
    key_ok = jnp.concatenate([cache_ok, jnp.take(mask_rows, true_row) == 1])
    bias = jnp.where(key_ok, 0.0, -jnp.inf).astype(jnp.float32)
    queries = queries[0:NEWTOK].reshape(NEWTOK, group_heads * head_dim)
    other_half = exchange(received, "head", 1)
    pieces = attend(
        queries,
        received.reshape(-1, head_dim),
        other_half.reshape(-1, head_dim),
        new_keys,
        new_values,
        part,
        bias.reshape(1, -1),
        true_row,
        head_number,
    )
    late_w, pieces = lax.optimization_barrier((held_w[1:], pieces))
    held_w = held_w[:1] + list(late_w)
    held_w = held_w + [exchange(piece, "head", 1) for piece in held_w]
    masks = masks + [m ^ 1 for m in masks]
    out = None
    for m, w_rows in zip(masks, held_w):
        block = pieces[row_masks.index(m)]
        block = block if m == 0 else exchange(block, "head", m)
        term = jnp.dot(block, w_rows, preferred_element_type=jnp.float32)
        out = term if out is None else out + term
    return out.astype(jnp.bfloat16)


def solution(mesh):
    in_specs = (
        P(("dp", "head"), None),
        P(),
        P(None, "head"),
        P(None, "head"),
        P("head", None),
        P("dp", None, None, None, None),
        P(),
        P(),
        P(),
    )
    out_specs = P(("dp", "head"), None)
    return jax.shard_map(body, mesh=mesh, in_specs=in_specs, out_specs=out_specs, check_vma=False)
```

```python
import math

import jax
import jax.numpy as jnp
from jax import lax
from jax.sharding import PartitionSpec as P
from jax.experimental import pallas as pl
from jax.experimental.pallas import tpu as pltpu

KEY_VALUE_HEADS = 2
HEAD_SIZE = 128
NEWTOK = 512
REQ_DEV = 1


rope_base = 100000000000.0


def from_partner(value, axis, stride):
    mask = 2**stride
    pairs = [(source, source ^ mask) for source in range(lax.axis_size(axis))]
    return lax.ppermute(value, axis, pairs)


def attend_kernel(
    n_cache, tk, scale, part_ref, q_ref, mine_hbm, other_hbm, nk_hbm, nv_hbm, bias_ref,
    *rest,
):
    *o_refs, k_scr, v_scr, s_scr, sems = rest
    bq, head_dim = q_ref.shape
    total = k_scr.shape[0]
    groups = tk // 128

    @pl.when(pl.program_id(0) == 0)
    def _():
        def load(src_k, src_v):
            copies = [
                pltpu.make_async_copy(src_k, k_scr.at[pl.ds(0, n_cache)], sems.at[0]),
                pltpu.make_async_copy(src_v, v_scr.at[pl.ds(0, n_cache)], sems.at[1]),
                pltpu.make_async_copy(nk_hbm, k_scr.at[pl.ds(n_cache, total - n_cache)], sems.at[2]),
                pltpu.make_async_copy(nv_hbm, v_scr.at[pl.ds(n_cache, total - n_cache)], sems.at[3]),
            ]
            for copy in copies:
                copy.start()
            for copy in copies:
                copy.wait()

        @pl.when(part_ref[0] == 0)
        def _():
            load(mine_hbm, other_hbm)

        @pl.when(part_ref[0] != 0)
        def _():
            load(other_hbm, mine_hbm)

    q = q_ref[...]
    part_rows = bq // len(o_refs)

    def true_index(offset, axis):
        place = offset + lax.broadcasted_iota(jnp.int32, (bq, tk), axis)
        block = place // part_rows
        base = jnp.zeros_like(place)
        for k in range(len(o_refs)):
            base = jnp.where(block == k, part_ref[1 + k], base)
        return base + place % part_rows

    def scores(c, top, causal):
        start = pl.multiple_of(c * tk, tk)
        keys = k_scr[pl.ds(start, tk), :]
        s = lax.dot_general(q, keys, (((1,), (1,)), ((), ())), preferred_element_type=jnp.float32)
        s = s * scale + bias_ref[:, pl.ds(start, tk)]
        if causal:
            s = jnp.where(true_index(start - n_cache, 1) <= true_index(0, 0), s, -jnp.inf)
        s_scr[:, pl.ds(start, tk)] = s
        for g in range(groups):
            top = jnp.maximum(top, s[:, g * 128:(g + 1) * 128])
        return top

    top = jnp.full((bq, 128), -jnp.inf, jnp.float32)
    top = lax.fori_loop(0, n_cache // tk, lambda c, t: scores(c, t, False), top, unroll=8)
    top = lax.fori_loop(n_cache // tk, total // tk, lambda c, t: scores(c, t, True), top)
    top = jnp.max(top, -1, keepdims=True)

    def expo(c, part):
        start = pl.multiple_of(c * tk, tk)
        e = jnp.exp(s_scr[:, pl.ds(start, tk)] - top)
        s_scr[:, pl.ds(start, tk)] = e
        for g in range(groups):
            part = part + e[:, g * 128:(g + 1) * 128]
        return part

    part = lax.fori_loop(0, total // tk, expo, jnp.zeros((bq, 128), jnp.float32), unroll=8)
    inverse = 1.0 / jnp.sum(part, -1, keepdims=True)

    def weigh(c, acc):
        start = pl.multiple_of(c * tk, tk)
        w = (s_scr[:, pl.ds(start, tk)] * inverse).astype(jnp.bfloat16)
        return acc + jnp.dot(w, v_scr[pl.ds(start, tk), :], preferred_element_type=jnp.float32)

    acc = lax.fori_loop(0, total // tk, weigh, jnp.zeros((bq, head_dim), jnp.float32), unroll=8)
    for k, o_ref in enumerate(o_refs):
        o_ref[...] = acc[k * part_rows:(k + 1) * part_rows].astype(o_ref.dtype)


def attend(queries, mine, other, new_keys, new_values, part, bias, block_base):
    rows, width = queries.shape
    splits = block_base.shape[0]
    n_cache, head_dim = mine.shape
    total = n_cache + new_keys.shape[0]
    heads = width // head_dim
    tk = next(t for t in (512, 256, 128) if total % t == 0 and n_cache % t == 0)
    scale = 1.0 / math.sqrt(head_dim)
    cost = pl.CostEstimate(
        flops=4 * rows * total * head_dim * heads,
        transcendentals=rows * total * heads,
        bytes_accessed=2 * (2 * total * head_dim + 2 * rows * width) + 4 * total,
    )
    any_spec = pl.BlockSpec(memory_space=pl.ANY)
    grid_spec = pltpu.PrefetchScalarGridSpec(
        num_scalar_prefetch=1,
        grid=(heads,),
        in_specs=[
            pl.BlockSpec((rows, head_dim), lambda h, p: (0, h)),
            any_spec,
            any_spec,
            any_spec,
            any_spec,
            pl.BlockSpec((1, total), lambda h, p: (0, 0)),
        ],
        out_specs=[pl.BlockSpec((rows // splits, head_dim), lambda h, p: (0, h))] * splits,
        scratch_shapes=[
            pltpu.VMEM((total, head_dim), jnp.bfloat16),
            pltpu.VMEM((total, head_dim), jnp.bfloat16),
            pltpu.VMEM((rows, total), jnp.float32),
            pltpu.SemaphoreType.DMA((4,)),
        ],
    )
    return pl.pallas_call(
        lambda *refs: attend_kernel(n_cache, tk, scale, *refs),
        out_shape=[jax.ShapeDtypeStruct((rows // splits, width), jnp.bfloat16)] * splits,
        grid_spec=grid_spec,
        compiler_params=pltpu.CompilerParams(dimension_semantics=("arbitrary",)),
        cost_estimate=cost,
        name="paged_prefill_attention",
    )(
        jnp.concatenate([part.reshape(1), block_base]).astype(jnp.int32),
        queries, mine, other, new_keys, new_values, bias,
    )


def exchange(value, axis, mask):
    pairs = [(source, source ^ mask) for source in range(lax.axis_size(axis))]
    return lax.ppermute(value, axis, pairs)


def rotate(values, positions):
    half_dim = values.shape[-1] // 2
    freqs = jnp.exp(
        jnp.arange(half_dim, dtype=jnp.float32) * (-2.0 * math.log(rope_base) / values.shape[-1])
    )
    angles = positions.astype(jnp.float32)[:, None] * freqs[None, :]
    cosine = jnp.cos(angles)[:, None, :]
    sine = jnp.sin(angles)[:, None, :]
    first = values[..., :half_dim]
    second = values[..., half_dim:]
    return jnp.concatenate([first * cosine - second * sine, second * cosine + first * sine], -1)


def body(
    tokens,
    norm_gain,
    w_query,
    key_value_weight,
    w_out,
    kv_pool,
    cache_lengths,
    page_table,
    token_mask,
):
    n_dp = lax.axis_size("dp")
    head_number = lax.axis_size("head")
    me_dp = lax.axis_index("dp")
    current_head = lax.axis_index("head")
    local_rows = tokens.shape[0]
    block_rows = local_rows * head_number
    head_dim = HEAD_SIZE
    group_heads = w_query.shape[1] // head_dim
    page_len = kv_pool.shape[3]
    pool_rows = kv_pool.shape[0]
    max_pages = page_table.shape[1]
    slots = max_pages // n_dp
    key_value_head = current_head // (head_number // KEY_VALUE_HEADS)
    owner_of = jnp.where(page_table >= 0, page_table // pool_rows, -1)
    mine = (owner_of == me_dp).astype(jnp.int32)
    rank = jnp.cumsum(mine, 1) - 1
    slot_ids = jnp.arange(slots, dtype=jnp.int32)
    select = (mine[:, None, :] == 1) & (rank[:, None, :] == slot_ids[None, :, None])
    local_page = jnp.sum(jnp.where(select, (page_table % pool_rows)[:, None, :], 0), -1)
    present = jnp.any(select, -1).reshape(-1)
    part = current_head % 2
    outgoing = kv_pool[local_page.reshape(-1), key_value_head, part]
    outgoing, tokens = lax.optimization_barrier((outgoing, tokens))
    received = lax.all_to_all(outgoing, "dp", split_axis=0, concat_axis=0, tiled=True)
    within = jnp.arange(page_len, dtype=jnp.int32)
    owners_mine = lax.dynamic_slice_in_dim(owner_of, me_dp * REQ_DEV, REQ_DEV, 0)
    hits = (owners_mine[None, :, :] == jnp.arange(n_dp, dtype=jnp.int32)[:, None, None]).astype(
        jnp.int32
    )
    hit_rank = jnp.cumsum(hits, -1) - 1
    chosen = (hits[:, :, None, :] == 1) & (hit_rank[:, :, None, :] == slot_ids[None, None, :, None])
    logical = jnp.sum(
        jnp.where(chosen, jnp.arange(max_pages, dtype=jnp.int32)[None, None, None, :], 0), -1
    )
    has_page = jnp.any(chosen, -1)
    key_pos = logical[..., None] * page_len + within[None, None, None, :]
    wide = tokens.astype(jnp.float32)
    meansq = jnp.mean(wide * wide, -1, keepdims=True)
    normalized_input = (wide * lax.rsqrt(meansq + 1e-05) * norm_gain.astype(jnp.float32)).astype(
        jnp.bfloat16
    )
    rows_in = [normalized_input]
    row_masks = [0]
    stride = head_number // 2
    while stride >= 1:
        rows_in = rows_in + [exchange(p, "head", stride) for p in rows_in]
        row_masks = row_masks + [m ^ stride for m in row_masks]
        stride //= 2
    piece = jnp.concatenate(rows_in, 0)
    within_rows = jnp.arange(local_rows, dtype=jnp.int32)
    true_row = jnp.concatenate([(current_head ^ m) * local_rows + within_rows for m in row_masks])
    held_w = [w_out]
    masks = [0]
    stride = head_number // 2
    while stride > 1:
        held_w = held_w + [exchange(p, "head", stride) for p in held_w]
        masks = masks + [m ^ stride for m in masks]
        stride //= 2
    q_part = jnp.dot(piece, w_query, preferred_element_type=jnp.float32)
    kv_part = jnp.dot(piece, key_value_weight, preferred_element_type=jnp.float32)
    projected = jnp.concatenate([q_part, kv_part], 1)
    q_width = group_heads * head_dim
    my_lengths = lax.dynamic_slice_in_dim(cache_lengths, me_dp * REQ_DEV, REQ_DEV, 0)
    positions = my_lengths[true_row // NEWTOK] + true_row % NEWTOK
    queries = rotate(
        projected[:, :q_width].reshape(block_rows, group_heads, head_dim), positions
    ).astype(jnp.bfloat16)
    own_part = projected[:, q_width:]
    holds_keys = current_head % 2 == 0
    turned = rotate(own_part[:, None, :], positions)[:, 0]
    own_ready = jnp.where(holds_keys, turned, own_part).astype(jnp.bfloat16)
    received, own_ready = lax.optimization_barrier((received, own_ready))
    partner_ready = from_partner(own_ready, "head", 0)
    partner_blocks = [row_masks.index(m ^ 1) for m in row_masks]
    partner_ready = jnp.concatenate(
        [partner_ready[j * local_rows:(j + 1) * local_rows] for j in partner_blocks], 0
    )
    new_keys = jnp.where(holds_keys, own_ready, partner_ready)
    new_values = jnp.where(holds_keys, partner_ready, own_ready)
    mask_rows = lax.dynamic_slice_in_dim(token_mask, me_dp * block_rows, block_rows, 0)
    cache_ok = (has_page[:, 0, :, None] & (key_pos[:, 0] < my_lengths[0])).reshape(-1)
    key_ok = jnp.concatenate([cache_ok, jnp.take(mask_rows, true_row) == 1])
    bias = jnp.where(key_ok, 0.0, -jnp.inf).astype(jnp.float32)
    queries = queries[0:NEWTOK].reshape(NEWTOK, group_heads * head_dim)
    other_half = exchange(received, "head", 1)
    pieces = attend(
        queries,
        received.reshape(-1, head_dim),
        other_half.reshape(-1, head_dim),
        new_keys,
        new_values,
        part,
        bias.reshape(1, -1),
        jnp.stack([(current_head ^ m) * local_rows for m in row_masks]),
    )
    late_w, pieces = lax.optimization_barrier((held_w[1:], pieces))
    held_w = held_w[:1] + list(late_w)
    held_w = held_w + [exchange(piece, "head", 1) for piece in held_w]
    masks = masks + [m ^ 1 for m in masks]
    held_w = jnp.concatenate(held_w, 0)
    columns = []
    for m in masks:
        block = pieces[row_masks.index(m)]
        columns.append(block if m == 0 else exchange(block, "head", m))
    ordered = jnp.concatenate(columns, 1)
    out = jnp.dot(ordered, held_w, preferred_element_type=jnp.float32)
    return out.astype(jnp.bfloat16)


def solution(mesh):
    in_specs = (
        P(("dp", "head"), None),
        P(),
        P(None, "head"),
        P(None, "head"),
        P("head", None),
        P("dp", None, None, None, None),
        P(),
        P(),
        P(),
    )
    out_specs = P(("dp", "head"), None)
    return jax.shard_map(body, mesh=mesh, in_specs=in_specs, out_specs=out_specs, check_vma=False)
```

```python
import math

import jax
import jax.numpy as jnp
from jax import lax
from jax.sharding import PartitionSpec as P
from jax.experimental import pallas as pl
from jax.experimental.pallas import tpu as pltpu

KEY_VALUE_HEADS = 2
HEAD_SIZE = 128
NEWTOK = 512
REQ_DEV = 1


rope_base = 100000000000.0


def from_partner(value, axis, stride):
    mask = 2**stride
    pairs = [(source, source ^ mask) for source in range(lax.axis_size(axis))]
    return lax.ppermute(value, axis, pairs)


def attend_kernel(
    n_cache, tk, scale, part_ref, q_ref, mine_hbm, other_hbm, nk_hbm, nv_hbm, bias_ref,
    *rest,
):
    *o_refs, k_scr, v_scr, s_scr, sems = rest
    bq, head_dim = q_ref.shape
    total = k_scr.shape[0]
    groups = tk // 128

    first = pl.program_id(0) == 0

    def loads(src_k, src_v, which=(0, 1, 2, 3)):
        plan = [
            (src_k, k_scr.at[pl.ds(0, n_cache)]),
            (nk_hbm, k_scr.at[pl.ds(n_cache, total - n_cache)]),
            (src_v, v_scr.at[pl.ds(0, n_cache)]),
            (nv_hbm, v_scr.at[pl.ds(n_cache, total - n_cache)]),
        ]
        return [pltpu.make_async_copy(*plan[i], sems.at[i]) for i in which]

    @pl.when(first & (part_ref[0] == 0))
    def _():
        for copy in loads(mine_hbm, other_hbm):
            copy.start()

    @pl.when(first & (part_ref[0] != 0))
    def _():
        for copy in loads(other_hbm, mine_hbm):
            copy.start()

    @pl.when(first)
    def _():
        for copy in loads(mine_hbm, other_hbm, (0, 1)):
            copy.wait()

    q = q_ref[...]
    part_rows = bq // len(o_refs)

    def true_index(offset, axis):
        place = offset + lax.broadcasted_iota(jnp.int32, (bq, tk), axis)
        block = place // part_rows
        base = jnp.zeros_like(place)
        for k in range(len(o_refs)):
            base = jnp.where(block == k, part_ref[1 + k], base)
        return base + place % part_rows

    def scores(c, top, causal):
        start = pl.multiple_of(c * tk, tk)
        keys = k_scr[pl.ds(start, tk), :]
        s = lax.dot_general(q, keys, (((1,), (1,)), ((), ())), preferred_element_type=jnp.float32)
        s = s * scale + bias_ref[:, pl.ds(start, tk)]
        if causal:
            s = jnp.where(true_index(start - n_cache, 1) <= true_index(0, 0), s, -jnp.inf)
        s_scr[:, pl.ds(start, tk)] = s
        for g in range(groups):
            top = jnp.maximum(top, s[:, g * 128:(g + 1) * 128])
        return top

    top = jnp.full((bq, 128), -jnp.inf, jnp.float32)
    top = lax.fori_loop(0, n_cache // tk, lambda c, t: scores(c, t, False), top, unroll=8)
    top = lax.fori_loop(n_cache // tk, total // tk, lambda c, t: scores(c, t, True), top)
    top = jnp.max(top, -1, keepdims=True)

    def expo(c, part):
        start = pl.multiple_of(c * tk, tk)
        e = jnp.exp(s_scr[:, pl.ds(start, tk)] - top)
        s_scr[:, pl.ds(start, tk)] = e
        for g in range(groups):
            part = part + e[:, g * 128:(g + 1) * 128]
        return part

    part = lax.fori_loop(0, total // tk, expo, jnp.zeros((bq, 128), jnp.float32), unroll=8)
    inverse = 1.0 / jnp.sum(part, -1, keepdims=True)

    def weigh(c, acc):
        start = pl.multiple_of(c * tk, tk)
        w = (s_scr[:, pl.ds(start, tk)] * inverse).astype(jnp.bfloat16)
        return acc + jnp.dot(w, v_scr[pl.ds(start, tk), :], preferred_element_type=jnp.float32)

    @pl.when(first)
    def _():
        for copy in loads(mine_hbm, other_hbm, (2, 3)):
            copy.wait()

    acc = lax.fori_loop(0, total // tk, weigh, jnp.zeros((bq, head_dim), jnp.float32), unroll=8)
    for k, o_ref in enumerate(o_refs):
        o_ref[...] = acc[k * part_rows:(k + 1) * part_rows].astype(o_ref.dtype)


def attend(queries, mine, other, new_keys, new_values, part, bias, block_base):
    rows, width = queries.shape
    splits = block_base.shape[0]
    n_cache, head_dim = mine.shape
    total = n_cache + new_keys.shape[0]
    heads = width // head_dim
    tk = next(t for t in (512, 256, 128) if total % t == 0 and n_cache % t == 0)
    scale = 1.0 / math.sqrt(head_dim)
    cost = pl.CostEstimate(
        flops=4 * rows * total * head_dim * heads,
        transcendentals=rows * total * heads,
        bytes_accessed=2 * (2 * total * head_dim + 2 * rows * width) + 4 * total,
    )
    any_spec = pl.BlockSpec(memory_space=pl.ANY)
    grid_spec = pltpu.PrefetchScalarGridSpec(
        num_scalar_prefetch=1,
        grid=(heads,),
        in_specs=[
            pl.BlockSpec((rows, head_dim), lambda h, p: (0, h)),
            any_spec,
            any_spec,
            any_spec,
            any_spec,
            pl.BlockSpec((1, total), lambda h, p: (0, 0)),
        ],
        out_specs=[pl.BlockSpec((rows // splits, head_dim), lambda h, p: (0, h))] * splits,
        scratch_shapes=[
            pltpu.VMEM((total, head_dim), jnp.bfloat16),
            pltpu.VMEM((total, head_dim), jnp.bfloat16),
            pltpu.VMEM((rows, total), jnp.float32),
            pltpu.SemaphoreType.DMA((4,)),
        ],
    )
    return pl.pallas_call(
        lambda *refs: attend_kernel(n_cache, tk, scale, *refs),
        out_shape=[jax.ShapeDtypeStruct((rows // splits, width), jnp.bfloat16)] * splits,
        grid_spec=grid_spec,
        compiler_params=pltpu.CompilerParams(dimension_semantics=("arbitrary",)),
        cost_estimate=cost,
        name="paged_prefill_attention",
    )(
        jnp.concatenate([part.reshape(1), block_base]).astype(jnp.int32),
        queries, mine, other, new_keys, new_values, bias,
    )


def exchange(value, axis, mask):
    pairs = [(source, source ^ mask) for source in range(lax.axis_size(axis))]
    return lax.ppermute(value, axis, pairs)


def rotate(values, positions):
    half_dim = values.shape[-1] // 2
    freqs = jnp.exp(
        jnp.arange(half_dim, dtype=jnp.float32) * (-2.0 * math.log(rope_base) / values.shape[-1])
    )
    angles = positions.astype(jnp.float32)[:, None] * freqs[None, :]
    cosine = jnp.cos(angles)[:, None, :]
    sine = jnp.sin(angles)[:, None, :]
    first = values[..., :half_dim]
    second = values[..., half_dim:]
    return jnp.concatenate([first * cosine - second * sine, second * cosine + first * sine], -1)


def body(
    tokens,
    norm_gain,
    w_query,
    key_value_weight,
    w_out,
    kv_pool,
    cache_lengths,
    page_table,
    token_mask,
):
    n_dp = lax.axis_size("dp")
    head_number = lax.axis_size("head")
    me_dp = lax.axis_index("dp")
    current_head = lax.axis_index("head")
    local_rows = tokens.shape[0]
    block_rows = local_rows * head_number
    head_dim = HEAD_SIZE
    group_heads = w_query.shape[1] // head_dim
    page_len = kv_pool.shape[3]
    pool_rows = kv_pool.shape[0]
    max_pages = page_table.shape[1]
    slots = max_pages // n_dp
    key_value_head = current_head // (head_number // KEY_VALUE_HEADS)
    owner_of = jnp.where(page_table >= 0, page_table // pool_rows, -1)
    mine = (owner_of == me_dp).astype(jnp.int32)
    rank = jnp.cumsum(mine, 1) - 1
    slot_ids = jnp.arange(slots, dtype=jnp.int32)
    select = (mine[:, None, :] == 1) & (rank[:, None, :] == slot_ids[None, :, None])
    local_page = jnp.sum(jnp.where(select, (page_table % pool_rows)[:, None, :], 0), -1)
    present = jnp.any(select, -1).reshape(-1)
    part = current_head % 2
    outgoing = kv_pool[local_page.reshape(-1), key_value_head, part]
    outgoing, tokens = lax.optimization_barrier((outgoing, tokens))
    received = lax.all_to_all(outgoing, "dp", split_axis=0, concat_axis=0, tiled=True)
    within = jnp.arange(page_len, dtype=jnp.int32)
    owners_mine = lax.dynamic_slice_in_dim(owner_of, me_dp * REQ_DEV, REQ_DEV, 0)
    hits = (owners_mine[None, :, :] == jnp.arange(n_dp, dtype=jnp.int32)[:, None, None]).astype(
        jnp.int32
    )
    hit_rank = jnp.cumsum(hits, -1) - 1
    chosen = (hits[:, :, None, :] == 1) & (hit_rank[:, :, None, :] == slot_ids[None, None, :, None])
    logical = jnp.sum(
        jnp.where(chosen, jnp.arange(max_pages, dtype=jnp.int32)[None, None, None, :], 0), -1
    )
    has_page = jnp.any(chosen, -1)
    key_pos = logical[..., None] * page_len + within[None, None, None, :]
    wide = tokens.astype(jnp.float32)
    meansq = jnp.mean(wide * wide, -1, keepdims=True)
    normalized_input = (wide * lax.rsqrt(meansq + 1e-05) * norm_gain.astype(jnp.float32)).astype(
        jnp.bfloat16
    )
    rows_in = [normalized_input]
    row_masks = [0]
    stride = head_number // 2
    while stride >= 1:
        rows_in = rows_in + [exchange(p, "head", stride) for p in rows_in]
        row_masks = row_masks + [m ^ stride for m in row_masks]
        stride //= 2
    piece = jnp.concatenate(rows_in, 0)
    within_rows = jnp.arange(local_rows, dtype=jnp.int32)
    true_row = jnp.concatenate([(current_head ^ m) * local_rows + within_rows for m in row_masks])
    held_w = [w_out]
    masks = [0]
    stride = head_number // 2
    while stride > 1:
        held_w = held_w + [exchange(p, "head", stride) for p in held_w]
        masks = masks + [m ^ stride for m in masks]
        stride //= 2
    q_part = jnp.dot(piece, w_query, preferred_element_type=jnp.float32)
    kv_part = jnp.dot(piece, key_value_weight, preferred_element_type=jnp.float32)
    projected = jnp.concatenate([q_part, kv_part], 1)
    q_width = group_heads * head_dim
    my_lengths = lax.dynamic_slice_in_dim(cache_lengths, me_dp * REQ_DEV, REQ_DEV, 0)
    positions = my_lengths[true_row // NEWTOK] + true_row % NEWTOK
    queries = rotate(
        projected[:, :q_width].reshape(block_rows, group_heads, head_dim), positions
    ).astype(jnp.bfloat16)
    own_part = projected[:, q_width:]
    holds_keys = current_head % 2 == 0
    turned = rotate(own_part[:, None, :], positions)[:, 0]
    own_ready = jnp.where(holds_keys, turned, own_part).astype(jnp.bfloat16)
    queries = queries[0:NEWTOK].reshape(NEWTOK, group_heads * head_dim)
    received, own_ready, queries = lax.optimization_barrier((received, own_ready, queries))
    partner_ready = from_partner(own_ready, "head", 0)
    partner_blocks = [row_masks.index(m ^ 1) for m in row_masks]
    partner_ready = jnp.concatenate(
        [partner_ready[j * local_rows:(j + 1) * local_rows] for j in partner_blocks], 0
    )
    new_keys = jnp.where(holds_keys, own_ready, partner_ready)
    new_values = jnp.where(holds_keys, partner_ready, own_ready)
    mask_rows = lax.dynamic_slice_in_dim(token_mask, me_dp * block_rows, block_rows, 0)
    cache_ok = (has_page[:, 0, :, None] & (key_pos[:, 0] < my_lengths[0])).reshape(-1)
    key_ok = jnp.concatenate([cache_ok, jnp.take(mask_rows, true_row) == 1])
    bias = jnp.where(key_ok, 0.0, -jnp.inf).astype(jnp.float32)
    other_half = exchange(received, "head", 1)
    pieces = attend(
        queries,
        received.reshape(-1, head_dim),
        other_half.reshape(-1, head_dim),
        new_keys,
        new_values,
        part,
        bias.reshape(1, -1),
        jnp.stack([(current_head ^ m) * local_rows for m in row_masks]),
    )
    late_w, pieces = lax.optimization_barrier((held_w[1:], pieces))
    held_w = held_w[:1] + list(late_w)
    held_w = held_w + [exchange(piece, "head", 1) for piece in held_w]
    masks = masks + [m ^ 1 for m in masks]
    held_w = jnp.concatenate(held_w, 0)
    columns = []
    for m in masks:
        block = pieces[row_masks.index(m)]
        columns.append(block if m == 0 else exchange(block, "head", m))
    ordered = jnp.concatenate(columns, 1)
    out = jnp.dot(ordered, held_w, preferred_element_type=jnp.float32)
    return out.astype(jnp.bfloat16)


def solution(mesh):
    in_specs = (
        P(("dp", "head"), None),
        P(),
        P(None, "head"),
        P(None, "head"),
        P("head", None),
        P("dp", None, None, None, None),
        P(),
        P(),
        P(),
    )
    out_specs = P(("dp", "head"), None)
    return jax.shard_map(body, mesh=mesh, in_specs=in_specs, out_specs=out_specs, check_vma=False)
```

```python
import math

import jax
import jax.numpy as jnp
from jax import lax
from jax.sharding import PartitionSpec as P
from jax.experimental import pallas as pl
from jax.experimental.pallas import tpu as pltpu

KEY_VALUE_HEADS = 2
HEAD_SIZE = 128
NEWTOK = 512
REQ_DEV = 1


rope_base = 100000000000.0


def from_partner(value, axis, stride):
    mask = 2**stride
    pairs = [(source, source ^ mask) for source in range(lax.axis_size(axis))]
    return lax.ppermute(value, axis, pairs)


def attend_kernel(
    n_cache, tk, scale, part_ref, q_ref, mine_hbm, other_hbm, nk_hbm, nv_hbm, bias_ref,
    *rest,
):
    *o_refs, k_scr, v_scr, s_scr, sems = rest
    bq, head_dim = q_ref.shape
    total = k_scr.shape[0]
    groups = tk // 128

    first = pl.program_id(0) == 0

    def loads(src_k, src_v, which=(0, 1, 2, 3)):
        plan = [
            (src_k, k_scr.at[pl.ds(0, n_cache)]),
            (nk_hbm, k_scr.at[pl.ds(n_cache, total - n_cache)]),
            (src_v, v_scr.at[pl.ds(0, n_cache)]),
            (nv_hbm, v_scr.at[pl.ds(n_cache, total - n_cache)]),
        ]
        return [pltpu.make_async_copy(*plan[i], sems.at[i]) for i in which]

    @pl.when(first & (part_ref[0] == 0))
    def _():
        for copy in loads(mine_hbm, other_hbm):
            copy.start()

    @pl.when(first & (part_ref[0] != 0))
    def _():
        for copy in loads(other_hbm, mine_hbm):
            copy.start()

    @pl.when(first)
    def _():
        for copy in loads(mine_hbm, other_hbm, (0, 1)):
            copy.wait()

    q = q_ref[...]
    part_rows = bq // len(o_refs)

    def true_index(offset, axis):
        place = offset + lax.broadcasted_iota(jnp.int32, (bq, tk), axis)
        block = place // part_rows
        base = jnp.zeros_like(place)
        for k in range(len(o_refs)):
            base = jnp.where(block == k, part_ref[1 + k], base)
        return base + place % part_rows

    def scores(c, top, causal):
        start = pl.multiple_of(c * tk, tk)
        keys = k_scr[pl.ds(start, tk), :]
        s = lax.dot_general(q, keys, (((1,), (1,)), ((), ())), preferred_element_type=jnp.float32)
        s = s * scale + bias_ref[:, pl.ds(start, tk)]
        if causal:
            s = jnp.where(true_index(start - n_cache, 1) <= true_index(0, 0), s, -jnp.inf)
        s_scr[:, pl.ds(start, tk)] = s
        for g in range(groups):
            top = jnp.maximum(top, s[:, g * 128:(g + 1) * 128])
        return top

    top = jnp.full((bq, 128), -jnp.inf, jnp.float32)
    top = lax.fori_loop(0, n_cache // tk, lambda c, t: scores(c, t, False), top, unroll=8)
    top = lax.fori_loop(n_cache // tk, total // tk, lambda c, t: scores(c, t, True), top)
    top = jnp.max(top, -1, keepdims=True)

    def expo(c, part):
        start = pl.multiple_of(c * tk, tk)
        e = jnp.exp(s_scr[:, pl.ds(start, tk)] - top)
        s_scr[:, pl.ds(start, tk)] = e
        for g in range(groups):
            part = part + e[:, g * 128:(g + 1) * 128]
        return part

    part = lax.fori_loop(0, total // tk, expo, jnp.zeros((bq, 128), jnp.float32), unroll=8)
    inverse = 1.0 / jnp.sum(part, -1, keepdims=True)

    def weigh(c, acc):
        start = pl.multiple_of(c * tk, tk)
        w = (s_scr[:, pl.ds(start, tk)] * inverse).astype(jnp.bfloat16)
        return acc + jnp.dot(w, v_scr[pl.ds(start, tk), :], preferred_element_type=jnp.float32)

    @pl.when(first)
    def _():
        for copy in loads(mine_hbm, other_hbm, (2, 3)):
            copy.wait()

    acc = lax.fori_loop(0, total // tk, weigh, jnp.zeros((bq, head_dim), jnp.float32), unroll=8)
    for k, o_ref in enumerate(o_refs):
        o_ref[...] = acc[k * part_rows:(k + 1) * part_rows].astype(o_ref.dtype)


def attend(queries, mine, other, new_keys, new_values, part, bias, block_base):
    rows, width = queries.shape
    splits = block_base.shape[0]
    n_cache, head_dim = mine.shape
    total = n_cache + new_keys.shape[0]
    heads = width // head_dim
    tk = next(t for t in (512, 256, 128) if total % t == 0 and n_cache % t == 0)
    scale = 1.0 / math.sqrt(head_dim)
    cost = pl.CostEstimate(
        flops=4 * rows * total * head_dim * heads,
        transcendentals=rows * total * heads,
        bytes_accessed=2 * (2 * total * head_dim + 2 * rows * width) + 4 * total,
    )
    any_spec = pl.BlockSpec(memory_space=pl.ANY)
    grid_spec = pltpu.PrefetchScalarGridSpec(
        num_scalar_prefetch=1,
        grid=(heads,),
        in_specs=[
            pl.BlockSpec((rows, head_dim), lambda h, p: (0, h)),
            any_spec,
            any_spec,
            any_spec,
            any_spec,
            pl.BlockSpec((1, total), lambda h, p: (0, 0)),
        ],
        out_specs=[pl.BlockSpec((rows // splits, head_dim), lambda h, p: (0, h))] * splits,
        scratch_shapes=[
            pltpu.VMEM((total, head_dim), jnp.bfloat16),
            pltpu.VMEM((total, head_dim), jnp.bfloat16),
            pltpu.VMEM((rows, total), jnp.float32),
            pltpu.SemaphoreType.DMA((4,)),
        ],
    )
    return pl.pallas_call(
        lambda *refs: attend_kernel(n_cache, tk, scale, *refs),
        out_shape=[jax.ShapeDtypeStruct((rows // splits, width), jnp.bfloat16)] * splits,
        grid_spec=grid_spec,
        compiler_params=pltpu.CompilerParams(dimension_semantics=("arbitrary",)),
        cost_estimate=cost,
        name="paged_prefill_attention",
    )(
        jnp.concatenate([part.reshape(1), block_base]).astype(jnp.int32),
        queries, mine, other, new_keys, new_values, bias,
    )


def exchange(value, axis, mask):
    pairs = [(source, source ^ mask) for source in range(lax.axis_size(axis))]
    return lax.ppermute(value, axis, pairs)


def rotate(values, positions):
    half_dim = values.shape[-1] // 2
    freqs = jnp.exp(
        jnp.arange(half_dim, dtype=jnp.float32) * (-2.0 * math.log(rope_base) / values.shape[-1])
    )
    angles = positions.astype(jnp.float32)[:, None] * freqs[None, :]
    cosine = jnp.cos(angles)[:, None, :]
    sine = jnp.sin(angles)[:, None, :]
    first = values[..., :half_dim]
    second = values[..., half_dim:]
    return jnp.concatenate([first * cosine - second * sine, second * cosine + first * sine], -1)


def body(
    tokens,
    norm_gain,
    w_query,
    key_value_weight,
    w_out,
    kv_pool,
    cache_lengths,
    page_table,
    token_mask,
):
    n_dp = lax.axis_size("dp")
    head_number = lax.axis_size("head")
    me_dp = lax.axis_index("dp")
    current_head = lax.axis_index("head")
    local_rows = tokens.shape[0]
    block_rows = local_rows * head_number
    head_dim = HEAD_SIZE
    group_heads = w_query.shape[1] // head_dim
    page_len = kv_pool.shape[3]
    pool_rows = kv_pool.shape[0]
    max_pages = page_table.shape[1]
    slots = max_pages // n_dp
    key_value_head = current_head // (head_number // KEY_VALUE_HEADS)
    owner_of = jnp.where(page_table >= 0, page_table // pool_rows, -1)
    mine = (owner_of == me_dp).astype(jnp.int32)
    rank = jnp.cumsum(mine, 1) - 1
    slot_ids = jnp.arange(slots, dtype=jnp.int32)
    select = (mine[:, None, :] == 1) & (rank[:, None, :] == slot_ids[None, :, None])
    local_page = jnp.sum(jnp.where(select, (page_table % pool_rows)[:, None, :], 0), -1)
    present = jnp.any(select, -1).reshape(-1)
    part = current_head % 2
    outgoing = kv_pool[local_page.reshape(-1), key_value_head, part]
    outgoing, tokens = lax.optimization_barrier((outgoing, tokens))
    received = lax.all_to_all(outgoing, "dp", split_axis=0, concat_axis=0, tiled=True)
    within = jnp.arange(page_len, dtype=jnp.int32)
    owners_mine = lax.dynamic_slice_in_dim(owner_of, me_dp * REQ_DEV, REQ_DEV, 0)
    hits = (owners_mine[None, :, :] == jnp.arange(n_dp, dtype=jnp.int32)[:, None, None]).astype(
        jnp.int32
    )
    hit_rank = jnp.cumsum(hits, -1) - 1
    chosen = (hits[:, :, None, :] == 1) & (hit_rank[:, :, None, :] == slot_ids[None, None, :, None])
    logical = jnp.sum(
        jnp.where(chosen, jnp.arange(max_pages, dtype=jnp.int32)[None, None, None, :], 0), -1
    )
    has_page = jnp.any(chosen, -1)
    key_pos = logical[..., None] * page_len + within[None, None, None, :]
    wide = tokens.astype(jnp.float32)
    meansq = jnp.mean(wide * wide, -1, keepdims=True)
    normalized_input = (wide * lax.rsqrt(meansq + 1e-05) * norm_gain.astype(jnp.float32)).astype(
        jnp.bfloat16
    )
    rows_in = [normalized_input]
    row_masks = [0]
    stride = head_number // 2
    while stride >= 1:
        rows_in = rows_in + [exchange(p, "head", stride) for p in rows_in]
        row_masks = row_masks + [m ^ stride for m in row_masks]
        stride //= 2
    piece = jnp.concatenate(rows_in, 0)
    within_rows = jnp.arange(local_rows, dtype=jnp.int32)
    true_row = jnp.concatenate([(current_head ^ m) * local_rows + within_rows for m in row_masks])
    held_w = [w_out]
    masks = [0]
    stride = head_number // 2
    while stride > 1:
        held_w = held_w + [exchange(p, "head", stride) for p in held_w]
        masks = masks + [m ^ stride for m in masks]
        stride //= 2
    q_part = jnp.dot(piece, w_query, preferred_element_type=jnp.float32)
    kv_part = jnp.dot(piece, key_value_weight, preferred_element_type=jnp.float32)
    projected = jnp.concatenate([q_part, kv_part], 1)
    q_width = group_heads * head_dim
    my_lengths = lax.dynamic_slice_in_dim(cache_lengths, me_dp * REQ_DEV, REQ_DEV, 0)
    positions = my_lengths[true_row // NEWTOK] + true_row % NEWTOK
    queries = rotate(
        projected[:, :q_width].reshape(block_rows, group_heads, head_dim), positions
    ).astype(jnp.bfloat16)
    own_part = projected[:, q_width:]
    holds_keys = current_head % 2 == 0
    turned = rotate(own_part[:, None, :], positions)[:, 0]
    own_ready = jnp.where(holds_keys, turned, own_part).astype(jnp.bfloat16)
    received, own_ready = lax.optimization_barrier((received, own_ready))
    partner_ready = from_partner(own_ready, "head", 0)
    partner_blocks = [row_masks.index(m ^ 1) for m in row_masks]
    partner_ready = jnp.concatenate(
        [partner_ready[j * local_rows:(j + 1) * local_rows] for j in partner_blocks], 0
    )
    new_keys = jnp.where(holds_keys, own_ready, partner_ready)
    new_values = jnp.where(holds_keys, partner_ready, own_ready)
    mask_rows = lax.dynamic_slice_in_dim(token_mask, me_dp * block_rows, block_rows, 0)
    cache_ok = (has_page[:, 0, :, None] & (key_pos[:, 0] < my_lengths[0])).reshape(-1)
    key_ok = jnp.concatenate([cache_ok, jnp.take(mask_rows, true_row) == 1])
    bias = jnp.where(key_ok, 0.0, -jnp.inf).astype(jnp.float32)
    queries = queries[0:NEWTOK].reshape(NEWTOK, group_heads * head_dim)
    other_half = exchange(received, "head", 1)
    pieces = attend(
        queries,
        received.reshape(-1, head_dim),
        other_half.reshape(-1, head_dim),
        new_keys,
        new_values,
        part,
        bias.reshape(1, -1),
        jnp.stack([(current_head ^ m) * local_rows for m in row_masks]),
    )
    late_w, pieces = lax.optimization_barrier((held_w[1:], pieces))
    held_w = held_w[:1] + list(late_w)
    held_w = held_w + [exchange(piece, "head", 1) for piece in held_w]
    masks = masks + [m ^ 1 for m in masks]
    held_w = jnp.concatenate(held_w, 0)
    columns = []
    for m in masks:
        block = pieces[row_masks.index(m)]
        columns.append(block if m == 0 else exchange(block, "head", m))
    ordered = jnp.concatenate(columns, 1)
    out = jnp.dot(ordered, held_w, preferred_element_type=jnp.float32)
    return out.astype(jnp.bfloat16)


def solution(mesh):
    in_specs = (
        P(("dp", "head"), None),
        P(),
        P(None, "head"),
        P(None, "head"),
        P("head", None),
        P("dp", None, None, None, None),
        P(),
        P(),
        P(),
    )
    out_specs = P(("dp", "head"), None)
    return jax.shard_map(body, mesh=mesh, in_specs=in_specs, out_specs=out_specs, check_vma=False)
```

```python
import math

import jax
import jax.numpy as jnp
from jax import lax
from jax.sharding import PartitionSpec as P
from jax.experimental import pallas as pl
from jax.experimental.pallas import tpu as pltpu

KEY_VALUE_HEADS = 2
HEAD_SIZE = 128
NEWTOK = 512
REQ_DEV = 1


rope_base = 100000000000.0


def from_partner(value, axis, stride):
    mask = 2**stride
    pairs = [(source, source ^ mask) for source in range(lax.axis_size(axis))]
    return lax.ppermute(value, axis, pairs)


def attend_kernel(
    n_cache, tk, scale, blocks, part_ref, q_ref, mine_hbm, other_hbm, own_hbm, partner_hbm,
    bias_ref, *rest,
):
    *o_refs, k_scr, v_scr, s_scr, sems = rest
    bq, head_dim = q_ref.shape
    total = k_scr.shape[0]
    groups = tk // 128

    @pl.when(pl.program_id(0) == 0)
    def _():
        def load(src_k, src_v, own_dst, partner_dst):
            span = (total - n_cache) // len(blocks)
            copies = [
                pltpu.make_async_copy(src_k, k_scr.at[pl.ds(0, n_cache)], sems.at[0]),
                pltpu.make_async_copy(src_v, v_scr.at[pl.ds(0, n_cache)], sems.at[1]),
                pltpu.make_async_copy(own_hbm, own_dst.at[pl.ds(n_cache, total - n_cache)], sems.at[2]),
            ] + [
                pltpu.make_async_copy(
                    partner_hbm.at[pl.ds(j * span, span)],
                    partner_dst.at[pl.ds(n_cache + k * span, span)],
                    sems.at[3 + k],
                )
                for k, j in enumerate(blocks)
            ]
            for copy in copies:
                copy.start()
            for copy in copies:
                copy.wait()

        @pl.when(part_ref[0] == 0)
        def _():
            load(mine_hbm, other_hbm, k_scr, v_scr)

        @pl.when(part_ref[0] != 0)
        def _():
            load(other_hbm, mine_hbm, v_scr, k_scr)

    q = q_ref[...]
    part_rows = bq // len(o_refs)

    def true_index(offset, axis):
        place = offset + lax.broadcasted_iota(jnp.int32, (bq, tk), axis)
        block = place // part_rows
        base = jnp.zeros_like(place)
        for k in range(len(o_refs)):
            base = jnp.where(block == k, part_ref[1 + k], base)
        return base + place % part_rows

    def scores(c, top, causal):
        start = pl.multiple_of(c * tk, tk)
        keys = k_scr[pl.ds(start, tk), :]
        s = lax.dot_general(q, keys, (((1,), (1,)), ((), ())), preferred_element_type=jnp.float32)
        s = s * scale + bias_ref[:, pl.ds(start, tk)]
        if causal:
            s = jnp.where(true_index(start - n_cache, 1) <= true_index(0, 0), s, -jnp.inf)
        s_scr[:, pl.ds(start, tk)] = s
        for g in range(groups):
            top = jnp.maximum(top, s[:, g * 128:(g + 1) * 128])
        return top

    top = jnp.full((bq, 128), -jnp.inf, jnp.float32)
    top = lax.fori_loop(0, n_cache // tk, lambda c, t: scores(c, t, False), top, unroll=8)
    top = lax.fori_loop(n_cache // tk, total // tk, lambda c, t: scores(c, t, True), top)
    top = jnp.max(top, -1, keepdims=True)

    def expo(c, part):
        start = pl.multiple_of(c * tk, tk)
        e = jnp.exp(s_scr[:, pl.ds(start, tk)] - top)
        s_scr[:, pl.ds(start, tk)] = e
        for g in range(groups):
            part = part + e[:, g * 128:(g + 1) * 128]
        return part

    part = lax.fori_loop(0, total // tk, expo, jnp.zeros((bq, 128), jnp.float32), unroll=8)
    inverse = 1.0 / jnp.sum(part, -1, keepdims=True)

    def weigh(c, acc):
        start = pl.multiple_of(c * tk, tk)
        w = (s_scr[:, pl.ds(start, tk)] * inverse).astype(jnp.bfloat16)
        return acc + jnp.dot(w, v_scr[pl.ds(start, tk), :], preferred_element_type=jnp.float32)

    acc = lax.fori_loop(0, total // tk, weigh, jnp.zeros((bq, head_dim), jnp.float32), unroll=8)
    for k, o_ref in enumerate(o_refs):
        o_ref[...] = acc[k * part_rows:(k + 1) * part_rows].astype(o_ref.dtype)


def attend(queries, mine, other, own_new, partner_new, blocks, part, bias, block_base):
    rows, width = queries.shape
    splits = block_base.shape[0]
    n_cache, head_dim = mine.shape
    total = n_cache + own_new.shape[0]
    heads = width // head_dim
    tk = next(t for t in (512, 256, 128) if total % t == 0 and n_cache % t == 0)
    scale = 1.0 / math.sqrt(head_dim)
    cost = pl.CostEstimate(
        flops=4 * rows * total * head_dim * heads,
        transcendentals=rows * total * heads,
        bytes_accessed=2 * (2 * total * head_dim + 2 * rows * width) + 4 * total,
    )
    any_spec = pl.BlockSpec(memory_space=pl.ANY)
    grid_spec = pltpu.PrefetchScalarGridSpec(
        num_scalar_prefetch=1,
        grid=(heads,),
        in_specs=[
            pl.BlockSpec((rows, head_dim), lambda h, p: (0, h)),
            any_spec,
            any_spec,
            any_spec,
            any_spec,
            pl.BlockSpec((1, total), lambda h, p: (0, 0)),
        ],
        out_specs=[pl.BlockSpec((rows // splits, head_dim), lambda h, p: (0, h))] * splits,
        scratch_shapes=[
            pltpu.VMEM((total, head_dim), jnp.bfloat16),
            pltpu.VMEM((total, head_dim), jnp.bfloat16),
            pltpu.VMEM((rows, total), jnp.float32),
            pltpu.SemaphoreType.DMA((3 + len(blocks),)),
        ],
    )
    return pl.pallas_call(
        lambda *refs: attend_kernel(n_cache, tk, scale, blocks, *refs),
        out_shape=[jax.ShapeDtypeStruct((rows // splits, width), jnp.bfloat16)] * splits,
        grid_spec=grid_spec,
        compiler_params=pltpu.CompilerParams(dimension_semantics=("arbitrary",)),
        cost_estimate=cost,
        name="paged_prefill_attention",
    )(
        jnp.concatenate([part.reshape(1), block_base]).astype(jnp.int32),
        queries, mine, other, own_new, partner_new, bias,
    )


def exchange(value, axis, mask):
    pairs = [(source, source ^ mask) for source in range(lax.axis_size(axis))]
    return lax.ppermute(value, axis, pairs)


def rotate(values, positions):
    half_dim = values.shape[-1] // 2
    freqs = jnp.exp(
        jnp.arange(half_dim, dtype=jnp.float32) * (-2.0 * math.log(rope_base) / values.shape[-1])
    )
    angles = positions.astype(jnp.float32)[:, None] * freqs[None, :]
    cosine = jnp.cos(angles)[:, None, :]
    sine = jnp.sin(angles)[:, None, :]
    first = values[..., :half_dim]
    second = values[..., half_dim:]
    return jnp.concatenate([first * cosine - second * sine, second * cosine + first * sine], -1)


def body(
    tokens,
    norm_gain,
    w_query,
    key_value_weight,
    w_out,
    kv_pool,
    cache_lengths,
    page_table,
    token_mask,
):
    n_dp = lax.axis_size("dp")
    head_number = lax.axis_size("head")
    me_dp = lax.axis_index("dp")
    current_head = lax.axis_index("head")
    local_rows = tokens.shape[0]
    block_rows = local_rows * head_number
    head_dim = HEAD_SIZE
    group_heads = w_query.shape[1] // head_dim
    page_len = kv_pool.shape[3]
    pool_rows = kv_pool.shape[0]
    max_pages = page_table.shape[1]
    slots = max_pages // n_dp
    key_value_head = current_head // (head_number // KEY_VALUE_HEADS)
    owner_of = jnp.where(page_table >= 0, page_table // pool_rows, -1)
    mine = (owner_of == me_dp).astype(jnp.int32)
    rank = jnp.cumsum(mine, 1) - 1
    slot_ids = jnp.arange(slots, dtype=jnp.int32)
    select = (mine[:, None, :] == 1) & (rank[:, None, :] == slot_ids[None, :, None])
    local_page = jnp.sum(jnp.where(select, (page_table % pool_rows)[:, None, :], 0), -1)
    present = jnp.any(select, -1).reshape(-1)
    part = current_head % 2
    outgoing = kv_pool[local_page.reshape(-1), key_value_head, part]
    outgoing, tokens = lax.optimization_barrier((outgoing, tokens))
    received = lax.all_to_all(outgoing, "dp", split_axis=0, concat_axis=0, tiled=True)
    within = jnp.arange(page_len, dtype=jnp.int32)
    owners_mine = lax.dynamic_slice_in_dim(owner_of, me_dp * REQ_DEV, REQ_DEV, 0)
    hits = (owners_mine[None, :, :] == jnp.arange(n_dp, dtype=jnp.int32)[:, None, None]).astype(
        jnp.int32
    )
    hit_rank = jnp.cumsum(hits, -1) - 1
    chosen = (hits[:, :, None, :] == 1) & (hit_rank[:, :, None, :] == slot_ids[None, None, :, None])
    logical = jnp.sum(
        jnp.where(chosen, jnp.arange(max_pages, dtype=jnp.int32)[None, None, None, :], 0), -1
    )
    has_page = jnp.any(chosen, -1)
    key_pos = logical[..., None] * page_len + within[None, None, None, :]
    wide = tokens.astype(jnp.float32)
    meansq = jnp.mean(wide * wide, -1, keepdims=True)
    normalized_input = (wide * lax.rsqrt(meansq + 1e-05) * norm_gain.astype(jnp.float32)).astype(
        jnp.bfloat16
    )
    rows_in = [normalized_input]
    row_masks = [0]
    stride = head_number // 2
    while stride >= 1:
        rows_in = rows_in + [exchange(p, "head", stride) for p in rows_in]
        row_masks = row_masks + [m ^ stride for m in row_masks]
        stride //= 2
    piece = jnp.concatenate(rows_in, 0)
    within_rows = jnp.arange(local_rows, dtype=jnp.int32)
    true_row = jnp.concatenate([(current_head ^ m) * local_rows + within_rows for m in row_masks])
    held_w = [w_out]
    masks = [0]
    stride = head_number // 2
    while stride > 1:
        held_w = held_w + [exchange(p, "head", stride) for p in held_w]
        masks = masks + [m ^ stride for m in masks]
        stride //= 2
    q_part = jnp.dot(piece, w_query, preferred_element_type=jnp.float32)
    kv_part = jnp.dot(piece, key_value_weight, preferred_element_type=jnp.float32)
    projected = jnp.concatenate([q_part, kv_part], 1)
    q_width = group_heads * head_dim
    my_lengths = lax.dynamic_slice_in_dim(cache_lengths, me_dp * REQ_DEV, REQ_DEV, 0)
    positions = my_lengths[true_row // NEWTOK] + true_row % NEWTOK
    queries = rotate(
        projected[:, :q_width].reshape(block_rows, group_heads, head_dim), positions
    ).astype(jnp.bfloat16)
    own_part = projected[:, q_width:]
    holds_keys = current_head % 2 == 0
    turned = rotate(own_part[:, None, :], positions)[:, 0]
    own_ready = jnp.where(holds_keys, turned, own_part).astype(jnp.bfloat16)
    received, own_ready = lax.optimization_barrier((received, own_ready))
    partner_ready = from_partner(own_ready, "head", 0)
    partner_blocks = [row_masks.index(m ^ 1) for m in row_masks]
    mask_rows = lax.dynamic_slice_in_dim(token_mask, me_dp * block_rows, block_rows, 0)
    cache_ok = (has_page[:, 0, :, None] & (key_pos[:, 0] < my_lengths[0])).reshape(-1)
    key_ok = jnp.concatenate([cache_ok, jnp.take(mask_rows, true_row) == 1])
    bias = jnp.where(key_ok, 0.0, -jnp.inf).astype(jnp.float32)
    queries = queries[0:NEWTOK].reshape(NEWTOK, group_heads * head_dim)
    other_half = exchange(received, "head", 1)
    pieces = attend(
        queries,
        received.reshape(-1, head_dim),
        other_half.reshape(-1, head_dim),
        own_ready,
        partner_ready,
        partner_blocks,
        part,
        bias.reshape(1, -1),
        jnp.stack([(current_head ^ m) * local_rows for m in row_masks]),
    )
    late_w, pieces = lax.optimization_barrier((held_w[1:], pieces))
    held_w = held_w[:1] + list(late_w)
    held_w = held_w + [exchange(piece, "head", 1) for piece in held_w]
    masks = masks + [m ^ 1 for m in masks]
    held_w = jnp.concatenate(held_w, 0)
    columns = []
    for m in masks:
        block = pieces[row_masks.index(m)]
        columns.append(block if m == 0 else exchange(block, "head", m))
    ordered = jnp.concatenate(columns, 1)
    out = jnp.dot(ordered, held_w, preferred_element_type=jnp.float32)
    return out.astype(jnp.bfloat16)


def solution(mesh):
    in_specs = (
        P(("dp", "head"), None),
        P(),
        P(None, "head"),
        P(None, "head"),
        P("head", None),
        P("dp", None, None, None, None),
        P(),
        P(),
        P(),
    )
    out_specs = P(("dp", "head"), None)
    return jax.shard_map(body, mesh=mesh, in_specs=in_specs, out_specs=out_specs, check_vma=False)
```

```python
import math

import jax
import jax.numpy as jnp
from jax import lax
from jax.sharding import PartitionSpec as P
from jax.experimental import pallas as pl
from jax.experimental.pallas import tpu as pltpu

KEY_VALUE_HEADS = 2
HEAD_SIZE = 128
NEWTOK = 512
REQ_DEV = 1


rope_base = 100000000000.0


def from_partner(value, axis, stride):
    mask = 2**stride
    pairs = [(source, source ^ mask) for source in range(lax.axis_size(axis))]
    return lax.ppermute(value, axis, pairs)


def attend_kernel(
    n_cache, tk, scale, part_ref, q_ref, mine_hbm, other_hbm, nk_hbm, nv_hbm, bias_ref,
    *rest,
):
    *o_refs, k_scr, v_scr, s_scr, sems = rest
    bq, head_dim = q_ref.shape
    total = k_scr.shape[0]
    groups = tk // 128

    @pl.when(pl.program_id(0) == 0)
    def _():
        def load(src_k, src_v):
            copies = [
                pltpu.make_async_copy(src_k, k_scr.at[pl.ds(0, n_cache)], sems.at[0]),
                pltpu.make_async_copy(src_v, v_scr.at[pl.ds(0, n_cache)], sems.at[1]),
                pltpu.make_async_copy(nk_hbm, k_scr.at[pl.ds(n_cache, total - n_cache)], sems.at[2]),
                pltpu.make_async_copy(nv_hbm, v_scr.at[pl.ds(n_cache, total - n_cache)], sems.at[3]),
            ]
            for copy in copies:
                copy.start()
            for copy in copies:
                copy.wait()

        @pl.when(part_ref[0] == 0)
        def _():
            load(mine_hbm, other_hbm)

        @pl.when(part_ref[0] != 0)
        def _():
            load(other_hbm, mine_hbm)

    q = q_ref[...]
    part_rows = bq // len(o_refs)

    def true_index(offset, axis):
        place = offset + lax.broadcasted_iota(jnp.int32, (bq, tk), axis)
        block = place // part_rows
        base = jnp.zeros_like(place)
        for k in range(len(o_refs)):
            base = jnp.where(block == k, part_ref[1 + k], base)
        return base + place % part_rows

    def scores(c, top, causal):
        start = pl.multiple_of(c * tk, tk)
        keys = k_scr[pl.ds(start, tk), :]
        s = lax.dot_general(q, keys, (((1,), (1,)), ((), ())), preferred_element_type=jnp.float32)
        s = s * scale + bias_ref[:, pl.ds(start, tk)]
        if causal:
            s = jnp.where(true_index(start - n_cache, 1) <= true_index(0, 0), s, -jnp.inf)
        s_scr[:, pl.ds(start, tk)] = s
        for g in range(groups):
            top = jnp.maximum(top, s[:, g * 128:(g + 1) * 128])
        return top

    top = jnp.full((bq, 128), -jnp.inf, jnp.float32)
    top = lax.fori_loop(0, n_cache // tk, lambda c, t: scores(c, t, False), top, unroll=8)
    top = lax.fori_loop(n_cache // tk, total // tk, lambda c, t: scores(c, t, True), top)
    top = jnp.max(top, -1, keepdims=True)

    def expo(c, part):
        start = pl.multiple_of(c * tk, tk)
        e = jnp.exp(s_scr[:, pl.ds(start, tk)] - top)
        s_scr[:, pl.ds(start, tk)] = e
        for g in range(groups):
            part = part + e[:, g * 128:(g + 1) * 128]
        return part

    part = lax.fori_loop(0, n_cache // tk, expo, jnp.zeros((bq, 128), jnp.float32), unroll=8)
    part = lax.fori_loop(n_cache // tk, total // tk, expo, part)
    inverse = 1.0 / jnp.sum(part, -1, keepdims=True)

    def weigh(c, acc):
        start = pl.multiple_of(c * tk, tk)
        w = (s_scr[:, pl.ds(start, tk)] * inverse).astype(jnp.bfloat16)
        return acc + jnp.dot(w, v_scr[pl.ds(start, tk), :], preferred_element_type=jnp.float32)

    acc = lax.fori_loop(0, n_cache // tk, weigh, jnp.zeros((bq, head_dim), jnp.float32), unroll=8)
    acc = lax.fori_loop(n_cache // tk, total // tk, weigh, acc)
    for k, o_ref in enumerate(o_refs):
        o_ref[...] = acc[k * part_rows:(k + 1) * part_rows].astype(o_ref.dtype)


def attend(queries, mine, other, new_keys, new_values, part, bias, block_base):
    rows, width = queries.shape
    splits = block_base.shape[0]
    n_cache, head_dim = mine.shape
    total = n_cache + new_keys.shape[0]
    heads = width // head_dim
    tk = next(t for t in (512, 256, 128) if total % t == 0 and n_cache % t == 0)
    scale = 1.0 / math.sqrt(head_dim)
    cost = pl.CostEstimate(
        flops=4 * rows * total * head_dim * heads,
        transcendentals=rows * total * heads,
        bytes_accessed=2 * (2 * total * head_dim + 2 * rows * width) + 4 * total,
    )
    any_spec = pl.BlockSpec(memory_space=pl.ANY)
    grid_spec = pltpu.PrefetchScalarGridSpec(
        num_scalar_prefetch=1,
        grid=(heads,),
        in_specs=[
            pl.BlockSpec((rows, head_dim), lambda h, p: (0, h)),
            any_spec,
            any_spec,
            any_spec,
            any_spec,
            pl.BlockSpec((1, total), lambda h, p: (0, 0)),
        ],
        out_specs=[pl.BlockSpec((rows // splits, head_dim), lambda h, p: (0, h))] * splits,
        scratch_shapes=[
            pltpu.VMEM((total, head_dim), jnp.bfloat16),
            pltpu.VMEM((total, head_dim), jnp.bfloat16),
            pltpu.VMEM((rows, total), jnp.float32),
            pltpu.SemaphoreType.DMA((4,)),
        ],
    )
    return pl.pallas_call(
        lambda *refs: attend_kernel(n_cache, tk, scale, *refs),
        out_shape=[jax.ShapeDtypeStruct((rows // splits, width), jnp.bfloat16)] * splits,
        grid_spec=grid_spec,
        compiler_params=pltpu.CompilerParams(dimension_semantics=("arbitrary",)),
        cost_estimate=cost,
        name="paged_prefill_attention",
    )(
        jnp.concatenate([part.reshape(1), block_base]).astype(jnp.int32),
        queries, mine, other, new_keys, new_values, bias,
    )


def exchange(value, axis, mask):
    pairs = [(source, source ^ mask) for source in range(lax.axis_size(axis))]
    return lax.ppermute(value, axis, pairs)


def rotate(values, positions):
    half_dim = values.shape[-1] // 2
    freqs = jnp.exp(
        jnp.arange(half_dim, dtype=jnp.float32) * (-2.0 * math.log(rope_base) / values.shape[-1])
    )
    angles = positions.astype(jnp.float32)[:, None] * freqs[None, :]
    cosine = jnp.cos(angles)[:, None, :]
    sine = jnp.sin(angles)[:, None, :]
    first = values[..., :half_dim]
    second = values[..., half_dim:]
    return jnp.concatenate([first * cosine - second * sine, second * cosine + first * sine], -1)


def body(
    tokens,
    norm_gain,
    w_query,
    key_value_weight,
    w_out,
    kv_pool,
    cache_lengths,
    page_table,
    token_mask,
):
    n_dp = lax.axis_size("dp")
    head_number = lax.axis_size("head")
    me_dp = lax.axis_index("dp")
    current_head = lax.axis_index("head")
    local_rows = tokens.shape[0]
    block_rows = local_rows * head_number
    head_dim = HEAD_SIZE
    group_heads = w_query.shape[1] // head_dim
    page_len = kv_pool.shape[3]
    pool_rows = kv_pool.shape[0]
    max_pages = page_table.shape[1]
    slots = max_pages // n_dp
    key_value_head = current_head // (head_number // KEY_VALUE_HEADS)
    owner_of = jnp.where(page_table >= 0, page_table // pool_rows, -1)
    mine = (owner_of == me_dp).astype(jnp.int32)
    rank = jnp.cumsum(mine, 1) - 1
    slot_ids = jnp.arange(slots, dtype=jnp.int32)
    select = (mine[:, None, :] == 1) & (rank[:, None, :] == slot_ids[None, :, None])
    local_page = jnp.sum(jnp.where(select, (page_table % pool_rows)[:, None, :], 0), -1)
    present = jnp.any(select, -1).reshape(-1)
    part = current_head % 2
    outgoing = kv_pool[local_page.reshape(-1), key_value_head, part]
    outgoing, tokens = lax.optimization_barrier((outgoing, tokens))
    received = lax.all_to_all(outgoing, "dp", split_axis=0, concat_axis=0, tiled=True)
    within = jnp.arange(page_len, dtype=jnp.int32)
    owners_mine = lax.dynamic_slice_in_dim(owner_of, me_dp * REQ_DEV, REQ_DEV, 0)
    hits = (owners_mine[None, :, :] == jnp.arange(n_dp, dtype=jnp.int32)[:, None, None]).astype(
        jnp.int32
    )
    hit_rank = jnp.cumsum(hits, -1) - 1
    chosen = (hits[:, :, None, :] == 1) & (hit_rank[:, :, None, :] == slot_ids[None, None, :, None])
    logical = jnp.sum(
        jnp.where(chosen, jnp.arange(max_pages, dtype=jnp.int32)[None, None, None, :], 0), -1
    )
    has_page = jnp.any(chosen, -1)
    key_pos = logical[..., None] * page_len + within[None, None, None, :]
    wide = tokens.astype(jnp.float32)
    meansq = jnp.mean(wide * wide, -1, keepdims=True)
    normalized_input = (wide * lax.rsqrt(meansq + 1e-05) * norm_gain.astype(jnp.float32)).astype(
        jnp.bfloat16
    )
    rows_in = [normalized_input]
    row_masks = [0]
    stride = head_number // 2
    while stride >= 1:
        rows_in = rows_in + [exchange(p, "head", stride) for p in rows_in]
        row_masks = row_masks + [m ^ stride for m in row_masks]
        stride //= 2
    piece = jnp.concatenate(rows_in, 0)
    within_rows = jnp.arange(local_rows, dtype=jnp.int32)
    true_row = jnp.concatenate([(current_head ^ m) * local_rows + within_rows for m in row_masks])
    held_w = [w_out]
    masks = [0]
    stride = head_number // 2
    while stride > 1:
        held_w = held_w + [exchange(p, "head", stride) for p in held_w]
        masks = masks + [m ^ stride for m in masks]
        stride //= 2
    q_part = jnp.dot(piece, w_query, preferred_element_type=jnp.float32)
    kv_part = jnp.dot(piece, key_value_weight, preferred_element_type=jnp.float32)
    projected = jnp.concatenate([q_part, kv_part], 1)
    q_width = group_heads * head_dim
    my_lengths = lax.dynamic_slice_in_dim(cache_lengths, me_dp * REQ_DEV, REQ_DEV, 0)
    positions = my_lengths[true_row // NEWTOK] + true_row % NEWTOK
    queries = rotate(
        projected[:, :q_width].reshape(block_rows, group_heads, head_dim), positions
    ).astype(jnp.bfloat16)
    own_part = projected[:, q_width:]
    holds_keys = current_head % 2 == 0
    turned = rotate(own_part[:, None, :], positions)[:, 0]
    own_ready = jnp.where(holds_keys, turned, own_part).astype(jnp.bfloat16)
    received, own_ready = lax.optimization_barrier((received, own_ready))
    partner_ready = from_partner(own_ready, "head", 0)
    partner_blocks = [row_masks.index(m ^ 1) for m in row_masks]
    partner_ready = jnp.concatenate(
        [partner_ready[j * local_rows:(j + 1) * local_rows] for j in partner_blocks], 0
    )
    new_keys = jnp.where(holds_keys, own_ready, partner_ready)
    new_values = jnp.where(holds_keys, partner_ready, own_ready)
    mask_rows = lax.dynamic_slice_in_dim(token_mask, me_dp * block_rows, block_rows, 0)
    cache_ok = (has_page[:, 0, :, None] & (key_pos[:, 0] < my_lengths[0])).reshape(-1)
    key_ok = jnp.concatenate([cache_ok, jnp.take(mask_rows, true_row) == 1])
    bias = jnp.where(key_ok, 0.0, -jnp.inf).astype(jnp.float32)
    queries = queries[0:NEWTOK].reshape(NEWTOK, group_heads * head_dim)
    other_half = exchange(received, "head", 1)
    pieces = attend(
        queries,
        received.reshape(-1, head_dim),
        other_half.reshape(-1, head_dim),
        new_keys,
        new_values,
        part,
        bias.reshape(1, -1),
        jnp.stack([(current_head ^ m) * local_rows for m in row_masks]),
    )
    late_w, pieces = lax.optimization_barrier((held_w[1:], pieces))
    held_w = held_w[:1] + list(late_w)
    held_w = held_w + [exchange(piece, "head", 1) for piece in held_w]
    masks = masks + [m ^ 1 for m in masks]
    held_w = jnp.concatenate(held_w, 0)
    columns = []
    for m in masks:
        block = pieces[row_masks.index(m)]
        columns.append(block if m == 0 else exchange(block, "head", m))
    ordered = jnp.concatenate(columns, 1)
    out = jnp.dot(ordered, held_w, preferred_element_type=jnp.float32)
    return out.astype(jnp.bfloat16)


def solution(mesh):
    in_specs = (
        P(("dp", "head"), None),
        P(),
        P(None, "head"),
        P(None, "head"),
        P("head", None),
        P("dp", None, None, None, None),
        P(),
        P(),
        P(),
    )
    out_specs = P(("dp", "head"), None)
    return jax.shard_map(body, mesh=mesh, in_specs=in_specs, out_specs=out_specs, check_vma=False)
```
